256 devices in a mesh: gx: 8 (over z_hi, y), gy: 8 (over x, core), gz: 4 (over z_lo).
Axes of the slice: x: 4, y: 4, z: 8 (z_hi: 2, z_lo: 4; z = z_hi * 4 + z_lo), core: 2. Of those that a mesh axis runs over, the one named last changes fastest.
Arguments:
- pressure: float32 [128, 128, 512], P('gx', 'gy', 'gz'), may hold values from -6 to 6
- velocity: float32 [3, 128, 128, 512], P(None, 'gx', 'gy', 'gz'), may hold values from -6 to 6
- inv_density: float32 [128, 128, 512], P('gx', 'gy', 'gz'), may hold values from 0.5 to 2
- bulk: float32 [128, 128, 512], P('gx', 'gy', 'gz'), may hold values from 0.25 to 1
- node_weight: float32 [8, 8, 256], P('gx', 'gy'), may hold values from 0.2 to 2
- node_patch: int32 [8, 8, 256], P('gx', 'gy'), may hold values from 0 to 8191, as said below
- patch_slot: int32 [8192], replicated, may hold values from 0 to 8191, as said below
- gauge_x: int32 [256], replicated, may hold values from 0 to 127
- gauge_y: int32 [256], replicated, may hold values from 0 to 127
- gauge_misfit: float32 [4, 256], replicated, may hold values from -6 to 6
Outputs:
- pressure_out: float32 [128, 128, 512], P('gx', 'gy', 'gz')
- velocity_out: float32 [3, 128, 128, 512], P(None, 'gx', 'gy', 'gz')
- slip_grad: float32 [8192], P(('gx', 'gy', 'gz'))
The draws below stay inside these ranges and needn't reach their ends.
Inputs may be any that keep to these rules, and one draw needn't show every extreme that they name: `node_patch`: of the seafloor nodes of one tile, at most 16 map to patches whose slot lies in one owner's range of 128 slots; in every draw one owner receives exactly 16 from every tile. `patch_slot`: A permutation of the patches.
All inputs are finite; a program needn't handle non-finite values.
Results may differ from the reference program's by a relative error of at most 0.00018.
Values sent between devices are 32-bit elements; how exact they have to be, the bound alone decides.
No kernel may reach another device: no remote copies, remote signals or barrier semaphores. Data moves between devices by JAX's collectives and lax.ppermute only.
A program may use at most 64 MiB of HBM per device.

```python
import math
import jax
import jax.numpy as jnp
from jax import lax

CX = 16
CY = 16
ITERS = 4
P_DEV = 128
GAUGES = 256
NX = 128
NY = 128
NZ = 512
SEA_DEV = 256
PATCHES = 8192
N_GX = 8
N_GY = 8


def route_tables(key):
    owners_count = N_GX * N_GY
    capacity = 4 * SEA_DEV // owners_count
    light_copies = max(capacity // 4, 1)
    popular_count = max(owners_count // 8, 1)
    ranking = jax.random.permutation(jax.random.fold_in(key, 11), owners_count).astype(jnp.int32)
    full_owner = ranking[0]
    popular = jnp.zeros((owners_count,), jnp.int32).at[ranking[1:1 + popular_count]].set(1)
    copies = jnp.where(popular == 1, capacity, light_copies).astype(jnp.int32)
    copies = copies.at[full_owner].set(0)
    element = jnp.arange(owners_count * capacity, dtype=jnp.int32)
    element_owner = element // capacity
    usable = element % capacity < copies[element_owner]
    remaining = SEA_DEV - capacity

    def one_device(device_key):
        key_score, key_place, key_patch = jax.random.split(device_key, 3)
        priority = jax.random.randint(key_score, (owners_count * capacity,), 0, 65536, dtype=jnp.int32) * (owners_count * capacity) + element
        priority = jnp.where(usable, priority, 2147483647)
        picked = lax.top_k(-priority, remaining)[1]
        chosen = jnp.concatenate([jnp.full((capacity,), full_owner, jnp.int32), element_owner[picked].astype(jnp.int32)])
        chosen = jax.random.permutation(key_place, chosen)
        within = jax.random.randint(key_patch, (SEA_DEV,), 0, P_DEV, dtype=jnp.int32)
        return (chosen * P_DEV + within).astype(jnp.int32)
    device_keys = jax.random.split(jax.random.fold_in(key, 12), owners_count)
    slots = jax.vmap(one_device)(device_keys).reshape(N_GX, N_GY, SEA_DEV)
    slot_of_patch = jax.random.permutation(jax.random.fold_in(key, 13), PATCHES).astype(jnp.int32)
    patch_at_slot = jnp.argsort(slot_of_patch).astype(jnp.int32)
    return (patch_at_slot[slots].astype(jnp.int32), slot_of_patch)


def draw_node_patch(key, part):
    return route_tables(key)[0]


def draw_patch_slot(key, part):
    return route_tables(key)[1]


def touch_ends(array, rng, least, high):
    longest = array.shape.index(max(array.shape))
    spots = []
    for shift in (0, 1):
        where = [jax.random.randint(jax.random.fold_in(rng, axis), (), 0, length) for axis, length in enumerate(array.shape)]
        where[longest] = (where[longest] + shift) % array.shape[longest]
        spots.append(tuple(where))
    return array.at[spots[0]].set(least).at[spots[1]].set(high)


def steps_of(own_key, dims, cuts, low, top_value):
    factor_of, own = 1.0, jax.random.fold_in(own_key, 6)
    for axis_at, blocks in cuts:
        heights = jnp.exp(jax.random.uniform(jax.random.fold_in(own, axis_at), (blocks,), jnp.float32, low / len(cuts), top_value / len(cuts)))
        factor_of = factor_of * jnp.repeat(heights, dims[axis_at] // blocks).reshape([-1 if axis == axis_at else 1 for axis in range(len(dims))])
    return factor_of


def bell_draw(key, extent, scale, limit, cuts=(), held_as=jnp.bfloat16):
    array = scale * jax.random.normal(key, extent, jnp.float32)
    if cuts:
        array = array * steps_of(key, extent, cuts, -0.22, 0.18)
    return jnp.clip(array, -limit, limit).astype(held_as)


def setup_inputs(seed: int = 0) -> dict:
    splits = jax.random.split(jax.random.key(seed), 11)
    pressure = bell_draw(splits[0], (NX, NY, NZ), 1.0, 6.0, ((0, 8), (1, 8), (2, 4)), jnp.float32)
    velocity = bell_draw(splits[1], (3, NX, NY, NZ), 1.0, 6.0, ((1, 8), (2, 8), (3, 4)), jnp.float32)
    inv_density = jnp.clip(jnp.exp(math.log(2.0) - 1.3862944 * jax.random.uniform(splits[2], (NX, NY, NZ), jnp.float32) ** steps_of(splits[2], (NX, NY, NZ), ((0, 8), (1, 8), (2, 4)), -0.2, 0.2)), 0.5, 2.0)
    bulk = jnp.clip(jnp.exp(math.log(1.0) - 1.3862944 * jax.random.uniform(splits[3], (NX, NY, NZ), jnp.float32) ** steps_of(splits[3], (NX, NY, NZ), ((0, 8), (1, 8), (2, 4)), -0.2, 0.2)), 0.25, 1.0)
    node_weight = jnp.clip(jnp.exp(math.log(2.0) - 2.3025851 * jax.random.uniform(splits[4], (N_GX, N_GY, SEA_DEV), jnp.float32) ** steps_of(splits[4], (N_GX, N_GY, SEA_DEV), ((0, 8), (1, 8)), -0.2, 0.2)), 0.2, 2.0)
    node_patch = draw_node_patch(jax.random.fold_in(splits[10], 71), 0)
    patch_slot = draw_patch_slot(jax.random.fold_in(splits[10], 71), 0)
    gauge_x = touch_ends(jax.random.randint(splits[7], (GAUGES,), 0, NX), jax.random.fold_in(splits[7], 1), 0, NX - 1).astype(jnp.int32)
    gauge_y = touch_ends(jax.random.randint(splits[8], (GAUGES,), 0, NY), jax.random.fold_in(splits[8], 1), 0, NY - 1).astype(jnp.int32)
    gauge_misfit = bell_draw(splits[9], (ITERS, GAUGES), 1.0, 6.0, (), jnp.float32)
    return dict(pressure=pressure, velocity=velocity, inv_density=inv_density, bulk=bulk, node_weight=node_weight, node_patch=node_patch, patch_slot=patch_slot, gauge_x=gauge_x, gauge_y=gauge_y, gauge_misfit=gauge_misfit)


time_step = 0.5


def depth_weights(levels, first_crust):
    ocean_last = levels == first_crust - 1
    crust_first = levels == first_crust
    weight_above = jnp.where(ocean_last, 0.5, jnp.where(crust_first, 1.0, 0.5)).astype(jnp.float32)
    weight_here = jnp.where(ocean_last, 0.5, jnp.where(crust_first, -1.5, 0.0)).astype(jnp.float32)
    weight_below = jnp.where(ocean_last, -1.0, jnp.where(crust_first, 0.5, -0.5)).astype(jnp.float32)
    return weight_above, weight_here, weight_below


def reference(pressure, velocity, inv_density, bulk, node_weight, node_patch, patch_slot, gauge_x, gauge_y, gauge_misfit):
    first_crust = NZ // 2
    weight_above, weight_here, weight_below = depth_weights(jnp.arange(NZ), first_crust)
    sources = jnp.zeros((ITERS, NX, NY), jnp.float32).at[:, gauge_x, gauge_y].add(gauge_misfit)
    seafloor = jnp.zeros((NX, NY), jnp.float32)
    for instant in range(ITERS):
        seafloor = seafloor + 0.5 * (pressure[:, :, first_crust - 1] + pressure[:, :, first_crust])
        padded = jnp.pad(pressure, 1)
        slope_x = 0.5 * (padded[2:, 1:-1, 1:-1] - padded[:-2, 1:-1, 1:-1])
        slope_y = 0.5 * (padded[1:-1, 2:, 1:-1] - padded[1:-1, :-2, 1:-1])
        slope_z = weight_above * padded[1:-1, 1:-1, 2:] + weight_here * pressure + weight_below * padded[1:-1, 1:-1, :-2]
        velocity = jnp.stack([velocity[0] - time_step * inv_density * slope_x,
                              velocity[1] - time_step * inv_density * slope_y,
                              velocity[2] - time_step * inv_density * slope_z])
        along_x = jnp.pad(velocity[0], ((1, 1), (0, 0), (0, 0)))
        along_y = jnp.pad(velocity[1], ((0, 0), (1, 1), (0, 0)))
        along_z = jnp.pad(velocity[2], ((0, 0), (0, 0), (1, 1)))
        spread = 0.5 * (along_x[2:] - along_x[:-2]) + 0.5 * (along_y[:, 2:] - along_y[:, :-2]) + (
            weight_above * along_z[:, :, 2:] + weight_here * velocity[2] + weight_below * along_z[:, :, :-2])
        pressure = pressure - time_step * bulk * spread
        pressure = pressure.at[:, :, 0].add(time_step * sources[instant])
    tiles = jnp.transpose(seafloor.reshape(N_GX, CX, N_GY, CY), (0, 2, 1, 3)).reshape(N_GX, N_GY, SEA_DEV)
    node_values = node_weight * tiles
    slots = patch_slot[node_patch]
    slip_grad = jax.ops.segment_sum(node_values.reshape(-1), slots.reshape(-1), num_segments=PATCHES)
    return pressure, velocity, slip_grad
```

```python
import jax
import jax.numpy as jnp
from jax import lax
from jax.sharding import PartitionSpec as P

ITERS = 4


time_step = 0.5
margin = 4


def extended(block, sides, width):
    for axis, dim in sides:
        count = lax.axis_size(axis)
        forward = [(i, i + 1) for i in range(count - 1)]
        backward = [(target, source) for source, target in forward]
        low = lax.ppermute(
            lax.slice_in_dim(block, block.shape[dim] - width, None, axis=dim), axis, forward
        )
        high = lax.ppermute(lax.slice_in_dim(block, 0, width, axis=dim), axis, backward)
        block = jnp.concatenate([low, block, high], axis=dim)
    return block


def in_blocks(x, dim, size):
    before, after = (x.shape[:dim], x.shape[dim + 1 :])
    return jnp.moveaxis(x.reshape(*before, size, -1, *after), dim, 0)


def summed_on_arrival(x, axis, dim):
    size = lax.axis_size(axis)
    parts = lax.all_to_all(in_blocks(x, dim, size), axis, 0, 0, tiled=True)
    return jnp.sum(parts, axis=0)


def picked(x, axis, root):
    return lax.dynamic_index_in_dim(lax.all_gather(x, axis), root, 0, keepdims=False)


def depth_weights(levels, first_crust):
    ocean_last = levels == first_crust - 1
    crust_first = levels == first_crust
    weight_above = jnp.where(ocean_last, 0.5, jnp.where(crust_first, 1.0, 0.5)).astype(jnp.float32)
    weight_here = jnp.where(ocean_last, 0.5, jnp.where(crust_first, -1.5, 0.0)).astype(jnp.float32)
    weight_below = jnp.where(ocean_last, -1.0, jnp.where(crust_first, 0.5, -0.5)).astype(
        jnp.float32
    )
    return (weight_above, weight_here, weight_below)


def source_planes(gauge_x, gauge_y, gauge_misfit, start_x, start_y, span_x, span_y):
    local_x = gauge_x - start_x
    local_y = gauge_y - start_y
    inside = (local_x >= 0) & (local_x < span_x) & (local_y >= 0) & (local_y < span_y)
    gauge_cell = jnp.where(inside, local_x * span_y + local_y, -1)
    gauge_table = (
        gauge_cell[:, None] == jnp.arange(span_x * span_y, dtype=jnp.int32)[None, :]
    ).astype(jnp.float32)
    return jnp.dot(gauge_misfit, gauge_table, precision=lax.Precision.HIGHEST).reshape(
        gauge_misfit.shape[0], span_x, span_y
    )


def local_step(pressure, velocity, inv_density, bulk, weights, source_plane, top_mask):
    weight_above, weight_here, weight_below = weights
    padded = jnp.pad(pressure, 1)
    slope_x = 0.5 * (padded[2:, 1:-1, 1:-1] - padded[:-2, 1:-1, 1:-1])
    slope_y = 0.5 * (padded[1:-1, 2:, 1:-1] - padded[1:-1, :-2, 1:-1])
    slope_z = (
        weight_above * padded[1:-1, 1:-1, 2:]
        + weight_here * pressure
        + weight_below * padded[1:-1, 1:-1, :-2]
    )
    velocity = jnp.stack(
        [
            velocity[0] - time_step * inv_density * slope_x,
            velocity[1] - time_step * inv_density * slope_y,
            velocity[2] - time_step * inv_density * slope_z,
        ]
    )
    along_x = jnp.pad(velocity[0], ((1, 1), (0, 0), (0, 0)))
    along_y = jnp.pad(velocity[1], ((0, 0), (1, 1), (0, 0)))
    along_z = jnp.pad(velocity[2], ((0, 0), (0, 0), (1, 1)))
    spread = (
        0.5 * (along_x[2:] - along_x[:-2])
        + 0.5 * (along_y[:, 2:] - along_y[:, :-2])
        + (
            weight_above * along_z[:, :, 2:]
            + weight_here * velocity[2]
            + weight_below * along_z[:, :, :-2]
        )
    )
    pressure = pressure - time_step * bulk * spread
    pressure = pressure + time_step * source_plane[:, :, None] * top_mask[None, None, :]
    return (pressure, velocity)


def local(
    pressure,
    velocity,
    inv_density,
    bulk,
    node_weight,
    node_patch,
    patch_slot,
    gauge_x,
    gauge_y,
    gauge_misfit,
):
    rows_x, rows_y, depth = pressure.shape
    tiles_z = lax.axis_size("gz")
    depth_index = lax.axis_index("gz")
    first_crust = tiles_z // 2 * depth
    seafloor = jnp.zeros((rows_x, rows_y), jnp.float32)
    levels = depth_index * depth - margin + jnp.arange(depth + 2 * margin, dtype=jnp.int32)
    weights = depth_weights(levels, first_crust)
    top_mask = (levels == 0).astype(jnp.float32)
    sources = source_planes(
        gauge_x,
        gauge_y,
        gauge_misfit,
        lax.axis_index("gx") * rows_x - margin,
        lax.axis_index("gy") * rows_y - margin,
        rows_x + 2 * margin,
        rows_y + 2 * margin,
    )
    fields = jnp.concatenate([pressure[None], velocity], axis=0)
    for group in range(ITERS // 2):
        if group == 0:
            wide = extended(
                jnp.concatenate([fields, inv_density[None], bulk[None]], axis=0),
                (("gx", 1), ("gy", 2), ("gz", 3)),
                margin,
            )
            media = wide[4:]
            wide = wide[:4]
        else:
            wide = extended(fields, (("gx", 1), ("gy", 2), ("gz", 3)), margin)
        wide_pressure = wide[0]
        wide_velocity = wide[1:]
        for inner in range(2):
            instant = 2 * group + inner
            seafloor = seafloor + 0.5 * (
                wide_pressure[margin:-margin, margin:-margin, margin - 1]
                + wide_pressure[margin:-margin, margin:-margin, margin]
            )
            wide_pressure, wide_velocity = local_step(
                wide_pressure,
                wide_velocity,
                media[0],
                media[1],
                weights,
                sources[instant],
                top_mask,
            )
        fields = jnp.concatenate([wide_pressure[None], wide_velocity], axis=0)[
            :, margin:-margin, margin:-margin, margin:-margin
        ]
    pressure = fields[0]
    velocity = fields[1:]
    sea_count = rows_x * rows_y
    owners_count = lax.axis_size("gx") * lax.axis_size("gy")
    patch_count = patch_slot.shape[0] // owners_count
    piece_count = patch_count // tiles_z
    root_tile = tiles_z // 2
    sea_values = node_weight[0, 0] * seafloor.reshape(sea_count)
    slots = patch_slot[node_patch[0, 0]]
    sea_values = jnp.where(depth_index == root_tile, sea_values, 0.0)
    partial_slip = jnp.zeros((patch_slot.shape[0],), jnp.float32).at[slots].add(sea_values)
    slip_grad = lax.psum_scatter(partial_slip, ("gx", "gy", "gz"), scatter_dimension=0, tiled=True)
    return (pressure, velocity, slip_grad)


def solution(mesh):
    placed = (
        P("gx", "gy", "gz"),
        P(None, "gx", "gy", "gz"),
        P("gx", "gy", "gz"),
        P("gx", "gy", "gz"),
        P("gx", "gy", None),
        P("gx", "gy", None),
        P(),
        P(),
        P(),
        P(),
    )
    return jax.shard_map(
        local,
        mesh=mesh,
        in_specs=placed,
        out_specs=(P("gx", "gy", "gz"), P(None, "gx", "gy", "gz"), P(("gx", "gy", "gz"))),
        check_vma=False,
    )
```

```python
import functools

import jax
import jax.numpy as jnp
from jax import lax
from jax.experimental import pallas as pl
from jax.experimental.pallas import tpu as pltpu
from jax.sharding import PartitionSpec as P

ITERS = 4


time_step = 0.5


def shifted_up(x, axis):
    count = lax.axis_size(axis)
    return lax.ppermute(x, axis, [(i, i + 1) for i in range(count - 1)])


def shifted_down(x, axis):
    count = lax.axis_size(axis)
    return lax.ppermute(x, axis, [(i + 1, i) for i in range(count - 1)])


def in_blocks(x, dim, size):
    before, after = (x.shape[:dim], x.shape[dim + 1 :])
    return jnp.moveaxis(x.reshape(*before, size, -1, *after), dim, 0)


def summed_on_arrival(x, axis, dim):
    size = lax.axis_size(axis)
    parts = lax.all_to_all(in_blocks(x, dim, size), axis, 0, 0, tiled=True)
    return jnp.sum(parts, axis=0)


def picked(x, axis, root):
    return lax.dynamic_index_in_dim(lax.all_gather(x, axis), root, 0, keepdims=False)


def depth_weights(levels, first_crust):
    ocean_last = levels == first_crust - 1
    crust_first = levels == first_crust
    weight_above = jnp.where(ocean_last, 0.5, jnp.where(crust_first, 1.0, 0.5)).astype(jnp.float32)
    weight_here = jnp.where(ocean_last, 0.5, jnp.where(crust_first, -1.5, 0.0)).astype(jnp.float32)
    weight_below = jnp.where(ocean_last, -1.0, jnp.where(crust_first, 0.5, -0.5)).astype(
        jnp.float32
    )
    return (weight_above, weight_here, weight_below)


def source_planes(gauge_x, gauge_y, gauge_misfit, start_x, start_y, span_x, span_y):
    local_x = gauge_x - start_x
    local_y = gauge_y - start_y
    inside = (local_x >= 0) & (local_x < span_x) & (local_y >= 0) & (local_y < span_y)
    gauge_cell = jnp.where(inside, local_x * span_y + local_y, -1)
    gauge_table = (
        gauge_cell[:, None] == jnp.arange(span_x * span_y, dtype=jnp.int32)[None, :]
    ).astype(jnp.float32)
    return jnp.dot(gauge_misfit, gauge_table, precision=lax.Precision.HIGHEST).reshape(
        gauge_misfit.shape[0], span_x, span_y
    )


def pick(a, axis, index):
    where = lax.broadcasted_iota(jnp.int32, a.shape, a.ndim + axis if axis < 0 else axis) == index
    return jnp.sum(jnp.where(where, a, 0.0), axis=axis, keepdims=True)


def pair(lo, hi, shape, axis):
    where = lax.broadcasted_iota(jnp.int32, shape, axis) == 0
    return jnp.where(where, jnp.broadcast_to(lo, shape), jnp.broadcast_to(hi, shape))


def step_kernel(
    scal_ref,
    wint_ref,
    p_ref,
    v_ref,
    idn_ref,
    bulk_ref,
    src_ref,
    sf_ref,
    pxl_ref,
    pxh_ref,
    pyl_ref,
    pyh_ref,
    pzl_ref,
    pzh_ref,
    vx_ref,
    vy_ref,
    vz_ref,
    ix_ref,
    iy_ref,
    iz_ref,
    po_ref,
    vo_ref,
    sfo_ref,
    vxo_ref,
    vyo_ref,
    vzo_ref,
    sxu_ref,
    sxd_ref,
    syu_ref,
    syd_ref,
    szu_ref,
    szd_ref,
):
    X, Y, Z = p_ref.shape
    rows = pyl_ref.shape[1]
    full = (X, Y, Z)
    yi = lax.broadcasted_iota(jnp.int32, full, 1)
    zi = lax.broadcasted_iota(jnp.int32, full, 2)
    wu = wint_ref[0]
    wm = wint_ref[1]
    wl = wint_ref[2]
    wu_lo = scal_ref[0]
    wm_lo = scal_ref[1]
    wl_lo = scal_ref[2]
    wu_hi = scal_ref[3]
    wm_hi = scal_ref[4]
    wl_hi = scal_ref[5]
    f_ocean = scal_ref[6]
    f_crust = scal_ref[7]

    pres = p_ref[...]
    idn = idn_ref[...]

    p_first = pick(pres, -1, 0)
    p_last = pick(pres, -1, Z - 1)
    pzl = pzl_ref[...]
    pzh = pzh_ref[...]
    zl2 = pick(pzl, -1, 0)
    zl1 = pick(pzl, -1, 1)
    zh1 = pick(pzh, -1, 0)
    zh2 = pick(pzh, -1, 1)
    sfo_ref[...] = sf_ref[...] + 0.5 * (f_ocean * (p_last + zh1) + f_crust * (zl1 + p_first))

    pxl = pxl_ref[...]
    pxh = pxh_ref[...]
    above_x = jnp.concatenate([pres[1:], pxh[0:1]], axis=0)
    below_x = jnp.concatenate([pxl[1:2], pres[:-1]], axis=0)
    slope_x = 0.5 * (above_x - below_x)
    v0 = v_ref[0] - time_step * idn * slope_x
    vx = vx_ref[...]
    ix = ix_ref[...]
    v0_lo = vx[0:1] - time_step * ix[0:1] * (0.5 * (pres[0:1] - pxl[0:1]))
    v0_hi = vx[1:2] - time_step * ix[1:2] * (0.5 * (pxh[1:2] - pres[X - 1 : X]))

    pyl = pyl_ref[...]
    pyh = pyh_ref[...]
    yl1 = pick(pyl, 1, rows - 1)
    yl2 = pick(pyl, 1, rows - 2)
    yh1 = pick(pyh, 1, 0)
    yh2 = pick(pyh, 1, 1)
    p_y0 = pick(pres, 1, 0)
    p_yl = pick(pres, 1, Y - 1)
    above_y = jnp.where(yi == Y - 1, jnp.broadcast_to(yh1, full), pltpu.roll(pres, Y - 1, 1))
    below_y = jnp.where(yi == 0, jnp.broadcast_to(yl1, full), pltpu.roll(pres, 1, 1))
    slope_y = 0.5 * (above_y - below_y)
    v1 = v_ref[1] - time_step * idn * slope_y
    vy = vy_ref[...]
    iy = iy_ref[...]
    v1_lo = pick(vy, 1, 0) - time_step * pick(iy, 1, 0) * (0.5 * (p_y0 - yl2))
    v1_hi = pick(vy, 1, 1) - time_step * pick(iy, 1, 1) * (0.5 * (yh2 - p_yl))

    above_z = jnp.where(zi == Z - 1, jnp.broadcast_to(zh1, full), pltpu.roll(pres, Z - 1, 2))
    below_z = jnp.where(zi == 0, jnp.broadcast_to(zl1, full), pltpu.roll(pres, 1, 2))
    slope_z = wu * above_z + wm * pres + wl * below_z
    v2 = v_ref[2] - time_step * idn * slope_z
    vz = vz_ref[...]
    iz = iz_ref[...]
    v2_lo = pick(vz, -1, 0) - time_step * pick(iz, -1, 0) * (wu_lo * p_first + wm_lo * zl1 + wl_lo * zl2)
    v2_hi = pick(vz, -1, 1) - time_step * pick(iz, -1, 1) * (wu_hi * zh2 + wm_hi * zh1 + wl_hi * p_last)

    vo_ref[0] = v0
    vo_ref[1] = v1
    vo_ref[2] = v2
    vxo_ref[0:1] = v0_lo
    vxo_ref[1:2] = v0_hi
    vyo_ref[...] = pair(v1_lo, v1_hi, vyo_ref.shape, 1)
    vzo_ref[...] = pair(v2_lo, v2_hi, vzo_ref.shape, 2)

    up_x = jnp.concatenate([v0[1:], v0_hi], axis=0)
    down_x = jnp.concatenate([v0_lo, v0[:-1]], axis=0)
    up_y = jnp.where(yi == Y - 1, jnp.broadcast_to(v1_hi, full), pltpu.roll(v1, Y - 1, 1))
    down_y = jnp.where(yi == 0, jnp.broadcast_to(v1_lo, full), pltpu.roll(v1, 1, 1))
    up_z = jnp.where(zi == Z - 1, jnp.broadcast_to(v2_hi, full), pltpu.roll(v2, Z - 1, 2))
    down_z = jnp.where(zi == 0, jnp.broadcast_to(v2_lo, full), pltpu.roll(v2, 1, 2))
    spread = (
        0.5 * (up_x - down_x)
        + 0.5 * (up_y - down_y)
        + (wu * up_z + wm * v2 + wl * down_z)
    )
    new_p = pres - time_step * bulk_ref[...] * spread
    new_p = jnp.where(zi == 0, new_p + jnp.broadcast_to(src_ref[...], full), new_p)
    po_ref[...] = new_p

    sxu_ref[...] = new_p[X - 2 :]
    sxd_ref[...] = new_p[0:2]
    syu_ref[...] = new_p[:, Y - rows :]
    syd_ref[...] = new_p[:, 0:rows]
    zshape = szu_ref.shape
    szu_ref[...] = pair(pick(new_p, -1, Z - 2), pick(new_p, -1, Z - 1), zshape, 2)
    szd_ref[...] = pair(pick(new_p, -1, 0), pick(new_p, -1, 1), zshape, 2)


def run_step(scal, wint, pres, vel, idn, bulk, src, sf, halos, tracked, media_halo):
    X, Y, Z = pres.shape
    rows = halos[2].shape[1]
    f32 = jnp.float32
    shapes = (
        jax.ShapeDtypeStruct((X, Y, Z), f32),
        jax.ShapeDtypeStruct((3, X, Y, Z), f32),
        jax.ShapeDtypeStruct((X, Y, 1), f32),
        jax.ShapeDtypeStruct((2, Y, Z), f32),
        jax.ShapeDtypeStruct((X, 2, Z), f32),
        jax.ShapeDtypeStruct((X, Y, 2), f32),
        jax.ShapeDtypeStruct((2, Y, Z), f32),
        jax.ShapeDtypeStruct((2, Y, Z), f32),
        jax.ShapeDtypeStruct((X, rows, Z), f32),
        jax.ShapeDtypeStruct((X, rows, Z), f32),
        jax.ShapeDtypeStruct((X, Y, 2), f32),
        jax.ShapeDtypeStruct((X, Y, 2), f32),
    )
    vmem = pl.BlockSpec(memory_space=pltpu.VMEM)
    in_specs = [pl.BlockSpec(memory_space=pltpu.SMEM)] + [vmem] * 19
    cells = X * Y * Z
    return pl.pallas_call(
        step_kernel,
        out_shape=shapes,
        in_specs=in_specs,
        out_specs=[vmem] * len(shapes),
        cost_estimate=pl.CostEstimate(
            flops=80 * cells, transcendentals=0, bytes_accessed=4 * 4 * 12 * cells // 4
        ),
    )(scal, wint, pres, vel, idn, bulk, src, sf, *halos, *tracked, *media_halo)


def local(
    pressure,
    velocity,
    inv_density,
    bulk,
    node_weight,
    node_patch,
    patch_slot,
    gauge_x,
    gauge_y,
    gauge_misfit,
):
    X, Y, Z = pressure.shape
    rows = 8
    tiles_z = lax.axis_size("gz")
    depth_index = lax.axis_index("gz")
    first_crust = tiles_z // 2 * Z
    levels = depth_index * Z + jnp.arange(Z, dtype=jnp.int32)
    wint = jnp.stack(depth_weights(levels, first_crust)).reshape(3, 1, 1, Z)
    edge_levels = jnp.stack([depth_index * Z - 1, depth_index * Z + Z])
    edge_w = depth_weights(edge_levels, first_crust)
    ocean_flag = (depth_index == first_crust // Z - 1).astype(jnp.float32)
    crust_flag = (depth_index == first_crust // Z).astype(jnp.float32)
    scal = jnp.stack(
        [edge_w[0][0], edge_w[1][0], edge_w[2][0], edge_w[0][1], edge_w[1][1], edge_w[2][1],
         ocean_flag, crust_flag]
    ).astype(jnp.float32)
    top_flag = (depth_index == 0).astype(jnp.float32)
    sources = source_planes(
        gauge_x,
        gauge_y,
        gauge_misfit,
        lax.axis_index("gx") * X,
        lax.axis_index("gy") * Y,
        X,
        Y,
    )
    src_all = (time_step * sources * top_flag)[..., None]

    v0, v1, v2 = velocity[0], velocity[1], velocity[2]
    x_up = jnp.concatenate([pressure[X - 2 :], v0[X - 1 :], inv_density[X - 1 :]], axis=0)
    x_dn = jnp.concatenate([pressure[:2], v0[:1], inv_density[:1]], axis=0)
    y_up = jnp.concatenate(
        [pressure[:, Y - rows :], v1[:, Y - 1 :], inv_density[:, Y - 1 :]], axis=1
    )
    y_dn = jnp.concatenate([pressure[:, :rows], v1[:, :1], inv_density[:, :1]], axis=1)
    z_up = jnp.concatenate(
        [pressure[:, :, Z - 2 :], v2[:, :, Z - 1 :], inv_density[:, :, Z - 1 :]], axis=2
    )
    z_dn = jnp.concatenate([pressure[:, :, :2], v2[:, :, :1], inv_density[:, :, :1]], axis=2)
    rx_lo = shifted_up(x_up, "gx")
    rx_hi = shifted_down(x_dn, "gx")
    ry_lo = shifted_up(y_up, "gy")
    ry_hi = shifted_down(y_dn, "gy")
    rz_lo = shifted_up(z_up, "gz")
    rz_hi = shifted_down(z_dn, "gz")
    halos = (
        rx_lo[:2],
        rx_hi[:2],
        ry_lo[:, :rows],
        ry_hi[:, :rows],
        rz_lo[:, :, :2],
        rz_hi[:, :, :2],
    )
    tracked = (
        jnp.concatenate([rx_lo[2:3], rx_hi[2:3]], axis=0),
        jnp.concatenate([ry_lo[:, rows : rows + 1], ry_hi[:, rows : rows + 1]], axis=1),
        jnp.concatenate([rz_lo[:, :, 2:3], rz_hi[:, :, 2:3]], axis=2),
    )
    media_halo = (
        jnp.concatenate([rx_lo[3:4], rx_hi[3:4]], axis=0),
        jnp.concatenate([ry_lo[:, rows + 1 : rows + 2], ry_hi[:, rows + 1 : rows + 2]], axis=1),
        jnp.concatenate([rz_lo[:, :, 3:4], rz_hi[:, :, 3:4]], axis=2),
    )
    sf = jnp.zeros((X, Y, 1), jnp.float32)
    pres, vel = pressure, velocity
    for instant in range(ITERS):
        if instant > 0:
            halos = (
                shifted_up(sends[0], "gx"),
                shifted_down(sends[1], "gx"),
                shifted_up(sends[2], "gy"),
                shifted_down(sends[3], "gy"),
                shifted_up(sends[4], "gz"),
                shifted_down(sends[5], "gz"),
            )
        outs = run_step(
            scal, wint, pres, vel, inv_density, bulk, src_all[instant], sf, halos, tracked,
            media_halo,
        )
        pres, vel, sf = outs[0], outs[1], outs[2]
        tracked = outs[3:6]
        sends = outs[6:12]
    seafloor = sf[:, :, 0]

    sea_count = X * Y
    owners_count = lax.axis_size("gx") * lax.axis_size("gy")
    patch_count = patch_slot.shape[0] // owners_count
    piece_count = patch_count // tiles_z
    root_tile = first_crust // Z
    sea_values = node_weight[0, 0] * seafloor.reshape(sea_count)
    slots = patch_slot[node_patch[0, 0]]
    partial_slip = jnp.zeros((patch_slot.shape[0],), jnp.float32).at[slots].add(sea_values)
    slip_grad = summed_on_arrival(partial_slip, ("gx", "gy"), 0)
    slip_grad = picked(slip_grad, "gz", root_tile)
    slip_grad = lax.dynamic_slice_in_dim(slip_grad, depth_index * piece_count, piece_count)
    return (pres, vel, slip_grad)


def solution(mesh):
    placed = (
        P("gx", "gy", "gz"),
        P(None, "gx", "gy", "gz"),
        P("gx", "gy", "gz"),
        P("gx", "gy", "gz"),
        P("gx", "gy", None),
        P("gx", "gy", None),
        P(),
        P(),
        P(),
        P(),
    )
    return jax.shard_map(
        local,
        mesh=mesh,
        in_specs=placed,
        out_specs=(P("gx", "gy", "gz"), P(None, "gx", "gy", "gz"), P(("gx", "gy", "gz"))),
        check_vma=False,
    )
```

```python
import functools

import jax
import jax.numpy as jnp
from jax import lax
from jax.experimental import pallas as pl
from jax.experimental.pallas import tpu as pltpu
from jax.sharding import PartitionSpec as P

ITERS = 4


time_step = 0.5


def shifted_up(x, axis):
    count = lax.axis_size(axis)
    return lax.ppermute(x, axis, [(i, i + 1) for i in range(count - 1)])


def shifted_down(x, axis):
    count = lax.axis_size(axis)
    return lax.ppermute(x, axis, [(i + 1, i) for i in range(count - 1)])


def in_blocks(x, dim, size):
    before, after = (x.shape[:dim], x.shape[dim + 1 :])
    return jnp.moveaxis(x.reshape(*before, size, -1, *after), dim, 0)


def summed_on_arrival(x, axis, dim):
    size = lax.axis_size(axis)
    parts = lax.all_to_all(in_blocks(x, dim, size), axis, 0, 0, tiled=True)
    return jnp.sum(parts, axis=0)


def depth_weights(levels, first_crust):
    ocean_last = levels == first_crust - 1
    crust_first = levels == first_crust
    weight_above = jnp.where(ocean_last, 0.5, jnp.where(crust_first, 1.0, 0.5)).astype(jnp.float32)
    weight_here = jnp.where(ocean_last, 0.5, jnp.where(crust_first, -1.5, 0.0)).astype(jnp.float32)
    weight_below = jnp.where(ocean_last, -1.0, jnp.where(crust_first, 0.5, -0.5)).astype(
        jnp.float32
    )
    return (weight_above, weight_here, weight_below)


def source_planes(gauge_x, gauge_y, gauge_misfit, start_x, start_y, span_x, span_y):
    local_x = gauge_x - start_x
    local_y = gauge_y - start_y
    inside = (local_x >= 0) & (local_x < span_x) & (local_y >= 0) & (local_y < span_y)
    gauge_cell = jnp.where(inside, local_x * span_y + local_y, -1)
    gauge_table = (
        gauge_cell[:, None] == jnp.arange(span_x * span_y, dtype=jnp.int32)[None, :]
    ).astype(jnp.float32)
    return jnp.dot(gauge_misfit, gauge_table, precision=lax.Precision.HIGHEST).reshape(
        gauge_misfit.shape[0], span_x, span_y
    )


def pick(a, axis, index):
    where = lax.broadcasted_iota(jnp.int32, a.shape, a.ndim + axis if axis < 0 else axis) == index
    return jnp.sum(jnp.where(where, a, 0.0), axis=axis, keepdims=True)


def pair(lo, hi, shape, axis):
    where = lax.broadcasted_iota(jnp.int32, shape, axis) == 0
    return jnp.where(where, jnp.broadcast_to(lo, shape), jnp.broadcast_to(hi, shape))


def step_kernel(
    scal_ref,
    wint_ref,
    p_ref,
    v_ref,
    idn_ref,
    bulk_ref,
    src_ref,
    sf_ref,
    pxl_ref,
    pxh_ref,
    pyl_ref,
    pyh_ref,
    pzl_ref,
    pzh_ref,
    vx_ref,
    vy_ref,
    vz_ref,
    ix_ref,
    iy_ref,
    iz_ref,
    po_ref,
    vo_ref,
    sfo_ref,
    vxo_ref,
    vyo_ref,
    vzo_ref,
    sxu_ref,
    sxd_ref,
    syu_ref,
    syd_ref,
    szu_ref,
    szd_ref,
):
    X, Y, Z = p_ref.shape
    rows = pyl_ref.shape[1]
    full = (X, Y, Z)
    yi = lax.broadcasted_iota(jnp.int32, full, 1)
    zi = lax.broadcasted_iota(jnp.int32, full, 2)
    wu = wint_ref[0]
    wm = wint_ref[1]
    wl = wint_ref[2]
    wu_lo = scal_ref[0]
    wm_lo = scal_ref[1]
    wl_lo = scal_ref[2]
    wu_hi = scal_ref[3]
    wm_hi = scal_ref[4]
    wl_hi = scal_ref[5]
    f_ocean = scal_ref[6]
    f_crust = scal_ref[7]

    pres = p_ref[...]
    idn = idn_ref[...]

    p_first = pick(pres, -1, 0)
    p_last = pick(pres, -1, Z - 1)
    pzl = pzl_ref[...]
    pzh = pzh_ref[...]
    zl2 = pick(pzl, -1, 0)
    zl1 = pick(pzl, -1, 1)
    zh1 = pick(pzh, -1, 0)
    zh2 = pick(pzh, -1, 1)
    sfo_ref[...] = sf_ref[...] + 0.5 * (f_ocean * p_last + f_crust * p_first)

    pxl = pxl_ref[...]
    pxh = pxh_ref[...]
    above_x = jnp.concatenate([pres[1:], pxh[0:1]], axis=0)
    below_x = jnp.concatenate([pxl[1:2], pres[:-1]], axis=0)
    slope_x = 0.5 * (above_x - below_x)
    v0 = v_ref[0] - time_step * idn * slope_x
    vx = vx_ref[...]
    ix = ix_ref[...]
    v0_lo = vx[0:1] - time_step * ix[0:1] * (0.5 * (pres[0:1] - pxl[0:1]))
    v0_hi = vx[1:2] - time_step * ix[1:2] * (0.5 * (pxh[1:2] - pres[X - 1 : X]))

    pyl = pyl_ref[...]
    pyh = pyh_ref[...]
    yl1 = pick(pyl, 1, rows - 1)
    yl2 = pick(pyl, 1, rows - 2)
    yh1 = pick(pyh, 1, 0)
    yh2 = pick(pyh, 1, 1)
    p_y0 = pick(pres, 1, 0)
    p_yl = pick(pres, 1, Y - 1)
    above_y = jnp.where(yi == Y - 1, jnp.broadcast_to(yh1, full), pltpu.roll(pres, Y - 1, 1))
    below_y = jnp.where(yi == 0, jnp.broadcast_to(yl1, full), pltpu.roll(pres, 1, 1))
    slope_y = 0.5 * (above_y - below_y)
    v1 = v_ref[1] - time_step * idn * slope_y
    vy = vy_ref[...]
    iy = iy_ref[...]
    v1_lo = pick(vy, 1, 0) - time_step * pick(iy, 1, 0) * (0.5 * (p_y0 - yl2))
    v1_hi = pick(vy, 1, 1) - time_step * pick(iy, 1, 1) * (0.5 * (yh2 - p_yl))

    above_z = jnp.where(zi == Z - 1, jnp.broadcast_to(zh1, full), pltpu.roll(pres, Z - 1, 2))
    below_z = jnp.where(zi == 0, jnp.broadcast_to(zl1, full), pltpu.roll(pres, 1, 2))
    slope_z = wu * above_z + wm * pres + wl * below_z
    v2 = v_ref[2] - time_step * idn * slope_z
    vz = vz_ref[...]
    iz = iz_ref[...]
    v2_lo = pick(vz, -1, 0) - time_step * pick(iz, -1, 0) * (wu_lo * p_first + wm_lo * zl1 + wl_lo * zl2)
    v2_hi = pick(vz, -1, 1) - time_step * pick(iz, -1, 1) * (wu_hi * zh2 + wm_hi * zh1 + wl_hi * p_last)

    vo_ref[0] = v0
    vo_ref[1] = v1
    vo_ref[2] = v2
    vxo_ref[0:1] = v0_lo
    vxo_ref[1:2] = v0_hi
    vyo_ref[...] = pair(v1_lo, v1_hi, vyo_ref.shape, 1)
    vzo_ref[...] = pair(v2_lo, v2_hi, vzo_ref.shape, 2)

    up_x = jnp.concatenate([v0[1:], v0_hi], axis=0)
    down_x = jnp.concatenate([v0_lo, v0[:-1]], axis=0)
    up_y = jnp.where(yi == Y - 1, jnp.broadcast_to(v1_hi, full), pltpu.roll(v1, Y - 1, 1))
    down_y = jnp.where(yi == 0, jnp.broadcast_to(v1_lo, full), pltpu.roll(v1, 1, 1))
    up_z = jnp.where(zi == Z - 1, jnp.broadcast_to(v2_hi, full), pltpu.roll(v2, Z - 1, 2))
    down_z = jnp.where(zi == 0, jnp.broadcast_to(v2_lo, full), pltpu.roll(v2, 1, 2))
    spread = (
        0.5 * (up_x - down_x)
        + 0.5 * (up_y - down_y)
        + (wu * up_z + wm * v2 + wl * down_z)
    )
    new_p = pres - time_step * bulk_ref[...] * spread
    new_p = jnp.where(zi == 0, new_p + jnp.broadcast_to(src_ref[...], full), new_p)
    po_ref[...] = new_p
    sfo_ref[...] = sfo_ref[...] + 0.5 * (
        scal_ref[8] * pick(new_p, -1, Z - 1) + scal_ref[9] * pick(new_p, -1, 0)
    )

    sxu_ref[...] = new_p[X - 2 :]
    sxd_ref[...] = new_p[0:2]
    syu_ref[...] = new_p[:, Y - rows :]
    syd_ref[...] = new_p[:, 0:rows]
    zshape = szu_ref.shape
    szu_ref[...] = pair(pick(new_p, -1, Z - 2), pick(new_p, -1, Z - 1), zshape, 2)
    szd_ref[...] = pair(pick(new_p, -1, 0), pick(new_p, -1, 1), zshape, 2)


def run_step(scal, wint, pres, vel, idn, bulk, src, sf, halos, tracked, media_halo):
    X, Y, Z = pres.shape
    rows = halos[2].shape[1]
    f32 = jnp.float32
    shapes = (
        jax.ShapeDtypeStruct((X, Y, Z), f32),
        jax.ShapeDtypeStruct((3, X, Y, Z), f32),
        jax.ShapeDtypeStruct((X, Y, 1), f32),
        jax.ShapeDtypeStruct((2, Y, Z), f32),
        jax.ShapeDtypeStruct((X, 2, Z), f32),
        jax.ShapeDtypeStruct((X, Y, 2), f32),
        jax.ShapeDtypeStruct((2, Y, Z), f32),
        jax.ShapeDtypeStruct((2, Y, Z), f32),
        jax.ShapeDtypeStruct((X, rows, Z), f32),
        jax.ShapeDtypeStruct((X, rows, Z), f32),
        jax.ShapeDtypeStruct((X, Y, 2), f32),
        jax.ShapeDtypeStruct((X, Y, 2), f32),
    )
    vmem = pl.BlockSpec(memory_space=pltpu.VMEM)
    in_specs = [pl.BlockSpec(memory_space=pltpu.SMEM)] + [vmem] * 19
    cells = X * Y * Z
    return pl.pallas_call(
        step_kernel,
        out_shape=shapes,
        in_specs=in_specs,
        out_specs=[vmem] * len(shapes),
        cost_estimate=pl.CostEstimate(
            flops=80 * cells, transcendentals=0, bytes_accessed=4 * 4 * 12 * cells // 4
        ),
    )(scal, wint, pres, vel, idn, bulk, src, sf, *halos, *tracked, *media_halo)


def seafloor_sums(seafloor, node_weight, node_patch, patch_slot):
    sea_values = node_weight[0, 0] * seafloor.reshape(-1)
    slots = patch_slot[node_patch[0, 0]]
    partial_slip = jnp.zeros((patch_slot.shape[0],), jnp.float32).at[slots].add(sea_values)
    return summed_on_arrival(partial_slip, ("gx", "gy"), 0)


def local(
    pressure,
    velocity,
    inv_density,
    bulk,
    node_weight,
    node_patch,
    patch_slot,
    gauge_x,
    gauge_y,
    gauge_misfit,
):
    X, Y, Z = pressure.shape
    rows = 8
    tiles_z = lax.axis_size("gz")
    depth_index = lax.axis_index("gz")
    first_crust = tiles_z // 2 * Z
    levels = depth_index * Z + jnp.arange(Z, dtype=jnp.int32)
    wint = jnp.stack(depth_weights(levels, first_crust)).reshape(3, 1, 1, Z)
    edge_levels = jnp.stack([depth_index * Z - 1, depth_index * Z + Z])
    edge_w = depth_weights(edge_levels, first_crust)
    ocean_flag = (depth_index == first_crust // Z - 1).astype(jnp.float32)
    crust_flag = (depth_index == first_crust // Z).astype(jnp.float32)
    def scal_of(instant):
        before = 1.0 if instant == 0 else 0.0
        after = 1.0 if instant < ITERS - 1 else 0.0
        return jnp.stack(
            [edge_w[0][0], edge_w[1][0], edge_w[2][0], edge_w[0][1], edge_w[1][1], edge_w[2][1],
             before * ocean_flag, before * crust_flag, after * ocean_flag, after * crust_flag]
        ).astype(jnp.float32)
    top_flag = (depth_index == 0).astype(jnp.float32)
    sources = source_planes(
        gauge_x,
        gauge_y,
        gauge_misfit,
        lax.axis_index("gx") * X,
        lax.axis_index("gy") * Y,
        X,
        Y,
    )
    src_all = (time_step * sources * top_flag)[..., None]

    v0, v1, v2 = velocity[0], velocity[1], velocity[2]
    x_up = jnp.concatenate([pressure[X - 2 :], v0[X - 1 :], inv_density[X - 1 :]], axis=0)
    x_dn = jnp.concatenate([pressure[:2], v0[:1], inv_density[:1]], axis=0)
    y_up = jnp.concatenate(
        [pressure[:, Y - rows :], v1[:, Y - 1 :], inv_density[:, Y - 1 :]], axis=1
    )
    y_dn = jnp.concatenate([pressure[:, :rows], v1[:, :1], inv_density[:, :1]], axis=1)
    z_up = jnp.concatenate(
        [pressure[:, :, Z - 2 :], v2[:, :, Z - 1 :], inv_density[:, :, Z - 1 :]], axis=2
    )
    z_dn = jnp.concatenate([pressure[:, :, :2], v2[:, :, :1], inv_density[:, :, :1]], axis=2)
    rx_lo = shifted_up(x_up, "gx")
    rx_hi = shifted_down(x_dn, "gx")
    ry_lo = shifted_up(y_up, "gy")
    ry_hi = shifted_down(y_dn, "gy")
    rz_lo = shifted_up(z_up, "gz")
    rz_hi = shifted_down(z_dn, "gz")
    halos = (
        rx_lo[:2],
        rx_hi[:2],
        ry_lo[:, :rows],
        ry_hi[:, :rows],
        rz_lo[:, :, :2],
        rz_hi[:, :, :2],
    )
    tracked = (
        jnp.concatenate([rx_lo[2:3], rx_hi[2:3]], axis=0),
        jnp.concatenate([ry_lo[:, rows : rows + 1], ry_hi[:, rows : rows + 1]], axis=1),
        jnp.concatenate([rz_lo[:, :, 2:3], rz_hi[:, :, 2:3]], axis=2),
    )
    media_halo = (
        jnp.concatenate([rx_lo[3:4], rx_hi[3:4]], axis=0),
        jnp.concatenate([ry_lo[:, rows + 1 : rows + 2], ry_hi[:, rows + 1 : rows + 2]], axis=1),
        jnp.concatenate([rz_lo[:, :, 3:4], rz_hi[:, :, 3:4]], axis=2),
    )
    sf = jnp.zeros((X, Y, 1), jnp.float32)
    pres, vel = pressure, velocity
    for instant in range(ITERS):
        if instant > 0:
            halos = (
                shifted_up(sends[0], "gx"),
                shifted_down(sends[1], "gx"),
                shifted_up(sends[2], "gy"),
                shifted_down(sends[3], "gy"),
                shifted_up(sends[4], "gz"),
                shifted_down(sends[5], "gz"),
            )
        outs = run_step(
            scal_of(instant), wint, pres, vel, inv_density, bulk, src_all[instant], sf, halos, tracked,
            media_halo,
        )
        pres, vel, sf = outs[0], outs[1], outs[2]
        tracked = outs[3:6]
        sends = outs[6:12]
        if instant == ITERS - 2:
            owner_sums = seafloor_sums(sf[:, :, 0], node_weight, node_patch, patch_slot)
    slip_grad = summed_on_arrival(owner_sums, "gz", 0)
    return (pres, vel, slip_grad)


def solution(mesh):
    placed = (
        P("gx", "gy", "gz"),
        P(None, "gx", "gy", "gz"),
        P("gx", "gy", "gz"),
        P("gx", "gy", "gz"),
        P("gx", "gy", None),
        P("gx", "gy", None),
        P(),
        P(),
        P(),
        P(),
    )
    return jax.shard_map(
        local,
        mesh=mesh,
        in_specs=placed,
        out_specs=(P("gx", "gy", "gz"), P(None, "gx", "gy", "gz"), P(("gx", "gy", "gz"))),
        check_vma=False,
    )
```

```python
import functools

import jax
import jax.numpy as jnp
from jax import lax
from jax.experimental import pallas as pl
from jax.experimental.pallas import tpu as pltpu
from jax.sharding import PartitionSpec as P

ITERS = 4


time_step = 0.5


def shifted_up(x, axis):
    count = lax.axis_size(axis)
    return lax.ppermute(x, axis, [(i, i + 1) for i in range(count - 1)])


def shifted_down(x, axis):
    count = lax.axis_size(axis)
    return lax.ppermute(x, axis, [(i + 1, i) for i in range(count - 1)])


def in_blocks(x, dim, size):
    before, after = (x.shape[:dim], x.shape[dim + 1 :])
    return jnp.moveaxis(x.reshape(*before, size, -1, *after), dim, 0)


def summed_on_arrival(x, axis, dim):
    size = lax.axis_size(axis)
    parts = lax.all_to_all(in_blocks(x, dim, size), axis, 0, 0, tiled=True)
    return jnp.sum(parts, axis=0)


def depth_weights(levels, first_crust):
    ocean_last = levels == first_crust - 1
    crust_first = levels == first_crust
    weight_above = jnp.where(ocean_last, 0.5, jnp.where(crust_first, 1.0, 0.5)).astype(jnp.float32)
    weight_here = jnp.where(ocean_last, 0.5, jnp.where(crust_first, -1.5, 0.0)).astype(jnp.float32)
    weight_below = jnp.where(ocean_last, -1.0, jnp.where(crust_first, 0.5, -0.5)).astype(
        jnp.float32
    )
    return (weight_above, weight_here, weight_below)


def source_planes(gauge_x, gauge_y, gauge_misfit, start_x, start_y, span_x, span_y):
    local_x = gauge_x - start_x
    local_y = gauge_y - start_y
    inside = (local_x >= 0) & (local_x < span_x) & (local_y >= 0) & (local_y < span_y)
    gauge_cell = jnp.where(inside, local_x * span_y + local_y, -1)
    gauge_table = (
        gauge_cell[:, None] == jnp.arange(span_x * span_y, dtype=jnp.int32)[None, :]
    ).astype(jnp.float32)
    return jnp.dot(gauge_misfit, gauge_table, precision=lax.Precision.HIGHEST).reshape(
        gauge_misfit.shape[0], span_x, span_y
    )


def pick(a, axis, index):
    where = lax.broadcasted_iota(jnp.int32, a.shape, a.ndim + axis if axis < 0 else axis) == index
    return jnp.sum(jnp.where(where, a, 0.0), axis=axis, keepdims=True)


def pair(lo, hi, shape, axis):
    where = lax.broadcasted_iota(jnp.int32, shape, axis) == 0
    return jnp.where(where, jnp.broadcast_to(lo, shape), jnp.broadcast_to(hi, shape))


def step_kernel(
    instant,
    scal_ref,
    wint_ref,
    p_ref,
    v_ref,
    idn_ref,
    bulk_ref,
    src_ref,
    sf_ref,
    pxl_ref,
    pxh_ref,
    pyl_ref,
    pyh_ref,
    pzl_ref,
    pzh_ref,
    vx_ref,
    vy_ref,
    vz_ref,
    ix_ref,
    iy_ref,
    iz_ref,
    po_ref,
    vo_ref,
    sfo_ref,
    vxo_ref,
    vyo_ref,
    vzo_ref,
    sxu_ref,
    sxd_ref,
    syu_ref,
    syd_ref,
    szu_ref,
    szd_ref,
):
    X, Y, Z = p_ref.shape
    rows = pyl_ref.shape[1]
    base = instant * 16
    full = (X, Y, Z)
    yi = lax.broadcasted_iota(jnp.int32, full, 1)
    zi = lax.broadcasted_iota(jnp.int32, full, 2)
    wu = wint_ref[0]
    wm = wint_ref[1]
    wl = wint_ref[2]
    wu_lo = scal_ref[base + 0]
    wm_lo = scal_ref[base + 1]
    wl_lo = scal_ref[base + 2]
    wu_hi = scal_ref[base + 3]
    wm_hi = scal_ref[base + 4]
    wl_hi = scal_ref[base + 5]
    f_ocean = scal_ref[base + 6]
    f_crust = scal_ref[base + 7]

    pres = p_ref[...]
    idn = idn_ref[...]

    p_first = pick(pres, -1, 0)
    p_last = pick(pres, -1, Z - 1)
    pzl = pzl_ref[...]
    pzh = pzh_ref[...]
    zl2 = pick(pzl, -1, 0)
    zl1 = pick(pzl, -1, 1)
    zh1 = pick(pzh, -1, 0)
    zh2 = pick(pzh, -1, 1)
    sfo_ref[...] = sf_ref[...] + 0.5 * (f_ocean * p_last + f_crust * p_first)

    pxl = pxl_ref[...]
    pxh = pxh_ref[...]
    above_x = jnp.concatenate([pres[1:], pxh[0:1]], axis=0)
    below_x = jnp.concatenate([pxl[1:2], pres[:-1]], axis=0)
    slope_x = 0.5 * (above_x - below_x)
    v0 = v_ref[0] - time_step * idn * slope_x
    vx = vx_ref[...]
    ix = ix_ref[...]
    v0_lo = vx[0:1] - time_step * ix[0:1] * (0.5 * (pres[0:1] - pxl[0:1]))
    v0_hi = vx[1:2] - time_step * ix[1:2] * (0.5 * (pxh[1:2] - pres[X - 1 : X]))

    pyl = pyl_ref[...]
    pyh = pyh_ref[...]
    yl1 = pick(pyl, 1, rows - 1)
    yl2 = pick(pyl, 1, rows - 2)
    yh1 = pick(pyh, 1, 0)
    yh2 = pick(pyh, 1, 1)
    p_y0 = pick(pres, 1, 0)
    p_yl = pick(pres, 1, Y - 1)
    above_y = jnp.where(yi == Y - 1, jnp.broadcast_to(yh1, full), pltpu.roll(pres, Y - 1, 1))
    below_y = jnp.where(yi == 0, jnp.broadcast_to(yl1, full), pltpu.roll(pres, 1, 1))
    slope_y = 0.5 * (above_y - below_y)
    v1 = v_ref[1] - time_step * idn * slope_y
    vy = vy_ref[...]
    iy = iy_ref[...]
    v1_lo = pick(vy, 1, 0) - time_step * pick(iy, 1, 0) * (0.5 * (p_y0 - yl2))
    v1_hi = pick(vy, 1, 1) - time_step * pick(iy, 1, 1) * (0.5 * (yh2 - p_yl))

    above_z = jnp.where(zi == Z - 1, jnp.broadcast_to(zh1, full), pltpu.roll(pres, Z - 1, 2))
    below_z = jnp.where(zi == 0, jnp.broadcast_to(zl1, full), pltpu.roll(pres, 1, 2))
    slope_z = wu * above_z + wm * pres + wl * below_z
    v2 = v_ref[2] - time_step * idn * slope_z
    vz = vz_ref[...]
    iz = iz_ref[...]
    v2_lo = pick(vz, -1, 0) - time_step * pick(iz, -1, 0) * (wu_lo * p_first + wm_lo * zl1 + wl_lo * zl2)
    v2_hi = pick(vz, -1, 1) - time_step * pick(iz, -1, 1) * (wu_hi * zh2 + wm_hi * zh1 + wl_hi * p_last)

    vo_ref[0] = v0
    vo_ref[1] = v1
    vo_ref[2] = v2
    vxo_ref[0:1] = v0_lo
    vxo_ref[1:2] = v0_hi
    vyo_ref[...] = pair(v1_lo, v1_hi, vyo_ref.shape, 1)
    vzo_ref[...] = pair(v2_lo, v2_hi, vzo_ref.shape, 2)

    up_x = jnp.concatenate([v0[1:], v0_hi], axis=0)
    down_x = jnp.concatenate([v0_lo, v0[:-1]], axis=0)
    up_y = jnp.where(yi == Y - 1, jnp.broadcast_to(v1_hi, full), pltpu.roll(v1, Y - 1, 1))
    down_y = jnp.where(yi == 0, jnp.broadcast_to(v1_lo, full), pltpu.roll(v1, 1, 1))
    up_z = jnp.where(zi == Z - 1, jnp.broadcast_to(v2_hi, full), pltpu.roll(v2, Z - 1, 2))
    down_z = jnp.where(zi == 0, jnp.broadcast_to(v2_lo, full), pltpu.roll(v2, 1, 2))
    spread = (
        0.5 * (up_x - down_x)
        + 0.5 * (up_y - down_y)
        + (wu * up_z + wm * v2 + wl * down_z)
    )
    new_p = pres - time_step * bulk_ref[...] * spread
    new_p = jnp.where(zi == 0, new_p + jnp.broadcast_to(src_ref[instant], full), new_p)
    po_ref[...] = new_p
    sfo_ref[...] = sfo_ref[...] + 0.5 * (
        scal_ref[base + 8] * pick(new_p, -1, Z - 1) + scal_ref[base + 9] * pick(new_p, -1, 0)
    )

    sxu_ref[...] = new_p[X - 2 :]
    sxd_ref[...] = new_p[0:2]
    syu_ref[...] = new_p[:, Y - rows :]
    syd_ref[...] = new_p[:, 0:rows]
    zshape = szu_ref.shape
    szu_ref[...] = pair(pick(new_p, -1, Z - 2), pick(new_p, -1, Z - 1), zshape, 2)
    szd_ref[...] = pair(pick(new_p, -1, 0), pick(new_p, -1, 1), zshape, 2)


def run_step(instant, scal, wint, pres, vel, idn, bulk, src, sf, halos, tracked, media_halo):
    X, Y, Z = pres.shape
    rows = halos[2].shape[1]
    f32 = jnp.float32
    shapes = (
        jax.ShapeDtypeStruct((X, Y, Z), f32),
        jax.ShapeDtypeStruct((3, X, Y, Z), f32),
        jax.ShapeDtypeStruct((X, Y, 1), f32),
        jax.ShapeDtypeStruct((2, Y, Z), f32),
        jax.ShapeDtypeStruct((X, 2, Z), f32),
        jax.ShapeDtypeStruct((X, Y, 2), f32),
        jax.ShapeDtypeStruct((2, Y, Z), f32),
        jax.ShapeDtypeStruct((2, Y, Z), f32),
        jax.ShapeDtypeStruct((X, rows, Z), f32),
        jax.ShapeDtypeStruct((X, rows, Z), f32),
        jax.ShapeDtypeStruct((X, Y, 2), f32),
        jax.ShapeDtypeStruct((X, Y, 2), f32),
    )
    vmem = pl.BlockSpec(memory_space=pltpu.VMEM)
    in_specs = [pl.BlockSpec(memory_space=pltpu.SMEM)] + [vmem] * 19
    cells = X * Y * Z
    return pl.pallas_call(
        functools.partial(step_kernel, instant),
        out_shape=shapes,
        in_specs=in_specs,
        out_specs=[vmem] * len(shapes),
        cost_estimate=pl.CostEstimate(
            flops=80 * cells, transcendentals=0, bytes_accessed=4 * 4 * 12 * cells // 4
        ),
    )(scal, wint, pres, vel, idn, bulk, src, sf, *halos, *tracked, *media_halo)


def seafloor_sums(seafloor, node_weight, node_patch, patch_slot):
    sea_values = node_weight[0, 0] * seafloor.reshape(-1)
    slots = patch_slot[node_patch[0, 0]]
    partial_slip = jnp.zeros((patch_slot.shape[0],), jnp.float32).at[slots].add(sea_values)
    return summed_on_arrival(partial_slip, ("gx", "gy"), 0)


def local(
    pressure,
    velocity,
    inv_density,
    bulk,
    node_weight,
    node_patch,
    patch_slot,
    gauge_x,
    gauge_y,
    gauge_misfit,
):
    X, Y, Z = pressure.shape
    rows = 8
    tiles_z = lax.axis_size("gz")
    depth_index = lax.axis_index("gz")
    first_crust = tiles_z // 2 * Z
    levels = depth_index * Z + jnp.arange(Z, dtype=jnp.int32)
    wint = jnp.stack(depth_weights(levels, first_crust)).reshape(3, 1, 1, Z)
    entry = lax.broadcasted_iota(jnp.int32, (ITERS, 16), 1)
    step_at = lax.broadcasted_iota(jnp.int32, (ITERS, 16), 0)
    edge_level = depth_index * Z + jnp.where(entry < 3, -1, Z)
    e_up, e_mid, e_low = depth_weights(edge_level, first_crust)
    kind = entry % 3
    edge_value = jnp.where(kind == 0, e_up, jnp.where(kind == 1, e_mid, e_low))
    ocean = depth_index == first_crust // Z - 1
    crust = depth_index == first_crust // Z
    before = step_at == 0
    after = step_at < ITERS - 1
    flag_value = jnp.where(
        entry == 6, before & ocean,
        jnp.where(entry == 7, before & crust,
                  jnp.where(entry == 8, after & ocean, after & crust)),
    ).astype(jnp.float32)
    scal_all = jnp.where(entry < 6, edge_value, jnp.where(entry < 10, flag_value, 0.0))
    scal_all = scal_all.astype(jnp.float32).reshape(ITERS * 16)
    top_flag = (depth_index == 0).astype(jnp.float32)
    sources = source_planes(
        gauge_x,
        gauge_y,
        gauge_misfit,
        lax.axis_index("gx") * X,
        lax.axis_index("gy") * Y,
        X,
        Y,
    )
    src_all = (time_step * sources * top_flag)[..., None]

    v0, v1, v2 = velocity[0], velocity[1], velocity[2]
    x_up = jnp.concatenate([pressure[X - 2 :], v0[X - 1 :], inv_density[X - 1 :]], axis=0)
    x_dn = jnp.concatenate([pressure[:2], v0[:1], inv_density[:1]], axis=0)
    y_up = jnp.concatenate(
        [pressure[:, Y - rows :], v1[:, Y - 1 :], inv_density[:, Y - 1 :]], axis=1
    )
    y_dn = jnp.concatenate([pressure[:, :rows], v1[:, :1], inv_density[:, :1]], axis=1)
    z_up = jnp.concatenate(
        [pressure[:, :, Z - 2 :], v2[:, :, Z - 1 :], inv_density[:, :, Z - 1 :]], axis=2
    )
    z_dn = jnp.concatenate([pressure[:, :, :2], v2[:, :, :1], inv_density[:, :, :1]], axis=2)
    rx_lo = shifted_up(x_up, "gx")
    rx_hi = shifted_down(x_dn, "gx")
    ry_lo = shifted_up(y_up, "gy")
    ry_hi = shifted_down(y_dn, "gy")
    rz_lo = shifted_up(z_up, "gz")
    rz_hi = shifted_down(z_dn, "gz")
    halos = (
        rx_lo[:2],
        rx_hi[:2],
        ry_lo[:, :rows],
        ry_hi[:, :rows],
        rz_lo[:, :, :2],
        rz_hi[:, :, :2],
    )
    tracked = (
        jnp.concatenate([rx_lo[2:3], rx_hi[2:3]], axis=0),
        jnp.concatenate([ry_lo[:, rows : rows + 1], ry_hi[:, rows : rows + 1]], axis=1),
        jnp.concatenate([rz_lo[:, :, 2:3], rz_hi[:, :, 2:3]], axis=2),
    )
    media_halo = (
        jnp.concatenate([rx_lo[3:4], rx_hi[3:4]], axis=0),
        jnp.concatenate([ry_lo[:, rows + 1 : rows + 2], ry_hi[:, rows + 1 : rows + 2]], axis=1),
        jnp.concatenate([rz_lo[:, :, 3:4], rz_hi[:, :, 3:4]], axis=2),
    )
    sf = jnp.zeros((X, Y, 1), jnp.float32)
    pres, vel = pressure, velocity
    for instant in range(ITERS):
        if instant > 0:
            halos = (
                shifted_up(sends[0], "gx"),
                shifted_down(sends[1], "gx"),
                shifted_up(sends[2], "gy"),
                shifted_down(sends[3], "gy"),
                shifted_up(sends[4], "gz"),
                shifted_down(sends[5], "gz"),
            )
        outs = run_step(
            instant, scal_all, wint, pres, vel, inv_density, bulk, src_all, sf, halos, tracked,
            media_halo,
        )
        pres, vel, sf = outs[0], outs[1], outs[2]
        tracked = outs[3:6]
        sends = outs[6:12]
        if instant == ITERS - 2:
            owner_sums = seafloor_sums(sf[:, :, 0], node_weight, node_patch, patch_slot)
    slip_grad = summed_on_arrival(owner_sums, "gz", 0)
    return (pres, vel, slip_grad)


def solution(mesh):
    placed = (
        P("gx", "gy", "gz"),
        P(None, "gx", "gy", "gz"),
        P("gx", "gy", "gz"),
        P("gx", "gy", "gz"),
        P("gx", "gy", None),
        P("gx", "gy", None),
        P(),
        P(),
        P(),
        P(),
    )
    return jax.shard_map(
        local,
        mesh=mesh,
        in_specs=placed,
        out_specs=(P("gx", "gy", "gz"), P(None, "gx", "gy", "gz"), P(("gx", "gy", "gz"))),
        check_vma=False,
    )
```

```python
import functools

import jax
import jax.numpy as jnp
from jax import lax
from jax.experimental import pallas as pl
from jax.experimental.pallas import tpu as pltpu
from jax.sharding import PartitionSpec as P

ITERS = 4


time_step = 0.5


def shifted_up(x, axis):
    count = lax.axis_size(axis)
    return lax.ppermute(x, axis, [(i, i + 1) for i in range(count - 1)])


def shifted_down(x, axis):
    count = lax.axis_size(axis)
    return lax.ppermute(x, axis, [(i + 1, i) for i in range(count - 1)])


def in_blocks(x, dim, size):
    before, after = (x.shape[:dim], x.shape[dim + 1 :])
    return jnp.moveaxis(x.reshape(*before, size, -1, *after), dim, 0)


def summed_on_arrival(x, axis, dim):
    size = lax.axis_size(axis)
    parts = lax.all_to_all(in_blocks(x, dim, size), axis, 0, 0, tiled=True)
    return jnp.sum(parts, axis=0)


def depth_weights(levels, first_crust):
    ocean_last = levels == first_crust - 1
    crust_first = levels == first_crust
    weight_above = jnp.where(ocean_last, 0.5, jnp.where(crust_first, 1.0, 0.5)).astype(jnp.float32)
    weight_here = jnp.where(ocean_last, 0.5, jnp.where(crust_first, -1.5, 0.0)).astype(jnp.float32)
    weight_below = jnp.where(ocean_last, -1.0, jnp.where(crust_first, 0.5, -0.5)).astype(
        jnp.float32
    )
    return (weight_above, weight_here, weight_below)


def source_planes(gauge_x, gauge_y, gauge_misfit, start_x, start_y, span_x, span_y):
    local_x = gauge_x - start_x
    local_y = gauge_y - start_y
    inside = (local_x >= 0) & (local_x < span_x) & (local_y >= 0) & (local_y < span_y)
    gauge_cell = jnp.where(inside, local_x * span_y + local_y, -1)
    gauge_table = (
        gauge_cell[:, None] == jnp.arange(span_x * span_y, dtype=jnp.int32)[None, :]
    ).astype(jnp.float32)
    return jnp.dot(gauge_misfit, gauge_table, precision=lax.Precision.HIGHEST).reshape(
        gauge_misfit.shape[0], span_x, span_y
    )


def pick(a, axis, index):
    where = lax.broadcasted_iota(jnp.int32, a.shape, a.ndim + axis if axis < 0 else axis) == index
    return jnp.sum(jnp.where(where, a, 0.0), axis=axis, keepdims=True)


def pair(lo, hi, shape, axis):
    where = lax.broadcasted_iota(jnp.int32, shape, axis) == 0
    return jnp.where(where, jnp.broadcast_to(lo, shape), jnp.broadcast_to(hi, shape))


def step_kernel(
    instant,
    scal_ref,
    wint_ref,
    p_ref,
    v_ref,
    idn_ref,
    bulk_ref,
    src_ref,
    sf_ref,
    pxl_ref,
    pxh_ref,
    pyl_ref,
    pyh_ref,
    pzl_ref,
    pzh_ref,
    vx_ref,
    vy_ref,
    vz_ref,
    ix_ref,
    iy_ref,
    iz_ref,
    po_ref,
    vo_ref,
    sfo_ref,
    vxo_ref,
    vyo_ref,
    vzo_ref,
    sxu_ref,
    sxd_ref,
    syu_ref,
    syd_ref,
    szu_ref,
    szd_ref,
):
    X, Y, Z = p_ref.shape
    rows = pyl_ref.shape[1]
    base = instant * 16
    full = (X, Y, Z)
    yi = lax.broadcasted_iota(jnp.int32, full, 1)
    zi = lax.broadcasted_iota(jnp.int32, full, 2)
    wu = wint_ref[0]
    wm = wint_ref[1]
    wl = wint_ref[2]
    wu_lo = scal_ref[base + 0]
    wm_lo = scal_ref[base + 1]
    wl_lo = scal_ref[base + 2]
    wu_hi = scal_ref[base + 3]
    wm_hi = scal_ref[base + 4]
    wl_hi = scal_ref[base + 5]
    f_ocean = scal_ref[base + 6]
    f_crust = scal_ref[base + 7]

    pres = p_ref[...]
    idn = idn_ref[...]

    p_first = pick(pres, -1, 0)
    p_last = pick(pres, -1, Z - 1)
    pzl = pzl_ref[...]
    pzh = pzh_ref[...]
    zl2 = pick(pzl, -1, 0)
    zl1 = pick(pzl, -1, 1)
    zh1 = pick(pzh, -1, 0)
    zh2 = pick(pzh, -1, 1)
    sfo_ref[...] = sf_ref[...] + 0.5 * (f_ocean * (p_last + zh1) + f_crust * (zl1 + p_first))

    pxl = pxl_ref[...]
    pxh = pxh_ref[...]
    above_x = jnp.concatenate([pres[1:], pxh[0:1]], axis=0)
    below_x = jnp.concatenate([pxl[1:2], pres[:-1]], axis=0)
    slope_x = 0.5 * (above_x - below_x)
    v0 = v_ref[0] - time_step * idn * slope_x
    vx = vx_ref[...]
    ix = ix_ref[...]
    v0_lo = vx[0:1] - time_step * ix[0:1] * (0.5 * (pres[0:1] - pxl[0:1]))
    v0_hi = vx[1:2] - time_step * ix[1:2] * (0.5 * (pxh[1:2] - pres[X - 1 : X]))

    pyl = pyl_ref[...]
    pyh = pyh_ref[...]
    yl1 = pick(pyl, 1, rows - 1)
    yl2 = pick(pyl, 1, rows - 2)
    yh1 = pick(pyh, 1, 0)
    yh2 = pick(pyh, 1, 1)
    p_y0 = pick(pres, 1, 0)
    p_yl = pick(pres, 1, Y - 1)
    above_y = jnp.where(yi == Y - 1, jnp.broadcast_to(yh1, full), pltpu.roll(pres, Y - 1, 1))
    below_y = jnp.where(yi == 0, jnp.broadcast_to(yl1, full), pltpu.roll(pres, 1, 1))
    slope_y = 0.5 * (above_y - below_y)
    v1 = v_ref[1] - time_step * idn * slope_y
    vy = vy_ref[...]
    iy = iy_ref[...]
    v1_lo = pick(vy, 1, 0) - time_step * pick(iy, 1, 0) * (0.5 * (p_y0 - yl2))
    v1_hi = pick(vy, 1, 1) - time_step * pick(iy, 1, 1) * (0.5 * (yh2 - p_yl))

    above_z = jnp.where(zi == Z - 1, jnp.broadcast_to(zh1, full), pltpu.roll(pres, Z - 1, 2))
    below_z = jnp.where(zi == 0, jnp.broadcast_to(zl1, full), pltpu.roll(pres, 1, 2))
    slope_z = wu * above_z + wm * pres + wl * below_z
    v2 = v_ref[2] - time_step * idn * slope_z
    vz = vz_ref[...]
    iz = iz_ref[...]
    v2_lo = pick(vz, -1, 0) - time_step * pick(iz, -1, 0) * (wu_lo * p_first + wm_lo * zl1 + wl_lo * zl2)
    v2_hi = pick(vz, -1, 1) - time_step * pick(iz, -1, 1) * (wu_hi * zh2 + wm_hi * zh1 + wl_hi * p_last)

    vo_ref[0] = v0
    vo_ref[1] = v1
    vo_ref[2] = v2
    vxo_ref[0:1] = v0_lo
    vxo_ref[1:2] = v0_hi
    vyo_ref[...] = pair(v1_lo, v1_hi, vyo_ref.shape, 1)
    vzo_ref[...] = pair(v2_lo, v2_hi, vzo_ref.shape, 2)

    up_x = jnp.concatenate([v0[1:], v0_hi], axis=0)
    down_x = jnp.concatenate([v0_lo, v0[:-1]], axis=0)
    up_y = jnp.where(yi == Y - 1, jnp.broadcast_to(v1_hi, full), pltpu.roll(v1, Y - 1, 1))
    down_y = jnp.where(yi == 0, jnp.broadcast_to(v1_lo, full), pltpu.roll(v1, 1, 1))
    up_z = jnp.where(zi == Z - 1, jnp.broadcast_to(v2_hi, full), pltpu.roll(v2, Z - 1, 2))
    down_z = jnp.where(zi == 0, jnp.broadcast_to(v2_lo, full), pltpu.roll(v2, 1, 2))
    spread = (
        0.5 * (up_x - down_x)
        + 0.5 * (up_y - down_y)
        + (wu * up_z + wm * v2 + wl * down_z)
    )
    new_p = pres - time_step * bulk_ref[...] * spread
    new_p = jnp.where(zi == 0, new_p + jnp.broadcast_to(src_ref[instant], full), new_p)
    po_ref[...] = new_p

    sxu_ref[...] = new_p[X - 2 :]
    sxd_ref[...] = new_p[0:2]
    syu_ref[...] = new_p[:, Y - rows :]
    syd_ref[...] = new_p[:, 0:rows]
    zshape = szu_ref.shape
    szu_ref[...] = pair(pick(new_p, -1, Z - 2), pick(new_p, -1, Z - 1), zshape, 2)
    szd_ref[...] = pair(pick(new_p, -1, 0), pick(new_p, -1, 1), zshape, 2)


def run_step(instant, scal, wint, pres, vel, idn, bulk, src, sf, halos, tracked, media_halo):
    X, Y, Z = pres.shape
    rows = halos[2].shape[1]
    f32 = jnp.float32
    shapes = (
        jax.ShapeDtypeStruct((X, Y, Z), f32),
        jax.ShapeDtypeStruct((3, X, Y, Z), f32),
        jax.ShapeDtypeStruct((X, Y, 1), f32),
        jax.ShapeDtypeStruct((2, Y, Z), f32),
        jax.ShapeDtypeStruct((X, 2, Z), f32),
        jax.ShapeDtypeStruct((X, Y, 2), f32),
        jax.ShapeDtypeStruct((2, Y, Z), f32),
        jax.ShapeDtypeStruct((2, Y, Z), f32),
        jax.ShapeDtypeStruct((X, rows, Z), f32),
        jax.ShapeDtypeStruct((X, rows, Z), f32),
        jax.ShapeDtypeStruct((X, Y, 2), f32),
        jax.ShapeDtypeStruct((X, Y, 2), f32),
    )
    vmem = pl.BlockSpec(memory_space=pltpu.VMEM)
    in_specs = [pl.BlockSpec(memory_space=pltpu.SMEM)] + [vmem] * 19
    cells = X * Y * Z
    return pl.pallas_call(
        functools.partial(step_kernel, instant),
        out_shape=shapes,
        in_specs=in_specs,
        out_specs=[vmem] * len(shapes),
        cost_estimate=pl.CostEstimate(
            flops=80 * cells, transcendentals=0, bytes_accessed=4 * 4 * 12 * cells // 4
        ),
    )(scal, wint, pres, vel, idn, bulk, src, sf, *halos, *tracked, *media_halo)


def seafloor_sums(seafloor, node_weight, node_patch, patch_slot):
    sea_values = node_weight[0, 0] * seafloor.reshape(-1)
    slots = patch_slot[node_patch[0, 0]]
    partial_slip = jnp.zeros((patch_slot.shape[0],), jnp.float32).at[slots].add(sea_values)
    return summed_on_arrival(partial_slip, ("gx", "gy"), 0)


def local(
    pressure,
    velocity,
    inv_density,
    bulk,
    node_weight,
    node_patch,
    patch_slot,
    gauge_x,
    gauge_y,
    gauge_misfit,
):
    X, Y, Z = pressure.shape
    rows = 8
    tiles_z = lax.axis_size("gz")
    depth_index = lax.axis_index("gz")
    first_crust = tiles_z // 2 * Z
    levels = depth_index * Z + jnp.arange(Z, dtype=jnp.int32)
    wint = jnp.stack(depth_weights(levels, first_crust)).reshape(3, 1, 1, Z)
    entry = lax.broadcasted_iota(jnp.int32, (ITERS, 16), 1)
    step_at = lax.broadcasted_iota(jnp.int32, (ITERS, 16), 0)
    edge_level = depth_index * Z + jnp.where(entry < 3, -1, Z)
    e_up, e_mid, e_low = depth_weights(edge_level, first_crust)
    kind = entry % 3
    edge_value = jnp.where(kind == 0, e_up, jnp.where(kind == 1, e_mid, e_low))
    ocean = depth_index == first_crust // Z - 1
    crust = depth_index == first_crust // Z
    before = step_at < ITERS - 1
    after = step_at < 0
    flag_value = jnp.where(
        entry == 6, before & ocean,
        jnp.where(entry == 7, before & crust,
                  jnp.where(entry == 8, after & ocean, after & crust)),
    ).astype(jnp.float32)
    scal_all = jnp.where(entry < 6, edge_value, jnp.where(entry < 10, flag_value, 0.0))
    scal_all = scal_all.astype(jnp.float32).reshape(ITERS * 16)
    top_flag = (depth_index == 0).astype(jnp.float32)
    sources = source_planes(
        gauge_x,
        gauge_y,
        gauge_misfit,
        lax.axis_index("gx") * X,
        lax.axis_index("gy") * Y,
        X,
        Y,
    )
    src_all = (time_step * sources * top_flag)[..., None]

    v0, v1, v2 = velocity[0], velocity[1], velocity[2]
    x_up = jnp.concatenate([pressure[X - 2 :], v0[X - 1 :], inv_density[X - 1 :]], axis=0)
    x_dn = jnp.concatenate([pressure[:2], v0[:1], inv_density[:1]], axis=0)
    y_up = jnp.concatenate(
        [pressure[:, Y - rows :], v1[:, Y - 1 :], inv_density[:, Y - 1 :]], axis=1
    )
    y_dn = jnp.concatenate([pressure[:, :rows], v1[:, :1], inv_density[:, :1]], axis=1)
    z_up = jnp.concatenate(
        [pressure[:, :, Z - 2 :], v2[:, :, Z - 1 :], inv_density[:, :, Z - 1 :]], axis=2
    )
    z_dn = jnp.concatenate([pressure[:, :, :2], v2[:, :, :1], inv_density[:, :, :1]], axis=2)
    rx_lo = shifted_up(x_up, "gx")
    rx_hi = shifted_down(x_dn, "gx")
    ry_lo = shifted_up(y_up, "gy")
    ry_hi = shifted_down(y_dn, "gy")
    rz_lo = shifted_up(z_up, "gz")
    rz_hi = shifted_down(z_dn, "gz")
    halos = (
        rx_lo[:2],
        rx_hi[:2],
        ry_lo[:, :rows],
        ry_hi[:, :rows],
        rz_lo[:, :, :2],
        rz_hi[:, :, :2],
    )
    tracked = (
        jnp.concatenate([rx_lo[2:3], rx_hi[2:3]], axis=0),
        jnp.concatenate([ry_lo[:, rows : rows + 1], ry_hi[:, rows : rows + 1]], axis=1),
        jnp.concatenate([rz_lo[:, :, 2:3], rz_hi[:, :, 2:3]], axis=2),
    )
    media_halo = (
        jnp.concatenate([rx_lo[3:4], rx_hi[3:4]], axis=0),
        jnp.concatenate([ry_lo[:, rows + 1 : rows + 2], ry_hi[:, rows + 1 : rows + 2]], axis=1),
        jnp.concatenate([rz_lo[:, :, 3:4], rz_hi[:, :, 3:4]], axis=2),
    )
    sf = jnp.zeros((X, Y, 1), jnp.float32)
    pres, vel = pressure, velocity
    for instant in range(ITERS):
        if instant > 0:
            halos = (
                shifted_up(sends[0], "gx"),
                shifted_down(sends[1], "gx"),
                shifted_up(sends[2], "gy"),
                shifted_down(sends[3], "gy"),
                shifted_up(sends[4], "gz"),
                shifted_down(sends[5], "gz"),
            )
        if instant == ITERS - 1:
            ocean = (depth_index == first_crust // Z - 1).astype(jnp.float32)
            crust = (depth_index == first_crust // Z).astype(jnp.float32)
            sf_last = sf + 0.5 * (
                ocean * (sends[4][:, :, 1:2] + halos[5][:, :, 0:1])
                + crust * (halos[4][:, :, 1:2] + sends[5][:, :, 0:1])
            )
            owner_sums = seafloor_sums(sf_last[:, :, 0], node_weight, node_patch, patch_slot)
        outs = run_step(
            instant, scal_all, wint, pres, vel, inv_density, bulk, src_all, sf, halos, tracked,
            media_halo,
        )
        pres, vel, sf = outs[0], outs[1], outs[2]
        tracked = outs[3:6]
        sends = outs[6:12]
    ocean_plane = first_crust // Z - 1
    crust_plane = first_crust // Z
    spread_out = lax.ppermute(
        owner_sums, "gz", [(ocean_plane, ocean_plane - 1), (crust_plane, crust_plane + 1)]
    )
    inner = (depth_index == ocean_plane) | (depth_index == crust_plane)
    owner_sums = jnp.where(inner, owner_sums, spread_out)
    piece = owner_sums.shape[0] // tiles_z
    slip_grad = lax.dynamic_slice_in_dim(owner_sums, depth_index * piece, piece)
    return (pres, vel, slip_grad)


def solution(mesh):
    placed = (
        P("gx", "gy", "gz"),
        P(None, "gx", "gy", "gz"),
        P("gx", "gy", "gz"),
        P("gx", "gy", "gz"),
        P("gx", "gy", None),
        P("gx", "gy", None),
        P(),
        P(),
        P(),
        P(),
    )
    return jax.shard_map(
        local,
        mesh=mesh,
        in_specs=placed,
        out_specs=(P("gx", "gy", "gz"), P(None, "gx", "gy", "gz"), P(("gx", "gy", "gz"))),
        check_vma=False,
    )
```

```python
import functools

import jax
import jax.numpy as jnp
from jax import lax
from jax.experimental import pallas as pl
from jax.experimental.pallas import tpu as pltpu
from jax.sharding import PartitionSpec as P

ITERS = 4


time_step = 0.5


def shifted_up(x, axis):
    count = lax.axis_size(axis)
    return lax.ppermute(x, axis, [(i, i + 1) for i in range(count - 1)])


def shifted_down(x, axis):
    count = lax.axis_size(axis)
    return lax.ppermute(x, axis, [(i + 1, i) for i in range(count - 1)])


def in_blocks(x, dim, size):
    before, after = (x.shape[:dim], x.shape[dim + 1 :])
    return jnp.moveaxis(x.reshape(*before, size, -1, *after), dim, 0)


def summed_on_arrival(x, axis, dim):
    size = lax.axis_size(axis)
    parts = lax.all_to_all(in_blocks(x, dim, size), axis, 0, 0, tiled=True)
    return jnp.sum(parts, axis=0)


def depth_weights(levels, first_crust):
    ocean_last = levels == first_crust - 1
    crust_first = levels == first_crust
    weight_above = jnp.where(ocean_last, 0.5, jnp.where(crust_first, 1.0, 0.5)).astype(jnp.float32)
    weight_here = jnp.where(ocean_last, 0.5, jnp.where(crust_first, -1.5, 0.0)).astype(jnp.float32)
    weight_below = jnp.where(ocean_last, -1.0, jnp.where(crust_first, 0.5, -0.5)).astype(
        jnp.float32
    )
    return (weight_above, weight_here, weight_below)


def source_planes(gauge_x, gauge_y, gauge_misfit, start_x, start_y, span_x, span_y):
    local_x = gauge_x - start_x
    local_y = gauge_y - start_y
    inside = (local_x >= 0) & (local_x < span_x) & (local_y >= 0) & (local_y < span_y)
    gauge_cell = jnp.where(inside, local_x * span_y + local_y, -1)
    gauge_table = (
        gauge_cell[:, None] == jnp.arange(span_x * span_y, dtype=jnp.int32)[None, :]
    ).astype(jnp.float32)
    return jnp.dot(gauge_misfit, gauge_table, precision=lax.Precision.HIGHEST).reshape(
        gauge_misfit.shape[0], span_x, span_y
    )


def pick(a, axis, index):
    where = lax.broadcasted_iota(jnp.int32, a.shape, a.ndim + axis if axis < 0 else axis) == index
    return jnp.sum(jnp.where(where, a, 0.0), axis=axis, keepdims=True)


def pair(lo, hi, shape, axis):
    where = lax.broadcasted_iota(jnp.int32, shape, axis) == 0
    return jnp.where(where, jnp.broadcast_to(lo, shape), jnp.broadcast_to(hi, shape))


def step_kernel(
    instant,
    scal_ref,
    wint_ref,
    p_ref,
    v_ref,
    idn_ref,
    bulk_ref,
    src_ref,
    sf_ref,
    pxl_ref,
    pxh_ref,
    pyl_ref,
    pyh_ref,
    pzl_ref,
    pzh_ref,
    vx_ref,
    vy_ref,
    vz_ref,
    ix_ref,
    iy_ref,
    iz_ref,
    po_ref,
    vo_ref,
    sfo_ref,
    vxo_ref,
    vyo_ref,
    vzo_ref,
    sxu_ref,
    sxd_ref,
    syu_ref,
    syd_ref,
    szu_ref,
    szd_ref,
):
    X, Y, Z = p_ref.shape
    rows = pyl_ref.shape[1]
    base = instant * 16
    full = (X, Y, Z)
    yi = lax.broadcasted_iota(jnp.int32, full, 1)
    zi = lax.broadcasted_iota(jnp.int32, full, 2)
    wu = wint_ref[0]
    wm = wint_ref[1]
    wl = wint_ref[2]
    wu_lo = scal_ref[base + 0]
    wm_lo = scal_ref[base + 1]
    wl_lo = scal_ref[base + 2]
    wu_hi = scal_ref[base + 3]
    wm_hi = scal_ref[base + 4]
    wl_hi = scal_ref[base + 5]
    f_ocean = scal_ref[base + 6]
    f_crust = scal_ref[base + 7]

    pres = p_ref[...]
    idn = idn_ref[...]

    p_first = pick(pres, -1, 0)
    p_last = pick(pres, -1, Z - 1)
    pzl = pzl_ref[...]
    pzh = pzh_ref[...]
    zl2 = pick(pzl, -1, 0)
    zl1 = pick(pzl, -1, 1)
    zh1 = pick(pzh, -1, 0)
    zh2 = pick(pzh, -1, 1)
    sfo_ref[...] = sf_ref[...] + 0.5 * (f_ocean * (p_last + zh1) + f_crust * (zl1 + p_first))

    pxl = pxl_ref[...]
    pxh = pxh_ref[...]
    above_x = jnp.concatenate([pres[1:], pxh[0:1]], axis=0)
    below_x = jnp.concatenate([pxl[1:2], pres[:-1]], axis=0)
    slope_x = 0.5 * (above_x - below_x)
    v0 = v_ref[0] - time_step * idn * slope_x
    vx = vx_ref[...]
    ix = ix_ref[...]
    v0_lo = vx[0:1] - time_step * ix[0:1] * (0.5 * (pres[0:1] - pxl[0:1]))
    v0_hi = vx[1:2] - time_step * ix[1:2] * (0.5 * (pxh[1:2] - pres[X - 1 : X]))

    pyl = pyl_ref[...]
    pyh = pyh_ref[...]
    yl1 = pick(pyl, 1, rows - 1)
    yl2 = pick(pyl, 1, rows - 2)
    yh1 = pick(pyh, 1, 0)
    yh2 = pick(pyh, 1, 1)
    p_y0 = pick(pres, 1, 0)
    p_yl = pick(pres, 1, Y - 1)
    above_y = jnp.where(yi == Y - 1, jnp.broadcast_to(yh1, full), pltpu.roll(pres, Y - 1, 1))
    below_y = jnp.where(yi == 0, jnp.broadcast_to(yl1, full), pltpu.roll(pres, 1, 1))
    slope_y = 0.5 * (above_y - below_y)
    v1 = v_ref[1] - time_step * idn * slope_y
    vy = vy_ref[...]
    iy = iy_ref[...]
    v1_lo = pick(vy, 1, 0) - time_step * pick(iy, 1, 0) * (0.5 * (p_y0 - yl2))
    v1_hi = pick(vy, 1, 1) - time_step * pick(iy, 1, 1) * (0.5 * (yh2 - p_yl))

    above_z = jnp.where(zi == Z - 1, jnp.broadcast_to(zh1, full), pltpu.roll(pres, Z - 1, 2))
    below_z = jnp.where(zi == 0, jnp.broadcast_to(zl1, full), pltpu.roll(pres, 1, 2))
    slope_z = wu * above_z + wm * pres + wl * below_z
    v2 = v_ref[2] - time_step * idn * slope_z
    vz = vz_ref[...]
    iz = iz_ref[...]
    v2_lo = pick(vz, -1, 0) - time_step * pick(iz, -1, 0) * (wu_lo * p_first + wm_lo * zl1 + wl_lo * zl2)
    v2_hi = pick(vz, -1, 1) - time_step * pick(iz, -1, 1) * (wu_hi * zh2 + wm_hi * zh1 + wl_hi * p_last)

    vo_ref[0] = v0
    vo_ref[1] = v1
    vo_ref[2] = v2
    vxo_ref[0:1] = v0_lo
    vxo_ref[1:2] = v0_hi
    vyo_ref[...] = pair(v1_lo, v1_hi, vyo_ref.shape, 1)
    vzo_ref[...] = pair(v2_lo, v2_hi, vzo_ref.shape, 2)

    up_x = jnp.concatenate([v0[1:], v0_hi], axis=0)
    down_x = jnp.concatenate([v0_lo, v0[:-1]], axis=0)
    up_y = jnp.where(yi == Y - 1, jnp.broadcast_to(v1_hi, full), pltpu.roll(v1, Y - 1, 1))
    down_y = jnp.where(yi == 0, jnp.broadcast_to(v1_lo, full), pltpu.roll(v1, 1, 1))
    up_z = jnp.where(zi == Z - 1, jnp.broadcast_to(v2_hi, full), pltpu.roll(v2, Z - 1, 2))
    down_z = jnp.where(zi == 0, jnp.broadcast_to(v2_lo, full), pltpu.roll(v2, 1, 2))
    spread = (
        0.5 * (up_x - down_x)
        + 0.5 * (up_y - down_y)
        + (wu * up_z + wm * v2 + wl * down_z)
    )
    new_p = pres - time_step * bulk_ref[...] * spread
    new_p = jnp.where(zi == 0, new_p + jnp.broadcast_to(src_ref[instant], full), new_p)
    po_ref[...] = new_p

    sxu_ref[...] = new_p[X - 2 :]
    sxd_ref[...] = new_p[0:2]
    syu_ref[...] = new_p[:, Y - rows :]
    syd_ref[...] = new_p[:, 0:rows]
    zshape = szu_ref.shape
    szu_ref[...] = pair(pick(new_p, -1, Z - 2), pick(new_p, -1, Z - 1), zshape, 2)
    szd_ref[...] = pair(pick(new_p, -1, 0), pick(new_p, -1, 1), zshape, 2)


def run_step(instant, scal, wint, pres, vel, idn, bulk, src, sf, halos, tracked, media_halo):
    X, Y, Z = pres.shape
    rows = halos[2].shape[1]
    f32 = jnp.float32
    shapes = (
        jax.ShapeDtypeStruct((X, Y, Z), f32),
        jax.ShapeDtypeStruct((3, X, Y, Z), f32),
        jax.ShapeDtypeStruct((X, Y, 1), f32),
        jax.ShapeDtypeStruct((2, Y, Z), f32),
        jax.ShapeDtypeStruct((X, 2, Z), f32),
        jax.ShapeDtypeStruct((X, Y, 2), f32),
        jax.ShapeDtypeStruct((2, Y, Z), f32),
        jax.ShapeDtypeStruct((2, Y, Z), f32),
        jax.ShapeDtypeStruct((X, rows, Z), f32),
        jax.ShapeDtypeStruct((X, rows, Z), f32),
        jax.ShapeDtypeStruct((X, Y, 2), f32),
        jax.ShapeDtypeStruct((X, Y, 2), f32),
    )
    vmem = pl.BlockSpec(memory_space=pltpu.VMEM)
    in_specs = [pl.BlockSpec(memory_space=pltpu.SMEM)] + [vmem] * 19
    cells = X * Y * Z
    return pl.pallas_call(
        functools.partial(step_kernel, instant),
        out_shape=shapes,
        in_specs=in_specs,
        out_specs=[vmem] * len(shapes),
        cost_estimate=pl.CostEstimate(
            flops=80 * cells, transcendentals=0, bytes_accessed=4 * 4 * 12 * cells // 4
        ),
    )(scal, wint, pres, vel, idn, bulk, src, sf, *halos, *tracked, *media_halo)


def seafloor_sums(seafloor, node_weight, node_patch, patch_slot):
    sea_values = node_weight[0, 0] * seafloor.reshape(-1)
    slots = patch_slot[node_patch[0, 0]]
    partial_slip = jnp.zeros((patch_slot.shape[0],), jnp.float32).at[slots].add(sea_values)
    rows_x, rows_y = lax.axis_size("gx"), lax.axis_size("gy")
    by_column = jnp.moveaxis(partial_slip.reshape(rows_x, rows_y, -1), 1, 0)
    column_sums = summed_on_arrival(by_column.reshape(-1), "gy", 0)
    return summed_on_arrival(column_sums, "gx", 0)


def local(
    pressure,
    velocity,
    inv_density,
    bulk,
    node_weight,
    node_patch,
    patch_slot,
    gauge_x,
    gauge_y,
    gauge_misfit,
):
    X, Y, Z = pressure.shape
    rows = 8
    tiles_z = lax.axis_size("gz")
    depth_index = lax.axis_index("gz")
    first_crust = tiles_z // 2 * Z
    levels = depth_index * Z + jnp.arange(Z, dtype=jnp.int32)
    wint = jnp.stack(depth_weights(levels, first_crust)).reshape(3, 1, 1, Z)
    entry = lax.broadcasted_iota(jnp.int32, (ITERS, 16), 1)
    step_at = lax.broadcasted_iota(jnp.int32, (ITERS, 16), 0)
    edge_level = depth_index * Z + jnp.where(entry < 3, -1, Z)
    e_up, e_mid, e_low = depth_weights(edge_level, first_crust)
    kind = entry % 3
    edge_value = jnp.where(kind == 0, e_up, jnp.where(kind == 1, e_mid, e_low))
    ocean = depth_index == first_crust // Z - 1
    crust = depth_index == first_crust // Z
    before = step_at < ITERS - 1
    after = step_at < 0
    flag_value = jnp.where(
        entry == 6, before & ocean,
        jnp.where(entry == 7, before & crust,
                  jnp.where(entry == 8, after & ocean, after & crust)),
    ).astype(jnp.float32)
    scal_all = jnp.where(entry < 6, edge_value, jnp.where(entry < 10, flag_value, 0.0))
    scal_all = scal_all.astype(jnp.float32).reshape(ITERS * 16)
    top_flag = (depth_index == 0).astype(jnp.float32)
    sources = source_planes(
        gauge_x,
        gauge_y,
        gauge_misfit,
        lax.axis_index("gx") * X,
        lax.axis_index("gy") * Y,
        X,
        Y,
    )
    src_all = (time_step * sources * top_flag)[..., None]

    v0, v1, v2 = velocity[0], velocity[1], velocity[2]
    x_up = jnp.concatenate([pressure[X - 2 :], v0[X - 1 :], inv_density[X - 1 :]], axis=0)
    x_dn = jnp.concatenate([pressure[:2], v0[:1], inv_density[:1]], axis=0)
    y_up = jnp.concatenate(
        [pressure[:, Y - rows :], v1[:, Y - 1 :], inv_density[:, Y - 1 :]], axis=1
    )
    y_dn = jnp.concatenate([pressure[:, :rows], v1[:, :1], inv_density[:, :1]], axis=1)
    z_up = jnp.concatenate(
        [pressure[:, :, Z - 2 :], v2[:, :, Z - 1 :], inv_density[:, :, Z - 1 :]], axis=2
    )
    z_dn = jnp.concatenate([pressure[:, :, :2], v2[:, :, :1], inv_density[:, :, :1]], axis=2)
    rx_lo = shifted_up(x_up, "gx")
    rx_hi = shifted_down(x_dn, "gx")
    ry_lo = shifted_up(y_up, "gy")
    ry_hi = shifted_down(y_dn, "gy")
    rz_lo = shifted_up(z_up, "gz")
    rz_hi = shifted_down(z_dn, "gz")
    halos = (
        rx_lo[:2],
        rx_hi[:2],
        ry_lo[:, :rows],
        ry_hi[:, :rows],
        rz_lo[:, :, :2],
        rz_hi[:, :, :2],
    )
    tracked = (
        jnp.concatenate([rx_lo[2:3], rx_hi[2:3]], axis=0),
        jnp.concatenate([ry_lo[:, rows : rows + 1], ry_hi[:, rows : rows + 1]], axis=1),
        jnp.concatenate([rz_lo[:, :, 2:3], rz_hi[:, :, 2:3]], axis=2),
    )
    media_halo = (
        jnp.concatenate([rx_lo[3:4], rx_hi[3:4]], axis=0),
        jnp.concatenate([ry_lo[:, rows + 1 : rows + 2], ry_hi[:, rows + 1 : rows + 2]], axis=1),
        jnp.concatenate([rz_lo[:, :, 3:4], rz_hi[:, :, 3:4]], axis=2),
    )
    sf = jnp.zeros((X, Y, 1), jnp.float32)
    pres, vel = pressure, velocity
    for instant in range(ITERS):
        if instant > 0:
            halos = (
                shifted_up(sends[0], "gx"),
                shifted_down(sends[1], "gx"),
                shifted_up(sends[2], "gy"),
                shifted_down(sends[3], "gy"),
                shifted_up(sends[4], "gz"),
                shifted_down(sends[5], "gz"),
            )
        if instant == ITERS - 1:
            ocean = (depth_index == first_crust // Z - 1).astype(jnp.float32)
            crust = (depth_index == first_crust // Z).astype(jnp.float32)
            sf_last = sf + 0.5 * (
                ocean * (sends[4][:, :, 1:2] + halos[5][:, :, 0:1])
                + crust * (halos[4][:, :, 1:2] + sends[5][:, :, 0:1])
            )
            owner_sums = seafloor_sums(sf_last[:, :, 0], node_weight, node_patch, patch_slot)
        outs = run_step(
            instant, scal_all, wint, pres, vel, inv_density, bulk, src_all, sf, halos, tracked,
            media_halo,
        )
        pres, vel, sf = outs[0], outs[1], outs[2]
        tracked = outs[3:6]
        sends = outs[6:12]
    ocean_plane = first_crust // Z - 1
    crust_plane = first_crust // Z
    spread_out = lax.ppermute(
        owner_sums, "gz", [(ocean_plane, ocean_plane - 1), (crust_plane, crust_plane + 1)]
    )
    inner = (depth_index == ocean_plane) | (depth_index == crust_plane)
    owner_sums = jnp.where(inner, owner_sums, spread_out)
    piece = owner_sums.shape[0] // tiles_z
    slip_grad = lax.dynamic_slice_in_dim(owner_sums, depth_index * piece, piece)
    return (pres, vel, slip_grad)


def solution(mesh):
    placed = (
        P("gx", "gy", "gz"),
        P(None, "gx", "gy", "gz"),
        P("gx", "gy", "gz"),
        P("gx", "gy", "gz"),
        P("gx", "gy", None),
        P("gx", "gy", None),
        P(),
        P(),
        P(),
        P(),
    )
    return jax.shard_map(
        local,
        mesh=mesh,
        in_specs=placed,
        out_specs=(P("gx", "gy", "gz"), P(None, "gx", "gy", "gz"), P(("gx", "gy", "gz"))),
        check_vma=False,
    )
```

```python
import functools

import jax
import jax.numpy as jnp
from jax import lax
from jax.experimental import pallas as pl
from jax.experimental.pallas import tpu as pltpu
from jax.sharding import PartitionSpec as P

ITERS = 4


time_step = 0.5


def shifted_up(x, axis):
    count = lax.axis_size(axis)
    return lax.ppermute(x, axis, [(i, i + 1) for i in range(count - 1)])


def shifted_down(x, axis):
    count = lax.axis_size(axis)
    return lax.ppermute(x, axis, [(i + 1, i) for i in range(count - 1)])


def in_blocks(x, dim, size):
    before, after = (x.shape[:dim], x.shape[dim + 1 :])
    return jnp.moveaxis(x.reshape(*before, size, -1, *after), dim, 0)


def summed_on_arrival(x, axis, dim):
    size = lax.axis_size(axis)
    parts = lax.all_to_all(in_blocks(x, dim, size), axis, 0, 0, tiled=True)
    return jnp.sum(parts, axis=0)


def depth_weights(levels, first_crust):
    ocean_last = levels == first_crust - 1
    crust_first = levels == first_crust
    weight_above = jnp.where(ocean_last, 0.5, jnp.where(crust_first, 1.0, 0.5)).astype(jnp.float32)
    weight_here = jnp.where(ocean_last, 0.5, jnp.where(crust_first, -1.5, 0.0)).astype(jnp.float32)
    weight_below = jnp.where(ocean_last, -1.0, jnp.where(crust_first, 0.5, -0.5)).astype(
        jnp.float32
    )
    return (weight_above, weight_here, weight_below)


def source_planes(gauge_x, gauge_y, gauge_misfit, start_x, start_y, span_x, span_y):
    local_x = gauge_x - start_x
    local_y = gauge_y - start_y
    inside = (local_x >= 0) & (local_x < span_x) & (local_y >= 0) & (local_y < span_y)
    gauge_cell = jnp.where(inside, local_x * span_y + local_y, -1)
    gauge_table = (
        gauge_cell[:, None] == jnp.arange(span_x * span_y, dtype=jnp.int32)[None, :]
    ).astype(jnp.float32)
    return jnp.dot(gauge_misfit, gauge_table, precision=lax.Precision.HIGHEST).reshape(
        gauge_misfit.shape[0], span_x, span_y
    )


def pick(a, axis, index):
    where = lax.broadcasted_iota(jnp.int32, a.shape, a.ndim + axis if axis < 0 else axis) == index
    return jnp.sum(jnp.where(where, a, 0.0), axis=axis, keepdims=True)


def pair(lo, hi, shape, axis):
    where = lax.broadcasted_iota(jnp.int32, shape, axis) == 0
    return jnp.where(where, jnp.broadcast_to(lo, shape), jnp.broadcast_to(hi, shape))


def step_kernel(instant, first, *refs):
    if first:
        (scal_ref, wint_ref, p_ref, v_ref, idn_ref, bulk_ref, src_ref,
         xl_ref, xh_ref, yl_ref, yh_ref, zl_ref, zh_ref) = refs[:13]
        outs = refs[13:]
    else:
        (scal_ref, wint_ref, p_ref, v_ref, idn_ref, bulk_ref, src_ref, sf_ref,
         xl_ref, xh_ref, yl_ref, yh_ref, zl_ref, zh_ref,
         vx_ref, vy_ref, vz_ref, ix_ref, iy_ref, iz_ref) = refs[:20]
        outs = refs[20:]
    (po_ref, vo_ref, sfo_ref, vxo_ref, vyo_ref, vzo_ref,
     sxu_ref, sxd_ref, syu_ref, syd_ref, szu_ref, szd_ref) = outs[:12]
    X, Y, Z = p_ref.shape
    rows = syu_ref.shape[1]
    base = instant * 16
    full = (X, Y, Z)
    yi = lax.broadcasted_iota(jnp.int32, full, 1)
    zi = lax.broadcasted_iota(jnp.int32, full, 2)
    wu = wint_ref[0]
    wm = wint_ref[1]
    wl = wint_ref[2]
    wu_lo = scal_ref[base + 0]
    wm_lo = scal_ref[base + 1]
    wl_lo = scal_ref[base + 2]
    wu_hi = scal_ref[base + 3]
    wm_hi = scal_ref[base + 4]
    wl_hi = scal_ref[base + 5]
    f_ocean = scal_ref[base + 6]
    f_crust = scal_ref[base + 7]

    xl = xl_ref[...]
    xh = xh_ref[...]
    yl = yl_ref[...]
    yh = yh_ref[...]
    zl = zl_ref[...]
    zh = zh_ref[...]
    pxl2, pxl1 = xl[0:1], xl[1:2]
    pxh1, pxh2 = xh[0:1], xh[1:2]
    yl2, yl1 = pick(yl, 1, rows - 2), pick(yl, 1, rows - 1)
    yh1, yh2 = pick(yh, 1, 0), pick(yh, 1, 1)
    zl2, zl1 = pick(zl, -1, 0), pick(zl, -1, 1)
    zh1, zh2 = pick(zh, -1, 0), pick(zh, -1, 1)
    if first:
        vx_lo, vx_hi, ix_lo, ix_hi = xl[2:3], xh[2:3], xl[3:4], xh[3:4]
        vy_lo, vy_hi = pick(yl, 1, rows), pick(yh, 1, rows)
        iy_lo, iy_hi = pick(yl, 1, rows + 1), pick(yh, 1, rows + 1)
        vz_lo, vz_hi, iz_lo, iz_hi = pick(zl, -1, 2), pick(zh, -1, 2), pick(zl, -1, 3), pick(zh, -1, 3)
        ixo_ref, iyo_ref, izo_ref = outs[12:15]
        ixo_ref[0:1] = ix_lo
        ixo_ref[1:2] = ix_hi
        iyo_ref[...] = pair(iy_lo, iy_hi, iyo_ref.shape, 1)
        izo_ref[...] = pair(iz_lo, iz_hi, izo_ref.shape, 2)
    else:
        vx = vx_ref[...]
        ix = ix_ref[...]
        vy = vy_ref[...]
        iy = iy_ref[...]
        vz = vz_ref[...]
        iz = iz_ref[...]
        vx_lo, vx_hi, ix_lo, ix_hi = vx[0:1], vx[1:2], ix[0:1], ix[1:2]
        vy_lo, vy_hi = pick(vy, 1, 0), pick(vy, 1, 1)
        iy_lo, iy_hi = pick(iy, 1, 0), pick(iy, 1, 1)
        vz_lo, vz_hi, iz_lo, iz_hi = pick(vz, -1, 0), pick(vz, -1, 1), pick(iz, -1, 0), pick(iz, -1, 1)

    pres = p_ref[...]
    idn = idn_ref[...]

    p_first = pick(pres, -1, 0)
    p_last = pick(pres, -1, Z - 1)
    sea = 0.5 * (f_ocean * (p_last + zh1) + f_crust * (zl1 + p_first))
    sfo_ref[...] = sea if first else sf_ref[...] + sea

    above_x = jnp.concatenate([pres[1:], pxh1], axis=0)
    below_x = jnp.concatenate([pxl1, pres[:-1]], axis=0)
    slope_x = 0.5 * (above_x - below_x)
    v0 = v_ref[0] - time_step * idn * slope_x
    v0_lo = vx_lo - time_step * ix_lo * (0.5 * (pres[0:1] - pxl2))
    v0_hi = vx_hi - time_step * ix_hi * (0.5 * (pxh2 - pres[X - 1 : X]))

    p_y0 = pick(pres, 1, 0)
    p_yl = pick(pres, 1, Y - 1)
    above_y = jnp.where(yi == Y - 1, jnp.broadcast_to(yh1, full), pltpu.roll(pres, Y - 1, 1))
    below_y = jnp.where(yi == 0, jnp.broadcast_to(yl1, full), pltpu.roll(pres, 1, 1))
    slope_y = 0.5 * (above_y - below_y)
    v1 = v_ref[1] - time_step * idn * slope_y
    v1_lo = vy_lo - time_step * iy_lo * (0.5 * (p_y0 - yl2))
    v1_hi = vy_hi - time_step * iy_hi * (0.5 * (yh2 - p_yl))

    above_z = jnp.where(zi == Z - 1, jnp.broadcast_to(zh1, full), pltpu.roll(pres, Z - 1, 2))
    below_z = jnp.where(zi == 0, jnp.broadcast_to(zl1, full), pltpu.roll(pres, 1, 2))
    slope_z = wu * above_z + wm * pres + wl * below_z
    v2 = v_ref[2] - time_step * idn * slope_z
    v2_lo = vz_lo - time_step * iz_lo * (wu_lo * p_first + wm_lo * zl1 + wl_lo * zl2)
    v2_hi = vz_hi - time_step * iz_hi * (wu_hi * zh2 + wm_hi * zh1 + wl_hi * p_last)

    vo_ref[0] = v0
    vo_ref[1] = v1
    vo_ref[2] = v2
    vxo_ref[0:1] = v0_lo
    vxo_ref[1:2] = v0_hi
    vyo_ref[...] = pair(v1_lo, v1_hi, vyo_ref.shape, 1)
    vzo_ref[...] = pair(v2_lo, v2_hi, vzo_ref.shape, 2)

    up_x = jnp.concatenate([v0[1:], v0_hi], axis=0)
    down_x = jnp.concatenate([v0_lo, v0[:-1]], axis=0)
    up_y = jnp.where(yi == Y - 1, jnp.broadcast_to(v1_hi, full), pltpu.roll(v1, Y - 1, 1))
    down_y = jnp.where(yi == 0, jnp.broadcast_to(v1_lo, full), pltpu.roll(v1, 1, 1))
    up_z = jnp.where(zi == Z - 1, jnp.broadcast_to(v2_hi, full), pltpu.roll(v2, Z - 1, 2))
    down_z = jnp.where(zi == 0, jnp.broadcast_to(v2_lo, full), pltpu.roll(v2, 1, 2))
    spread = (
        0.5 * (up_x - down_x)
        + 0.5 * (up_y - down_y)
        + (wu * up_z + wm * v2 + wl * down_z)
    )
    new_p = pres - time_step * bulk_ref[...] * spread
    new_p = jnp.where(zi == 0, new_p + jnp.broadcast_to(src_ref[instant], full), new_p)
    po_ref[...] = new_p

    sxu_ref[...] = new_p[X - 2 :]
    sxd_ref[...] = new_p[0:2]
    syu_ref[...] = new_p[:, Y - rows :]
    syd_ref[...] = new_p[:, 0:rows]
    zshape = szu_ref.shape
    szu_ref[...] = pair(pick(new_p, -1, Z - 2), pick(new_p, -1, Z - 1), zshape, 2)
    szd_ref[...] = pair(pick(new_p, -1, 0), pick(new_p, -1, 1), zshape, 2)


def run_step(instant, operands, rows):
    pres = operands[2]
    X, Y, Z = pres.shape
    first = instant == 0
    f32 = jnp.float32
    shapes = [
        jax.ShapeDtypeStruct((X, Y, Z), f32),
        jax.ShapeDtypeStruct((3, X, Y, Z), f32),
        jax.ShapeDtypeStruct((X, Y, 1), f32),
        jax.ShapeDtypeStruct((2, Y, Z), f32),
        jax.ShapeDtypeStruct((X, 2, Z), f32),
        jax.ShapeDtypeStruct((X, Y, 2), f32),
        jax.ShapeDtypeStruct((2, Y, Z), f32),
        jax.ShapeDtypeStruct((2, Y, Z), f32),
        jax.ShapeDtypeStruct((X, rows, Z), f32),
        jax.ShapeDtypeStruct((X, rows, Z), f32),
        jax.ShapeDtypeStruct((X, Y, 2), f32),
        jax.ShapeDtypeStruct((X, Y, 2), f32),
    ]
    if first:
        shapes += shapes[3:6]
    vmem = pl.BlockSpec(memory_space=pltpu.VMEM)
    in_specs = [pl.BlockSpec(memory_space=pltpu.SMEM)] + [vmem] * (len(operands) - 1)
    cells = X * Y * Z
    return pl.pallas_call(
        functools.partial(step_kernel, instant, first),
        out_shape=tuple(shapes),
        in_specs=in_specs,
        out_specs=[vmem] * len(shapes),
        cost_estimate=pl.CostEstimate(
            flops=80 * cells, transcendentals=0, bytes_accessed=4 * 4 * 12 * cells // 4
        ),
    )(*operands)


def seafloor_sums(seafloor, node_weight, node_patch, patch_slot):
    sea_values = node_weight[0, 0] * seafloor.reshape(-1)
    slots = patch_slot[node_patch[0, 0]]
    partial_slip = jnp.zeros((patch_slot.shape[0],), jnp.float32).at[slots].add(sea_values)
    return summed_on_arrival(partial_slip, ("gx", "gy"), 0)


def local(
    pressure,
    velocity,
    inv_density,
    bulk,
    node_weight,
    node_patch,
    patch_slot,
    gauge_x,
    gauge_y,
    gauge_misfit,
):
    X, Y, Z = pressure.shape
    rows = 8
    tiles_z = lax.axis_size("gz")
    depth_index = lax.axis_index("gz")
    first_crust = tiles_z // 2 * Z
    levels = depth_index * Z + jnp.arange(Z, dtype=jnp.int32)
    wint = jnp.stack(depth_weights(levels, first_crust)).reshape(3, 1, 1, Z)
    entry = lax.broadcasted_iota(jnp.int32, (ITERS, 16), 1)
    step_at = lax.broadcasted_iota(jnp.int32, (ITERS, 16), 0)
    edge_level = depth_index * Z + jnp.where(entry < 3, -1, Z)
    e_up, e_mid, e_low = depth_weights(edge_level, first_crust)
    kind = entry % 3
    edge_value = jnp.where(kind == 0, e_up, jnp.where(kind == 1, e_mid, e_low))
    ocean = depth_index == first_crust // Z - 1
    crust = depth_index == first_crust // Z
    before = step_at < ITERS - 1
    after = step_at < 0
    flag_value = jnp.where(
        entry == 6, before & ocean,
        jnp.where(entry == 7, before & crust,
                  jnp.where(entry == 8, after & ocean, after & crust)),
    ).astype(jnp.float32)
    scal_all = jnp.where(entry < 6, edge_value, jnp.where(entry < 10, flag_value, 0.0))
    scal_all = scal_all.astype(jnp.float32).reshape(ITERS * 16)
    top_flag = (depth_index == 0).astype(jnp.float32)
    sources = source_planes(
        gauge_x,
        gauge_y,
        gauge_misfit,
        lax.axis_index("gx") * X,
        lax.axis_index("gy") * Y,
        X,
        Y,
    )
    src_all = (time_step * sources * top_flag)[..., None]

    v0, v1, v2 = velocity[0], velocity[1], velocity[2]
    x_up = jnp.concatenate([pressure[X - 2 :], v0[X - 1 :], inv_density[X - 1 :]], axis=0)
    x_dn = jnp.concatenate([pressure[:2], v0[:1], inv_density[:1]], axis=0)
    y_up = jnp.concatenate(
        [pressure[:, Y - rows :], v1[:, Y - 1 :], inv_density[:, Y - 1 :]], axis=1
    )
    y_dn = jnp.concatenate([pressure[:, :rows], v1[:, :1], inv_density[:, :1]], axis=1)
    z_up = jnp.concatenate(
        [pressure[:, :, Z - 2 :], v2[:, :, Z - 1 :], inv_density[:, :, Z - 1 :]], axis=2
    )
    z_dn = jnp.concatenate([pressure[:, :, :2], v2[:, :, :1], inv_density[:, :, :1]], axis=2)
    halos = (
        shifted_up(x_up, "gx"),
        shifted_down(x_dn, "gx"),
        shifted_up(y_up, "gy"),
        shifted_down(y_dn, "gy"),
        shifted_up(z_up, "gz"),
        shifted_down(z_dn, "gz"),
    )
    common = (scal_all, wint)
    pres, vel = pressure, velocity
    for instant in range(ITERS):
        if instant > 0:
            halos = (
                shifted_up(sends[0], "gx"),
                shifted_down(sends[1], "gx"),
                shifted_up(sends[2], "gy"),
                shifted_down(sends[3], "gy"),
                shifted_up(sends[4], "gz"),
                shifted_down(sends[5], "gz"),
            )
        if instant == ITERS - 1:
            ocean = (depth_index == first_crust // Z - 1).astype(jnp.float32)
            crust = (depth_index == first_crust // Z).astype(jnp.float32)
            sf_last = sf + 0.5 * (
                ocean * (sends[4][:, :, 1:2] + halos[5][:, :, 0:1])
                + crust * (halos[4][:, :, 1:2] + sends[5][:, :, 0:1])
            )
            owner_sums = seafloor_sums(sf_last[:, :, 0], node_weight, node_patch, patch_slot)
        if instant == 0:
            operands = common + (pres, vel, inv_density, bulk, src_all) + halos
        else:
            operands = common + (pres, vel, inv_density, bulk, src_all, sf) + halos + tracked + media_halo
        outs = run_step(instant, operands, rows)
        pres, vel, sf = outs[0], outs[1], outs[2]
        tracked = outs[3:6]
        sends = outs[6:12]
        if instant == 0:
            media_halo = outs[12:15]
    ocean_plane = first_crust // Z - 1
    crust_plane = first_crust // Z
    spread_out = lax.ppermute(
        owner_sums, "gz", [(ocean_plane, ocean_plane - 1), (crust_plane, crust_plane + 1)]
    )
    inner = (depth_index == ocean_plane) | (depth_index == crust_plane)
    owner_sums = jnp.where(inner, owner_sums, spread_out)
    piece = owner_sums.shape[0] // tiles_z
    slip_grad = lax.dynamic_slice_in_dim(owner_sums, depth_index * piece, piece)
    return (pres, vel, slip_grad)


def solution(mesh):
    placed = (
        P("gx", "gy", "gz"),
        P(None, "gx", "gy", "gz"),
        P("gx", "gy", "gz"),
        P("gx", "gy", "gz"),
        P("gx", "gy", None),
        P("gx", "gy", None),
        P(),
        P(),
        P(),
        P(),
    )
    return jax.shard_map(
        local,
        mesh=mesh,
        in_specs=placed,
        out_specs=(P("gx", "gy", "gz"), P(None, "gx", "gy", "gz"), P(("gx", "gy", "gz"))),
        check_vma=False,
    )
```

```python
import functools

import jax
import jax.numpy as jnp
from jax import lax
from jax.experimental import pallas as pl
from jax.experimental.pallas import tpu as pltpu
from jax.sharding import PartitionSpec as P

ITERS = 4


time_step = 0.5


def shifted_up(x, axis):
    count = lax.axis_size(axis)
    return lax.ppermute(x, axis, [(i, i + 1) for i in range(count - 1)])


def shifted_down(x, axis):
    count = lax.axis_size(axis)
    return lax.ppermute(x, axis, [(i + 1, i) for i in range(count - 1)])


def in_blocks(x, dim, size):
    before, after = (x.shape[:dim], x.shape[dim + 1 :])
    return jnp.moveaxis(x.reshape(*before, size, -1, *after), dim, 0)


def summed_on_arrival(x, axis, dim):
    size = lax.axis_size(axis)
    parts = lax.all_to_all(in_blocks(x, dim, size), axis, 0, 0, tiled=True)
    return jnp.sum(parts, axis=0)


def depth_weights(levels, first_crust):
    ocean_last = levels == first_crust - 1
    crust_first = levels == first_crust
    weight_above = jnp.where(ocean_last, 0.5, jnp.where(crust_first, 1.0, 0.5)).astype(jnp.float32)
    weight_here = jnp.where(ocean_last, 0.5, jnp.where(crust_first, -1.5, 0.0)).astype(jnp.float32)
    weight_below = jnp.where(ocean_last, -1.0, jnp.where(crust_first, 0.5, -0.5)).astype(
        jnp.float32
    )
    return (weight_above, weight_here, weight_below)


def source_planes(gauge_x, gauge_y, gauge_misfit, start_x, start_y, span_x, span_y):
    local_x = gauge_x - start_x
    local_y = gauge_y - start_y
    inside = (local_x >= 0) & (local_x < span_x) & (local_y >= 0) & (local_y < span_y)
    gauge_cell = jnp.where(inside, local_x * span_y + local_y, -1)
    gauge_table = (
        gauge_cell[:, None] == jnp.arange(span_x * span_y, dtype=jnp.int32)[None, :]
    ).astype(jnp.float32)
    return jnp.dot(gauge_misfit, gauge_table, precision=lax.Precision.HIGHEST).reshape(
        gauge_misfit.shape[0], span_x, span_y
    )


def pick(a, axis, index):
    return lax.slice_in_dim(a, index, index + 1, axis=axis % a.ndim)


def pair(lo, hi, shape, axis):
    where = lax.broadcasted_iota(jnp.int32, shape, axis) == 0
    return jnp.where(where, jnp.broadcast_to(lo, shape), jnp.broadcast_to(hi, shape))


def step_kernel(instant, first, *refs):
    if first:
        (scal_ref, wint_ref, p_ref, v_ref, idn_ref, bulk_ref, src_ref,
         xl_ref, xh_ref, yl_ref, yh_ref, zl_ref, zh_ref) = refs[:13]
        outs = refs[13:]
    else:
        (scal_ref, wint_ref, p_ref, v_ref, idn_ref, bulk_ref, src_ref, sf_ref,
         xl_ref, xh_ref, yl_ref, yh_ref, zl_ref, zh_ref,
         vx_ref, vy_ref, vz_ref, ix_ref, iy_ref, iz_ref) = refs[:20]
        outs = refs[20:]
    (po_ref, vo_ref, sfo_ref, vxo_ref, vyo_ref, vzo_ref,
     sxu_ref, sxd_ref, syu_ref, syd_ref, szu_ref, szd_ref) = outs[:12]
    X, Y, Z = p_ref.shape
    rows = syu_ref.shape[1]
    base = instant * 16
    full = (X, Y, Z)
    yi = lax.broadcasted_iota(jnp.int32, full, 1)
    zi = lax.broadcasted_iota(jnp.int32, full, 2)
    wu = wint_ref[0]
    wm = wint_ref[1]
    wl = wint_ref[2]
    wu_lo = scal_ref[base + 0]
    wm_lo = scal_ref[base + 1]
    wl_lo = scal_ref[base + 2]
    wu_hi = scal_ref[base + 3]
    wm_hi = scal_ref[base + 4]
    wl_hi = scal_ref[base + 5]
    f_ocean = scal_ref[base + 6]
    f_crust = scal_ref[base + 7]

    xl = xl_ref[...]
    xh = xh_ref[...]
    yl = yl_ref[...]
    yh = yh_ref[...]
    zl = zl_ref[...]
    zh = zh_ref[...]
    pxl2, pxl1 = xl[0:1], xl[1:2]
    pxh1, pxh2 = xh[0:1], xh[1:2]
    yl2, yl1 = pick(yl, 1, rows - 2), pick(yl, 1, rows - 1)
    yh1, yh2 = pick(yh, 1, 0), pick(yh, 1, 1)
    zl2, zl1 = pick(zl, -1, 0), pick(zl, -1, 1)
    zh1, zh2 = pick(zh, -1, 0), pick(zh, -1, 1)
    if first:
        vx_lo, vx_hi, ix_lo, ix_hi = xl[2:3], xh[2:3], xl[3:4], xh[3:4]
        vy_lo, vy_hi = pick(yl, 1, rows), pick(yh, 1, rows)
        iy_lo, iy_hi = pick(yl, 1, rows + 1), pick(yh, 1, rows + 1)
        vz_lo, vz_hi, iz_lo, iz_hi = pick(zl, -1, 2), pick(zh, -1, 2), pick(zl, -1, 3), pick(zh, -1, 3)
        ixo_ref, iyo_ref, izo_ref = outs[12:15]
        ixo_ref[0:1] = ix_lo
        ixo_ref[1:2] = ix_hi
        iyo_ref[...] = pair(iy_lo, iy_hi, iyo_ref.shape, 1)
        izo_ref[...] = pair(iz_lo, iz_hi, izo_ref.shape, 2)
    else:
        vx = vx_ref[...]
        ix = ix_ref[...]
        vy = vy_ref[...]
        iy = iy_ref[...]
        vz = vz_ref[...]
        iz = iz_ref[...]
        vx_lo, vx_hi, ix_lo, ix_hi = vx[0:1], vx[1:2], ix[0:1], ix[1:2]
        vy_lo, vy_hi = pick(vy, 1, 0), pick(vy, 1, 1)
        iy_lo, iy_hi = pick(iy, 1, 0), pick(iy, 1, 1)
        vz_lo, vz_hi, iz_lo, iz_hi = pick(vz, -1, 0), pick(vz, -1, 1), pick(iz, -1, 0), pick(iz, -1, 1)

    pres = p_ref[...]
    idn = idn_ref[...]

    p_first = pick(pres, -1, 0)
    p_last = pick(pres, -1, Z - 1)
    sea = 0.5 * (f_ocean * (p_last + zh1) + f_crust * (zl1 + p_first))
    sfo_ref[...] = sea if first else sf_ref[...] + sea

    above_x = jnp.concatenate([pres[1:], pxh1], axis=0)
    below_x = jnp.concatenate([pxl1, pres[:-1]], axis=0)
    slope_x = 0.5 * (above_x - below_x)
    v0 = v_ref[0] - time_step * idn * slope_x
    v0_lo = vx_lo - time_step * ix_lo * (0.5 * (pres[0:1] - pxl2))
    v0_hi = vx_hi - time_step * ix_hi * (0.5 * (pxh2 - pres[X - 1 : X]))

    p_y0 = pick(pres, 1, 0)
    p_yl = pick(pres, 1, Y - 1)
    above_y = jnp.where(yi == Y - 1, jnp.broadcast_to(yh1, full), pltpu.roll(pres, Y - 1, 1))
    below_y = jnp.where(yi == 0, jnp.broadcast_to(yl1, full), pltpu.roll(pres, 1, 1))
    slope_y = 0.5 * (above_y - below_y)
    v1 = v_ref[1] - time_step * idn * slope_y
    v1_lo = vy_lo - time_step * iy_lo * (0.5 * (p_y0 - yl2))
    v1_hi = vy_hi - time_step * iy_hi * (0.5 * (yh2 - p_yl))

    above_z = jnp.where(zi == Z - 1, jnp.broadcast_to(zh1, full), pltpu.roll(pres, Z - 1, 2))
    below_z = jnp.where(zi == 0, jnp.broadcast_to(zl1, full), pltpu.roll(pres, 1, 2))
    slope_z = wu * above_z + wm * pres + wl * below_z
    v2 = v_ref[2] - time_step * idn * slope_z
    v2_lo = vz_lo - time_step * iz_lo * (wu_lo * p_first + wm_lo * zl1 + wl_lo * zl2)
    v2_hi = vz_hi - time_step * iz_hi * (wu_hi * zh2 + wm_hi * zh1 + wl_hi * p_last)

    vo_ref[0] = v0
    vo_ref[1] = v1
    vo_ref[2] = v2
    vxo_ref[0:1] = v0_lo
    vxo_ref[1:2] = v0_hi
    vyo_ref[...] = pair(v1_lo, v1_hi, vyo_ref.shape, 1)
    vzo_ref[...] = pair(v2_lo, v2_hi, vzo_ref.shape, 2)

    up_x = jnp.concatenate([v0[1:], v0_hi], axis=0)
    down_x = jnp.concatenate([v0_lo, v0[:-1]], axis=0)
    up_y = jnp.where(yi == Y - 1, jnp.broadcast_to(v1_hi, full), pltpu.roll(v1, Y - 1, 1))
    down_y = jnp.where(yi == 0, jnp.broadcast_to(v1_lo, full), pltpu.roll(v1, 1, 1))
    up_z = jnp.where(zi == Z - 1, jnp.broadcast_to(v2_hi, full), pltpu.roll(v2, Z - 1, 2))
    down_z = jnp.where(zi == 0, jnp.broadcast_to(v2_lo, full), pltpu.roll(v2, 1, 2))
    spread = (
        0.5 * (up_x - down_x)
        + 0.5 * (up_y - down_y)
        + (wu * up_z + wm * v2 + wl * down_z)
    )
    new_p = pres - time_step * bulk_ref[...] * spread
    new_p = jnp.where(zi == 0, new_p + jnp.broadcast_to(src_ref[instant], full), new_p)
    po_ref[...] = new_p

    sxu_ref[...] = new_p[X - 2 :]
    sxd_ref[...] = new_p[0:2]
    syu_ref[...] = new_p[:, Y - rows :]
    syd_ref[...] = new_p[:, 0:rows]
    zshape = szu_ref.shape
    szu_ref[...] = pair(pick(new_p, -1, Z - 2), pick(new_p, -1, Z - 1), zshape, 2)
    szd_ref[...] = pair(pick(new_p, -1, 0), pick(new_p, -1, 1), zshape, 2)


def run_step(instant, operands, rows):
    pres = operands[2]
    X, Y, Z = pres.shape
    first = instant == 0
    f32 = jnp.float32
    shapes = [
        jax.ShapeDtypeStruct((X, Y, Z), f32),
        jax.ShapeDtypeStruct((3, X, Y, Z), f32),
        jax.ShapeDtypeStruct((X, Y, 1), f32),
        jax.ShapeDtypeStruct((2, Y, Z), f32),
        jax.ShapeDtypeStruct((X, 2, Z), f32),
        jax.ShapeDtypeStruct((X, Y, 2), f32),
        jax.ShapeDtypeStruct((2, Y, Z), f32),
        jax.ShapeDtypeStruct((2, Y, Z), f32),
        jax.ShapeDtypeStruct((X, rows, Z), f32),
        jax.ShapeDtypeStruct((X, rows, Z), f32),
        jax.ShapeDtypeStruct((X, Y, 2), f32),
        jax.ShapeDtypeStruct((X, Y, 2), f32),
    ]
    if first:
        shapes += shapes[3:6]
    vmem = pl.BlockSpec(memory_space=pltpu.VMEM)
    in_specs = [pl.BlockSpec(memory_space=pltpu.SMEM)] + [vmem] * (len(operands) - 1)
    cells = X * Y * Z
    return pl.pallas_call(
        functools.partial(step_kernel, instant, first),
        out_shape=tuple(shapes),
        in_specs=in_specs,
        out_specs=[vmem] * len(shapes),
        cost_estimate=pl.CostEstimate(
            flops=80 * cells, transcendentals=0, bytes_accessed=4 * 4 * 12 * cells // 4
        ),
    )(*operands)


def seafloor_sums(seafloor, node_weight, node_patch, patch_slot):
    sea_values = node_weight[0, 0] * seafloor.reshape(-1)
    slots = patch_slot[node_patch[0, 0]]
    partial_slip = jnp.zeros((patch_slot.shape[0],), jnp.float32).at[slots].add(sea_values)
    return summed_on_arrival(partial_slip, ("gx", "gy"), 0)


def local(
    pressure,
    velocity,
    inv_density,
    bulk,
    node_weight,
    node_patch,
    patch_slot,
    gauge_x,
    gauge_y,
    gauge_misfit,
):
    X, Y, Z = pressure.shape
    rows = 8
    tiles_z = lax.axis_size("gz")
    depth_index = lax.axis_index("gz")
    first_crust = tiles_z // 2 * Z
    levels = depth_index * Z + jnp.arange(Z, dtype=jnp.int32)
    wint = jnp.stack(depth_weights(levels, first_crust)).reshape(3, 1, 1, Z)
    entry = lax.broadcasted_iota(jnp.int32, (ITERS, 16), 1)
    step_at = lax.broadcasted_iota(jnp.int32, (ITERS, 16), 0)
    edge_level = depth_index * Z + jnp.where(entry < 3, -1, Z)
    e_up, e_mid, e_low = depth_weights(edge_level, first_crust)
    kind = entry % 3
    edge_value = jnp.where(kind == 0, e_up, jnp.where(kind == 1, e_mid, e_low))
    ocean = depth_index == first_crust // Z - 1
    crust = depth_index == first_crust // Z
    before = step_at < ITERS - 1
    after = step_at < 0
    flag_value = jnp.where(
        entry == 6, before & ocean,
        jnp.where(entry == 7, before & crust,
                  jnp.where(entry == 8, after & ocean, after & crust)),
    ).astype(jnp.float32)
    scal_all = jnp.where(entry < 6, edge_value, jnp.where(entry < 10, flag_value, 0.0))
    scal_all = scal_all.astype(jnp.float32).reshape(ITERS * 16)
    top_flag = (depth_index == 0).astype(jnp.float32)
    sources = source_planes(
        gauge_x,
        gauge_y,
        gauge_misfit,
        lax.axis_index("gx") * X,
        lax.axis_index("gy") * Y,
        X,
        Y,
    )
    src_all = (time_step * sources * top_flag)[..., None]

    v0, v1, v2 = velocity[0], velocity[1], velocity[2]
    x_up = jnp.concatenate([pressure[X - 2 :], v0[X - 1 :], inv_density[X - 1 :]], axis=0)
    x_dn = jnp.concatenate([pressure[:2], v0[:1], inv_density[:1]], axis=0)
    y_up = jnp.concatenate(
        [pressure[:, Y - rows :], v1[:, Y - 1 :], inv_density[:, Y - 1 :]], axis=1
    )
    y_dn = jnp.concatenate([pressure[:, :rows], v1[:, :1], inv_density[:, :1]], axis=1)
    z_up = jnp.concatenate(
        [pressure[:, :, Z - 2 :], v2[:, :, Z - 1 :], inv_density[:, :, Z - 1 :]], axis=2
    )
    z_dn = jnp.concatenate([pressure[:, :, :2], v2[:, :, :1], inv_density[:, :, :1]], axis=2)
    halos = (
        shifted_up(x_up, "gx"),
        shifted_down(x_dn, "gx"),
        shifted_up(y_up, "gy"),
        shifted_down(y_dn, "gy"),
        shifted_up(z_up, "gz"),
        shifted_down(z_dn, "gz"),
    )
    common = (scal_all, wint)
    pres, vel = pressure, velocity
    for instant in range(ITERS):
        if instant > 0:
            halos = (
                shifted_up(sends[0], "gx"),
                shifted_down(sends[1], "gx"),
                shifted_up(sends[2], "gy"),
                shifted_down(sends[3], "gy"),
                shifted_up(sends[4], "gz"),
                shifted_down(sends[5], "gz"),
            )
        if instant == ITERS - 1:
            ocean = (depth_index == first_crust // Z - 1).astype(jnp.float32)
            crust = (depth_index == first_crust // Z).astype(jnp.float32)
            sf_last = sf + 0.5 * (
                ocean * (sends[4][:, :, 1:2] + halos[5][:, :, 0:1])
                + crust * (halos[4][:, :, 1:2] + sends[5][:, :, 0:1])
            )
            owner_sums = seafloor_sums(sf_last[:, :, 0], node_weight, node_patch, patch_slot)
        if instant == 0:
            operands = common + (pres, vel, inv_density, bulk, src_all) + halos
        else:
            operands = common + (pres, vel, inv_density, bulk, src_all, sf) + halos + tracked + media_halo
        outs = run_step(instant, operands, rows)
        pres, vel, sf = outs[0], outs[1], outs[2]
        tracked = outs[3:6]
        sends = outs[6:12]
        if instant == 0:
            media_halo = outs[12:15]
    ocean_plane = first_crust // Z - 1
    crust_plane = first_crust // Z
    spread_out = lax.ppermute(
        owner_sums, "gz", [(ocean_plane, ocean_plane - 1), (crust_plane, crust_plane + 1)]
    )
    inner = (depth_index == ocean_plane) | (depth_index == crust_plane)
    owner_sums = jnp.where(inner, owner_sums, spread_out)
    piece = owner_sums.shape[0] // tiles_z
    slip_grad = lax.dynamic_slice_in_dim(owner_sums, depth_index * piece, piece)
    return (pres, vel, slip_grad)


def solution(mesh):
    placed = (
        P("gx", "gy", "gz"),
        P(None, "gx", "gy", "gz"),
        P("gx", "gy", "gz"),
        P("gx", "gy", "gz"),
        P("gx", "gy", None),
        P("gx", "gy", None),
        P(),
        P(),
        P(),
        P(),
    )
    return jax.shard_map(
        local,
        mesh=mesh,
        in_specs=placed,
        out_specs=(P("gx", "gy", "gz"), P(None, "gx", "gy", "gz"), P(("gx", "gy", "gz"))),
        check_vma=False,
    )
```

```python
import functools

import jax
import jax.numpy as jnp
from jax import lax
from jax.experimental import pallas as pl
from jax.experimental.pallas import tpu as pltpu
from jax.sharding import PartitionSpec as P

ITERS = 4


time_step = 0.5


def shifted_up(x, axis):
    count = lax.axis_size(axis)
    return lax.ppermute(x, axis, [(i, i + 1) for i in range(count - 1)])


def shifted_down(x, axis):
    count = lax.axis_size(axis)
    return lax.ppermute(x, axis, [(i + 1, i) for i in range(count - 1)])


def in_blocks(x, dim, size):
    before, after = (x.shape[:dim], x.shape[dim + 1 :])
    return jnp.moveaxis(x.reshape(*before, size, -1, *after), dim, 0)


def summed_on_arrival(x, axis, dim):
    size = lax.axis_size(axis)
    parts = lax.all_to_all(in_blocks(x, dim, size), axis, 0, 0, tiled=True)
    return jnp.sum(parts, axis=0)


def depth_weights(levels, first_crust):
    ocean_last = levels == first_crust - 1
    crust_first = levels == first_crust
    weight_above = jnp.where(ocean_last, 0.5, jnp.where(crust_first, 1.0, 0.5)).astype(jnp.float32)
    weight_here = jnp.where(ocean_last, 0.5, jnp.where(crust_first, -1.5, 0.0)).astype(jnp.float32)
    weight_below = jnp.where(ocean_last, -1.0, jnp.where(crust_first, 0.5, -0.5)).astype(
        jnp.float32
    )
    return (weight_above, weight_here, weight_below)


def source_planes(gauge_x, gauge_y, gauge_misfit, start_x, start_y, span_x, span_y):
    local_x = gauge_x - start_x
    local_y = gauge_y - start_y
    inside = (local_x >= 0) & (local_x < span_x) & (local_y >= 0) & (local_y < span_y)
    gauge_cell = jnp.where(inside, local_x * span_y + local_y, -1)
    gauge_table = (
        gauge_cell[:, None] == jnp.arange(span_x * span_y, dtype=jnp.int32)[None, :]
    ).astype(jnp.float32)
    return jnp.dot(gauge_misfit, gauge_table, precision=lax.Precision.HIGHEST).reshape(
        gauge_misfit.shape[0], span_x, span_y
    )


def pick(a, axis, index):
    return lax.slice_in_dim(a, index, index + 1, axis=axis % a.ndim)


def pair(lo, hi, shape, axis):
    where = lax.broadcasted_iota(jnp.int32, shape, axis) == 0
    return jnp.where(where, jnp.broadcast_to(lo, shape), jnp.broadcast_to(hi, shape))


def step_kernel(instant, first, *refs):
    if first:
        (scal_ref, wint_ref, p_ref, v_ref, idn_ref, bulk_ref, src_ref,
         xl_ref, xh_ref, yl_ref, yh_ref, zl_ref, zh_ref) = refs[:13]
        outs = refs[13:]
    else:
        (scal_ref, wint_ref, p_ref, v_ref, idn_ref, bulk_ref, src_ref, sf_ref,
         xl_ref, xh_ref, yl_ref, yh_ref, zl_ref, zh_ref,
         vx_ref, vy_ref, vz_ref, ix_ref, iy_ref, iz_ref) = refs[:20]
        outs = refs[20:]
    (po_ref, vo_ref, sfo_ref, vxo_ref, vyo_ref, vzo_ref,
     sxu_ref, sxd_ref, syu_ref, syd_ref, szu_ref, szd_ref) = outs[:12]
    X, Y, Z = p_ref.shape
    rows = syu_ref.shape[1]
    base = instant * 16
    full = (X, Y, Z)
    yi = lax.broadcasted_iota(jnp.int32, full, 1)
    zi = lax.broadcasted_iota(jnp.int32, full, 2)
    wu = wint_ref[0]
    wm = wint_ref[1]
    wl = wint_ref[2]
    wu_lo = scal_ref[base + 0]
    wm_lo = scal_ref[base + 1]
    wl_lo = scal_ref[base + 2]
    wu_hi = scal_ref[base + 3]
    wm_hi = scal_ref[base + 4]
    wl_hi = scal_ref[base + 5]
    f_ocean = scal_ref[base + 6]
    f_crust = scal_ref[base + 7]

    xl = xl_ref[...]
    xh = xh_ref[...]
    yl = yl_ref[...]
    yh = yh_ref[...]
    zl = zl_ref[...]
    zh = zh_ref[...]
    pxl2, pxl1 = (xl[0:1], xl[1:2]) if first else (xl[-2:-1], xl[-1:])
    pxh1, pxh2 = xh[0:1], xh[1:2]
    yl2, yl1 = pick(yl, 1, rows - 2), pick(yl, 1, rows - 1)
    yh1, yh2 = pick(yh, 1, 0), pick(yh, 1, 1)
    zl2, zl1 = pick(zl, -1, 0), pick(zl, -1, 1)
    zh1, zh2 = pick(zh, -1, 0), pick(zh, -1, 1)
    if first:
        vx_lo, vx_hi, ix_lo, ix_hi = xl[2:3], xh[2:3], xl[3:4], xh[3:4]
        vy_lo, vy_hi = pick(yl, 1, rows), pick(yh, 1, rows)
        iy_lo, iy_hi = pick(yl, 1, rows + 1), pick(yh, 1, rows + 1)
        vz_lo, vz_hi, iz_lo, iz_hi = pick(zl, -1, 2), pick(zh, -1, 2), pick(zl, -1, 3), pick(zh, -1, 3)
        ixo_ref, iyo_ref, izo_ref = outs[12:15]
        ixo_ref[0:1] = ix_lo
        ixo_ref[1:2] = ix_hi
        iyo_ref[...] = pair(iy_lo, iy_hi, iyo_ref.shape, 1)
        izo_ref[...] = pair(iz_lo, iz_hi, izo_ref.shape, 2)
    else:
        vx = vx_ref[...]
        ix = ix_ref[...]
        vy = vy_ref[...]
        iy = iy_ref[...]
        vz = vz_ref[...]
        iz = iz_ref[...]
        vx_lo, vx_hi, ix_lo, ix_hi = vx[0:1], vx[1:2], ix[0:1], ix[1:2]
        vy_lo, vy_hi = pick(vy, 1, 0), pick(vy, 1, 1)
        iy_lo, iy_hi = pick(iy, 1, 0), pick(iy, 1, 1)
        vz_lo, vz_hi, iz_lo, iz_hi = pick(vz, -1, 0), pick(vz, -1, 1), pick(iz, -1, 0), pick(iz, -1, 1)

    pres = p_ref[...]
    idn = idn_ref[...]

    p_first = pick(pres, -1, 0)
    p_last = pick(pres, -1, Z - 1)
    sea = 0.5 * (f_ocean * (p_last + zh1) + f_crust * (zl1 + p_first))
    sfo_ref[...] = sea if first else sf_ref[...] + sea

    above_x = jnp.concatenate([pres[1:], pxh1], axis=0)
    below_x = jnp.concatenate([pxl1, pres[:-1]], axis=0)
    slope_x = 0.5 * (above_x - below_x)
    v0 = v_ref[0] - time_step * idn * slope_x
    v0_lo = vx_lo - time_step * ix_lo * (0.5 * (pres[0:1] - pxl2))
    v0_hi = vx_hi - time_step * ix_hi * (0.5 * (pxh2 - pres[X - 1 : X]))

    p_y0 = pick(pres, 1, 0)
    p_yl = pick(pres, 1, Y - 1)
    above_y = jnp.where(yi == Y - 1, jnp.broadcast_to(yh1, full), pltpu.roll(pres, Y - 1, 1))
    below_y = jnp.where(yi == 0, jnp.broadcast_to(yl1, full), pltpu.roll(pres, 1, 1))
    slope_y = 0.5 * (above_y - below_y)
    v1 = v_ref[1] - time_step * idn * slope_y
    v1_lo = vy_lo - time_step * iy_lo * (0.5 * (p_y0 - yl2))
    v1_hi = vy_hi - time_step * iy_hi * (0.5 * (yh2 - p_yl))

    above_z = jnp.where(zi == Z - 1, jnp.broadcast_to(zh1, full), pltpu.roll(pres, Z - 1, 2))
    below_z = jnp.where(zi == 0, jnp.broadcast_to(zl1, full), pltpu.roll(pres, 1, 2))
    slope_z = wu * above_z + wm * pres + wl * below_z
    v2 = v_ref[2] - time_step * idn * slope_z
    v2_lo = vz_lo - time_step * iz_lo * (wu_lo * p_first + wm_lo * zl1 + wl_lo * zl2)
    v2_hi = vz_hi - time_step * iz_hi * (wu_hi * zh2 + wm_hi * zh1 + wl_hi * p_last)

    vo_ref[0] = v0
    vo_ref[1] = v1
    vo_ref[2] = v2
    vxo_ref[0:1] = v0_lo
    vxo_ref[1:2] = v0_hi
    vyo_ref[...] = pair(v1_lo, v1_hi, vyo_ref.shape, 1)
    vzo_ref[...] = pair(v2_lo, v2_hi, vzo_ref.shape, 2)

    up_x = jnp.concatenate([v0[1:], v0_hi], axis=0)
    down_x = jnp.concatenate([v0_lo, v0[:-1]], axis=0)
    up_y = jnp.where(yi == Y - 1, jnp.broadcast_to(v1_hi, full), pltpu.roll(v1, Y - 1, 1))
    down_y = jnp.where(yi == 0, jnp.broadcast_to(v1_lo, full), pltpu.roll(v1, 1, 1))
    up_z = jnp.where(zi == Z - 1, jnp.broadcast_to(v2_hi, full), pltpu.roll(v2, Z - 1, 2))
    down_z = jnp.where(zi == 0, jnp.broadcast_to(v2_lo, full), pltpu.roll(v2, 1, 2))
    spread = (
        0.5 * (up_x - down_x)
        + 0.5 * (up_y - down_y)
        + (wu * up_z + wm * v2 + wl * down_z)
    )
    new_p = pres - time_step * bulk_ref[...] * spread
    new_p = jnp.where(zi == 0, new_p + jnp.broadcast_to(src_ref[instant], full), new_p)
    po_ref[...] = new_p

    sxu_ref[...] = new_p[X - sxu_ref.shape[0] :]
    sxd_ref[...] = new_p[0 : sxd_ref.shape[0]]
    syu_ref[...] = new_p[:, Y - rows :]
    syd_ref[...] = new_p[:, 0:rows]
    zshape = szu_ref.shape
    szu_ref[...] = pair(pick(new_p, -1, Z - 2), pick(new_p, -1, Z - 1), zshape, 2)
    szd_ref[...] = pair(pick(new_p, -1, 0), pick(new_p, -1, 1), zshape, 2)


def run_step(instant, operands, rows):
    pres = operands[2]
    X, Y, Z = pres.shape
    first = instant == 0
    f32 = jnp.float32
    shapes = [
        jax.ShapeDtypeStruct((X, Y, Z), f32),
        jax.ShapeDtypeStruct((3, X, Y, Z), f32),
        jax.ShapeDtypeStruct((X, Y, 1), f32),
        jax.ShapeDtypeStruct((2, Y, Z), f32),
        jax.ShapeDtypeStruct((X, 2, Z), f32),
        jax.ShapeDtypeStruct((X, Y, 2), f32),
        jax.ShapeDtypeStruct((rows, Y, Z), f32),
        jax.ShapeDtypeStruct((rows, Y, Z), f32),
        jax.ShapeDtypeStruct((X, rows, Z), f32),
        jax.ShapeDtypeStruct((X, rows, Z), f32),
        jax.ShapeDtypeStruct((X, Y, 2), f32),
        jax.ShapeDtypeStruct((X, Y, 2), f32),
    ]
    if first:
        shapes += shapes[3:6]
    vmem = pl.BlockSpec(memory_space=pltpu.VMEM)
    in_specs = [pl.BlockSpec(memory_space=pltpu.SMEM)] + [vmem] * (len(operands) - 1)
    cells = X * Y * Z
    return pl.pallas_call(
        functools.partial(step_kernel, instant, first),
        out_shape=tuple(shapes),
        in_specs=in_specs,
        out_specs=[vmem] * len(shapes),
        cost_estimate=pl.CostEstimate(
            flops=80 * cells, transcendentals=0, bytes_accessed=4 * 4 * 12 * cells // 4
        ),
    )(*operands)


def seafloor_sums(seafloor, node_weight, node_patch, patch_slot):
    sea_values = node_weight[0, 0] * seafloor.reshape(-1)
    slots = patch_slot[node_patch[0, 0]]
    partial_slip = jnp.zeros((patch_slot.shape[0],), jnp.float32).at[slots].add(sea_values)
    return summed_on_arrival(partial_slip, ("gx", "gy"), 0)


def local(
    pressure,
    velocity,
    inv_density,
    bulk,
    node_weight,
    node_patch,
    patch_slot,
    gauge_x,
    gauge_y,
    gauge_misfit,
):
    X, Y, Z = pressure.shape
    rows = 8
    tiles_z = lax.axis_size("gz")
    depth_index = lax.axis_index("gz")
    first_crust = tiles_z // 2 * Z
    levels = depth_index * Z + jnp.arange(Z, dtype=jnp.int32)
    wint = jnp.stack(depth_weights(levels, first_crust)).reshape(3, 1, 1, Z)
    entry = lax.broadcasted_iota(jnp.int32, (ITERS, 16), 1)
    step_at = lax.broadcasted_iota(jnp.int32, (ITERS, 16), 0)
    edge_level = depth_index * Z + jnp.where(entry < 3, -1, Z)
    e_up, e_mid, e_low = depth_weights(edge_level, first_crust)
    kind = entry % 3
    edge_value = jnp.where(kind == 0, e_up, jnp.where(kind == 1, e_mid, e_low))
    ocean = depth_index == first_crust // Z - 1
    crust = depth_index == first_crust // Z
    before = step_at < ITERS - 1
    after = step_at < 0
    flag_value = jnp.where(
        entry == 6, before & ocean,
        jnp.where(entry == 7, before & crust,
                  jnp.where(entry == 8, after & ocean, after & crust)),
    ).astype(jnp.float32)
    scal_all = jnp.where(entry < 6, edge_value, jnp.where(entry < 10, flag_value, 0.0))
    scal_all = scal_all.astype(jnp.float32).reshape(ITERS * 16)
    top_flag = (depth_index == 0).astype(jnp.float32)
    sources = source_planes(
        gauge_x,
        gauge_y,
        gauge_misfit,
        lax.axis_index("gx") * X,
        lax.axis_index("gy") * Y,
        X,
        Y,
    )
    src_all = (time_step * sources * top_flag)[..., None]

    v0, v1, v2 = velocity[0], velocity[1], velocity[2]
    x_up = jnp.concatenate([pressure[X - 2 :], v0[X - 1 :], inv_density[X - 1 :]], axis=0)
    x_dn = jnp.concatenate([pressure[:2], v0[:1], inv_density[:1]], axis=0)
    y_up = jnp.concatenate(
        [pressure[:, Y - rows :], v1[:, Y - 1 :], inv_density[:, Y - 1 :]], axis=1
    )
    y_dn = jnp.concatenate([pressure[:, :rows], v1[:, :1], inv_density[:, :1]], axis=1)
    z_up = jnp.concatenate(
        [pressure[:, :, Z - 2 :], v2[:, :, Z - 1 :], inv_density[:, :, Z - 1 :]], axis=2
    )
    z_dn = jnp.concatenate([pressure[:, :, :2], v2[:, :, :1], inv_density[:, :, :1]], axis=2)
    halos = (
        shifted_up(x_up, "gx"),
        shifted_down(x_dn, "gx"),
        shifted_up(y_up, "gy"),
        shifted_down(y_dn, "gy"),
        shifted_up(z_up, "gz"),
        shifted_down(z_dn, "gz"),
    )
    common = (scal_all, wint)
    pres, vel = pressure, velocity
    for instant in range(ITERS):
        if instant > 0:
            halos = (
                shifted_up(sends[0], "gx"),
                shifted_down(sends[1], "gx"),
                shifted_up(sends[2], "gy"),
                shifted_down(sends[3], "gy"),
                shifted_up(sends[4], "gz"),
                shifted_down(sends[5], "gz"),
            )
        if instant == ITERS - 1:
            ocean = (depth_index == first_crust // Z - 1).astype(jnp.float32)
            crust = (depth_index == first_crust // Z).astype(jnp.float32)
            sf_last = sf + 0.5 * (
                ocean * (sends[4][:, :, 1:2] + halos[5][:, :, 0:1])
                + crust * (halos[4][:, :, 1:2] + sends[5][:, :, 0:1])
            )
            owner_sums = seafloor_sums(sf_last[:, :, 0], node_weight, node_patch, patch_slot)
        if instant == 0:
            operands = common + (pres, vel, inv_density, bulk, src_all) + halos
        else:
            operands = common + (pres, vel, inv_density, bulk, src_all, sf) + halos + tracked + media_halo
        outs = run_step(instant, operands, rows)
        pres, vel, sf = outs[0], outs[1], outs[2]
        tracked = outs[3:6]
        sends = outs[6:12]
        if instant == 0:
            media_halo = outs[12:15]
    ocean_plane = first_crust // Z - 1
    crust_plane = first_crust // Z
    spread_out = lax.ppermute(
        owner_sums, "gz", [(ocean_plane, ocean_plane - 1), (crust_plane, crust_plane + 1)]
    )
    inner = (depth_index == ocean_plane) | (depth_index == crust_plane)
    owner_sums = jnp.where(inner, owner_sums, spread_out)
    piece = owner_sums.shape[0] // tiles_z
    slip_grad = lax.dynamic_slice_in_dim(owner_sums, depth_index * piece, piece)
    return (pres, vel, slip_grad)


def solution(mesh):
    placed = (
        P("gx", "gy", "gz"),
        P(None, "gx", "gy", "gz"),
        P("gx", "gy", "gz"),
        P("gx", "gy", "gz"),
        P("gx", "gy", None),
        P("gx", "gy", None),
        P(),
        P(),
        P(),
        P(),
    )
    return jax.shard_map(
        local,
        mesh=mesh,
        in_specs=placed,
        out_specs=(P("gx", "gy", "gz"), P(None, "gx", "gy", "gz"), P(("gx", "gy", "gz"))),
        check_vma=False,
    )
```

```python
import functools

import jax
import jax.numpy as jnp
from jax import lax
from jax.experimental import pallas as pl
from jax.experimental.pallas import tpu as pltpu
from jax.sharding import PartitionSpec as P

ITERS = 4


time_step = 0.5


def shifted_up(x, axis):
    count = lax.axis_size(axis)
    return lax.ppermute(x, axis, [(i, i + 1) for i in range(count - 1)])


def shifted_down(x, axis):
    count = lax.axis_size(axis)
    return lax.ppermute(x, axis, [(i + 1, i) for i in range(count - 1)])


def in_blocks(x, dim, size):
    before, after = (x.shape[:dim], x.shape[dim + 1 :])
    return jnp.moveaxis(x.reshape(*before, size, -1, *after), dim, 0)


def summed_on_arrival(x, axis, dim):
    size = lax.axis_size(axis)
    parts = lax.all_to_all(in_blocks(x, dim, size), axis, 0, 0, tiled=True)
    return jnp.sum(parts, axis=0)


def depth_weights(levels, first_crust):
    ocean_last = levels == first_crust - 1
    crust_first = levels == first_crust
    weight_above = jnp.where(ocean_last, 0.5, jnp.where(crust_first, 1.0, 0.5)).astype(jnp.float32)
    weight_here = jnp.where(ocean_last, 0.5, jnp.where(crust_first, -1.5, 0.0)).astype(jnp.float32)
    weight_below = jnp.where(ocean_last, -1.0, jnp.where(crust_first, 0.5, -0.5)).astype(
        jnp.float32
    )
    return (weight_above, weight_here, weight_below)


def source_planes(gauge_x, gauge_y, gauge_misfit, start_x, start_y, span_x, span_y):
    local_x = gauge_x - start_x
    local_y = gauge_y - start_y
    inside = (local_x >= 0) & (local_x < span_x) & (local_y >= 0) & (local_y < span_y)
    gauge_cell = jnp.where(inside, local_x * span_y + local_y, -1)
    gauge_table = (
        gauge_cell[:, None] == jnp.arange(span_x * span_y, dtype=jnp.int32)[None, :]
    ).astype(jnp.float32)
    return jnp.dot(gauge_misfit, gauge_table, precision=lax.Precision.HIGHEST).reshape(
        gauge_misfit.shape[0], span_x, span_y
    )


def pick(a, axis, index):
    return lax.slice_in_dim(a, index, index + 1, axis=axis % a.ndim)


def pair(lo, hi, shape, axis):
    where = lax.broadcasted_iota(jnp.int32, shape, axis) == 0
    return jnp.where(where, jnp.broadcast_to(lo, shape), jnp.broadcast_to(hi, shape))


def step_kernel(instant, first, *refs):
    if first:
        (scal_ref, wint_ref, p_ref, v_ref, idn_ref, bulk_ref, src_ref,
         xl_ref, xh_ref, yl_ref, yh_ref, zl_ref, zh_ref) = refs[:13]
        outs = refs[13:]
    else:
        (scal_ref, wint_ref, p_ref, v_ref, idn_ref, bulk_ref, src_ref, sf_ref,
         xl_ref, xh_ref, yl_ref, yh_ref, zl_ref, zh_ref,
         vx_ref, vy_ref, vz_ref, ix_ref, iy_ref, iz_ref) = refs[:20]
        outs = refs[20:]
    (po_ref, vo_ref, sfo_ref, vxo_ref, vyo_ref, vzo_ref,
     sxu_ref, sxd_ref, syu_ref, syd_ref, szu_ref, szd_ref) = outs[:12]
    X, Y, Z = p_ref.shape
    rows = syu_ref.shape[1]
    base = instant * 16
    full = (X, Y, Z)
    yi = lax.broadcasted_iota(jnp.int32, full, 1)
    zi = lax.broadcasted_iota(jnp.int32, full, 2)
    wu = wint_ref[0]
    wm = wint_ref[1]
    wl = wint_ref[2]
    wu_lo = scal_ref[base + 0]
    wm_lo = scal_ref[base + 1]
    wl_lo = scal_ref[base + 2]
    wu_hi = scal_ref[base + 3]
    wm_hi = scal_ref[base + 4]
    wl_hi = scal_ref[base + 5]
    f_ocean = scal_ref[base + 6]
    f_crust = scal_ref[base + 7]

    xl = xl_ref[...]
    xh = xh_ref[...]
    yl = yl_ref[...]
    yh = yh_ref[...]
    zl = zl_ref[...]
    zh = zh_ref[...]
    pxl2, pxl1 = xl[0:1], xl[1:2]
    pxh1, pxh2 = xh[0:1], xh[1:2]
    yl2, yl1 = pick(yl, 1, rows - 2), pick(yl, 1, rows - 1)
    yh1, yh2 = pick(yh, 1, 0), pick(yh, 1, 1)
    zl2, zl1 = pick(zl, -1, 0), pick(zl, -1, 1)
    zh1, zh2 = pick(zh, -1, 0), pick(zh, -1, 1)
    if first:
        vx_lo, vx_hi, ix_lo, ix_hi = xl[2:3], xh[2:3], xl[3:4], xh[3:4]
        vy_lo, vy_hi = pick(yl, 1, rows), pick(yh, 1, rows)
        iy_lo, iy_hi = pick(yl, 1, rows + 1), pick(yh, 1, rows + 1)
        vz_lo, vz_hi, iz_lo, iz_hi = pick(zl, -1, 2), pick(zh, -1, 2), pick(zl, -1, 3), pick(zh, -1, 3)
        ixo_ref, iyo_ref, izo_ref = outs[12:15]
        ixo_ref[0:1] = ix_lo
        ixo_ref[1:2] = ix_hi
        iyo_ref[...] = pair(iy_lo, iy_hi, iyo_ref.shape, 1)
        izo_ref[...] = pair(iz_lo, iz_hi, izo_ref.shape, 2)
    else:
        vx = vx_ref[...]
        ix = ix_ref[...]
        vy = vy_ref[...]
        iy = iy_ref[...]
        vz = vz_ref[...]
        iz = iz_ref[...]
        vx_lo, vx_hi, ix_lo, ix_hi = vx[0:1], vx[1:2], ix[0:1], ix[1:2]
        vy_lo, vy_hi = pick(vy, 1, 0), pick(vy, 1, 1)
        iy_lo, iy_hi = pick(iy, 1, 0), pick(iy, 1, 1)
        vz_lo, vz_hi, iz_lo, iz_hi = pick(vz, -1, 0), pick(vz, -1, 1), pick(iz, -1, 0), pick(iz, -1, 1)

    pres = p_ref[...]
    idn = idn_ref[...]

    p_first = pick(pres, -1, 0)
    p_last = pick(pres, -1, Z - 1)
    sea = 0.5 * (f_ocean * (p_last + zh1) + f_crust * (zl1 + p_first))
    sfo_ref[...] = sea if first else sf_ref[...] + sea

    above_x = jnp.concatenate([pres[1:], pxh1], axis=0)
    below_x = jnp.concatenate([pxl1, pres[:-1]], axis=0)
    slope_x = 0.5 * (above_x - below_x)
    v0 = v_ref[0] - time_step * idn * slope_x
    v0_lo = vx_lo - time_step * ix_lo * (0.5 * (pres[0:1] - pxl2))
    v0_hi = vx_hi - time_step * ix_hi * (0.5 * (pxh2 - pres[X - 1 : X]))

    p_y0 = pick(pres, 1, 0)
    p_yl = pick(pres, 1, Y - 1)
    above_y = jnp.where(yi == Y - 1, jnp.broadcast_to(yh1, full), pltpu.roll(pres, Y - 1, 1))
    below_y = jnp.where(yi == 0, jnp.broadcast_to(yl1, full), pltpu.roll(pres, 1, 1))
    slope_y = 0.5 * (above_y - below_y)
    v1 = v_ref[1] - time_step * idn * slope_y
    v1_lo = vy_lo - time_step * iy_lo * (0.5 * (p_y0 - yl2))
    v1_hi = vy_hi - time_step * iy_hi * (0.5 * (yh2 - p_yl))

    above_z = jnp.where(zi == Z - 1, jnp.broadcast_to(zh1, full), pltpu.roll(pres, Z - 1, 2))
    below_z = jnp.where(zi == 0, jnp.broadcast_to(zl1, full), pltpu.roll(pres, 1, 2))
    slope_z = wu * above_z + wm * pres + wl * below_z
    v2 = v_ref[2] - time_step * idn * slope_z
    v2_lo = vz_lo - time_step * iz_lo * (wu_lo * p_first + wm_lo * zl1 + wl_lo * zl2)
    v2_hi = vz_hi - time_step * iz_hi * (wu_hi * zh2 + wm_hi * zh1 + wl_hi * p_last)

    vo_ref[0] = v0
    vo_ref[1] = v1
    vo_ref[2] = v2
    vxo_ref[0:1] = v0_lo
    vxo_ref[1:2] = v0_hi
    vyo_ref[...] = pair(v1_lo, v1_hi, vyo_ref.shape, 1)
    vzo_ref[...] = pair(v2_lo, v2_hi, vzo_ref.shape, 2)

    up_x = jnp.concatenate([v0[1:], v0_hi], axis=0)
    down_x = jnp.concatenate([v0_lo, v0[:-1]], axis=0)
    up_y = jnp.where(yi == Y - 1, jnp.broadcast_to(v1_hi, full), pltpu.roll(v1, Y - 1, 1))
    down_y = jnp.where(yi == 0, jnp.broadcast_to(v1_lo, full), pltpu.roll(v1, 1, 1))
    up_z = jnp.where(zi == Z - 1, jnp.broadcast_to(v2_hi, full), pltpu.roll(v2, Z - 1, 2))
    down_z = jnp.where(zi == 0, jnp.broadcast_to(v2_lo, full), pltpu.roll(v2, 1, 2))
    spread = (
        0.5 * (up_x - down_x)
        + 0.5 * (up_y - down_y)
        + (wu * up_z + wm * v2 + wl * down_z)
    )
    new_p = pres - time_step * bulk_ref[...] * spread
    new_p = jnp.where(zi == 0, new_p + jnp.broadcast_to(src_ref[instant], full), new_p)
    po_ref[...] = new_p

    sxu_ref[...] = new_p[X - 2 :]
    sxd_ref[...] = new_p[0:2]
    syu_ref[...] = new_p[:, Y - rows :]
    syd_ref[...] = new_p[:, 0:rows]
    zshape = szu_ref.shape
    szu_ref[...] = pair(pick(new_p, -1, Z - 2), pick(new_p, -1, Z - 1), zshape, 2)
    szd_ref[...] = pair(pick(new_p, -1, 0), pick(new_p, -1, 1), zshape, 2)


def run_step(instant, operands, rows):
    pres = operands[2]
    X, Y, Z = pres.shape
    first = instant == 0
    f32 = jnp.float32
    shapes = [
        jax.ShapeDtypeStruct((X, Y, Z), f32),
        jax.ShapeDtypeStruct((3, X, Y, Z), f32),
        jax.ShapeDtypeStruct((X, Y, 1), f32),
        jax.ShapeDtypeStruct((2, Y, Z), f32),
        jax.ShapeDtypeStruct((X, 2, Z), f32),
        jax.ShapeDtypeStruct((X, Y, 2), f32),
        jax.ShapeDtypeStruct((2, Y, Z), f32),
        jax.ShapeDtypeStruct((2, Y, Z), f32),
        jax.ShapeDtypeStruct((X, rows, Z), f32),
        jax.ShapeDtypeStruct((X, rows, Z), f32),
        jax.ShapeDtypeStruct((X, Y, 2), f32),
        jax.ShapeDtypeStruct((X, Y, 2), f32),
    ]
    if first:
        shapes += shapes[3:6]
    vmem = pl.BlockSpec(memory_space=pltpu.VMEM)
    in_specs = [pl.BlockSpec(memory_space=pltpu.SMEM)] + [vmem] * (len(operands) - 1)
    cells = X * Y * Z
    return pl.pallas_call(
        functools.partial(step_kernel, instant, first),
        out_shape=tuple(shapes),
        in_specs=in_specs,
        out_specs=[vmem] * len(shapes),
        cost_estimate=pl.CostEstimate(
            flops=80 * cells, transcendentals=0, bytes_accessed=4 * 4 * 12 * cells // 4
        ),
    )(*operands)


def seafloor_sums(seafloor, node_weight, node_patch, patch_slot):
    sea_values = node_weight[0, 0] * seafloor.reshape(-1)
    slots = patch_slot[node_patch[0, 0]]
    owners = lax.axis_size("gx") * lax.axis_size("gy")
    per_owner = patch_slot.shape[0] // owners
    owner_hot = slots[None, :] // per_owner == jnp.arange(owners, dtype=jnp.int32)[:, None]
    within_hot = (
        slots[:, None] % per_owner == jnp.arange(per_owner, dtype=jnp.int32)[None, :]
    ).astype(jnp.float32)
    weighted = jnp.where(owner_hot, sea_values[None, :], 0.0)
    partial_slip = jnp.dot(weighted, within_hot, precision=lax.Precision.HIGHEST).reshape(-1)
    return summed_on_arrival(partial_slip, ("gx", "gy"), 0)


def local(
    pressure,
    velocity,
    inv_density,
    bulk,
    node_weight,
    node_patch,
    patch_slot,
    gauge_x,
    gauge_y,
    gauge_misfit,
):
    X, Y, Z = pressure.shape
    rows = 8
    tiles_z = lax.axis_size("gz")
    depth_index = lax.axis_index("gz")
    first_crust = tiles_z // 2 * Z
    levels = depth_index * Z + jnp.arange(Z, dtype=jnp.int32)
    level_grid = depth_index * Z + lax.broadcasted_iota(jnp.int32, (3, 1, 1, Z), 3)
    w_up, w_mid, w_low = depth_weights(level_grid, first_crust)
    which = lax.broadcasted_iota(jnp.int32, (3, 1, 1, Z), 0)
    wint = jnp.where(which == 0, w_up, jnp.where(which == 1, w_mid, w_low))
    entry = lax.broadcasted_iota(jnp.int32, (ITERS * 16,), 0) % 16
    step_at = lax.broadcasted_iota(jnp.int32, (ITERS * 16,), 0) // 16
    edge_level = depth_index * Z + jnp.where(entry < 3, -1, Z)
    e_up, e_mid, e_low = depth_weights(edge_level, first_crust)
    kind = entry % 3
    edge_value = jnp.where(kind == 0, e_up, jnp.where(kind == 1, e_mid, e_low))
    ocean = depth_index == first_crust // Z - 1
    crust = depth_index == first_crust // Z
    before = step_at < ITERS - 1
    after = step_at < 0
    flag_value = jnp.where(
        entry == 6, before & ocean,
        jnp.where(entry == 7, before & crust,
                  jnp.where(entry == 8, after & ocean, after & crust)),
    ).astype(jnp.float32)
    scal_all = jnp.where(entry < 6, edge_value, jnp.where(entry < 10, flag_value, 0.0))
    scal_all = scal_all.astype(jnp.float32)
    top_flag = (depth_index == 0).astype(jnp.float32)
    sources = source_planes(
        gauge_x,
        gauge_y,
        gauge_misfit,
        lax.axis_index("gx") * X,
        lax.axis_index("gy") * Y,
        X,
        Y,
    )
    src_all = (time_step * sources * top_flag)[..., None]

    v0, v1, v2 = velocity[0], velocity[1], velocity[2]
    x_up = jnp.concatenate([pressure[X - 2 :], v0[X - 1 :], inv_density[X - 1 :]], axis=0)
    x_dn = jnp.concatenate([pressure[:2], v0[:1], inv_density[:1]], axis=0)
    y_up = jnp.concatenate(
        [pressure[:, Y - rows :], v1[:, Y - 1 :], inv_density[:, Y - 1 :]], axis=1
    )
    y_dn = jnp.concatenate([pressure[:, :rows], v1[:, :1], inv_density[:, :1]], axis=1)
    z_up = jnp.concatenate(
        [pressure[:, :, Z - 2 :], v2[:, :, Z - 1 :], inv_density[:, :, Z - 1 :]], axis=2
    )
    z_dn = jnp.concatenate([pressure[:, :, :2], v2[:, :, :1], inv_density[:, :, :1]], axis=2)
    halos = (
        shifted_up(x_up, "gx"),
        shifted_down(x_dn, "gx"),
        shifted_up(y_up, "gy"),
        shifted_down(y_dn, "gy"),
        shifted_up(z_up, "gz"),
        shifted_down(z_dn, "gz"),
    )
    common = (scal_all, wint)
    pres, vel = pressure, velocity
    for instant in range(ITERS):
        if instant > 0:
            halos = (
                shifted_up(sends[0], "gx"),
                shifted_down(sends[1], "gx"),
                shifted_up(sends[2], "gy"),
                shifted_down(sends[3], "gy"),
                shifted_up(sends[4], "gz"),
                shifted_down(sends[5], "gz"),
            )
        if instant == ITERS - 1:
            ocean = (depth_index == first_crust // Z - 1).astype(jnp.float32)
            crust = (depth_index == first_crust // Z).astype(jnp.float32)
            sf_last = sf + 0.5 * (
                ocean * (sends[4][:, :, 1:2] + halos[5][:, :, 0:1])
                + crust * (halos[4][:, :, 1:2] + sends[5][:, :, 0:1])
            )
            owner_sums = seafloor_sums(sf_last[:, :, 0], node_weight, node_patch, patch_slot)
        if instant == 0:
            operands = common + (pres, vel, inv_density, bulk, src_all) + halos
        else:
            operands = common + (pres, vel, inv_density, bulk, src_all, sf) + halos + tracked + media_halo
        outs = run_step(instant, operands, rows)
        pres, vel, sf = outs[0], outs[1], outs[2]
        tracked = outs[3:6]
        sends = outs[6:12]
        if instant == 0:
            media_halo = outs[12:15]
    ocean_plane = first_crust // Z - 1
    crust_plane = first_crust // Z
    spread_out = lax.ppermute(
        owner_sums, "gz", [(ocean_plane, ocean_plane - 1), (crust_plane, crust_plane + 1)]
    )
    inner = (depth_index == ocean_plane) | (depth_index == crust_plane)
    owner_sums = jnp.where(inner, owner_sums, spread_out)
    piece = owner_sums.shape[0] // tiles_z
    slip_grad = lax.dynamic_slice_in_dim(owner_sums, depth_index * piece, piece)
    return (pres, vel, slip_grad)


def solution(mesh):
    placed = (
        P("gx", "gy", "gz"),
        P(None, "gx", "gy", "gz"),
        P("gx", "gy", "gz"),
        P("gx", "gy", "gz"),
        P("gx", "gy", None),
        P("gx", "gy", None),
        P(),
        P(),
        P(),
        P(),
    )
    return jax.shard_map(
        local,
        mesh=mesh,
        in_specs=placed,
        out_specs=(P("gx", "gy", "gz"), P(None, "gx", "gy", "gz"), P(("gx", "gy", "gz"))),
        check_vma=False,
    )
```

```python
import functools

import jax
import jax.numpy as jnp
from jax import lax
from jax.experimental import pallas as pl
from jax.experimental.pallas import tpu as pltpu
from jax.sharding import PartitionSpec as P

ITERS = 4


time_step = 0.5


def shifted_up(x, axis):
    count = lax.axis_size(axis)
    return lax.ppermute(x, axis, [(i, i + 1) for i in range(count - 1)])


def shifted_down(x, axis):
    count = lax.axis_size(axis)
    return lax.ppermute(x, axis, [(i + 1, i) for i in range(count - 1)])


def in_blocks(x, dim, size):
    before, after = (x.shape[:dim], x.shape[dim + 1 :])
    return jnp.moveaxis(x.reshape(*before, size, -1, *after), dim, 0)


def summed_on_arrival(x, axis, dim):
    size = lax.axis_size(axis)
    parts = lax.all_to_all(in_blocks(x, dim, size), axis, 0, 0, tiled=True)
    return jnp.sum(parts, axis=0)


def depth_weights(levels, first_crust):
    ocean_last = levels == first_crust - 1
    crust_first = levels == first_crust
    weight_above = jnp.where(ocean_last, 0.5, jnp.where(crust_first, 1.0, 0.5)).astype(jnp.float32)
    weight_here = jnp.where(ocean_last, 0.5, jnp.where(crust_first, -1.5, 0.0)).astype(jnp.float32)
    weight_below = jnp.where(ocean_last, -1.0, jnp.where(crust_first, 0.5, -0.5)).astype(
        jnp.float32
    )
    return (weight_above, weight_here, weight_below)


def source_planes(gauge_x, gauge_y, gauge_misfit, start_x, start_y, span_x, span_y):
    local_x = gauge_x - start_x
    local_y = gauge_y - start_y
    inside = (local_x >= 0) & (local_x < span_x) & (local_y >= 0) & (local_y < span_y)
    gauge_cell = jnp.where(inside, local_x * span_y + local_y, -1)
    gauge_table = (
        gauge_cell[:, None] == jnp.arange(span_x * span_y, dtype=jnp.int32)[None, :]
    ).astype(jnp.float32)
    return jnp.dot(gauge_misfit, gauge_table, precision=lax.Precision.HIGHEST).reshape(
        gauge_misfit.shape[0], span_x, span_y
    )


def pick(a, axis, index):
    return lax.slice_in_dim(a, index, index + 1, axis=axis % a.ndim)


def pair(lo, hi, shape, axis):
    where = lax.broadcasted_iota(jnp.int32, shape, axis) == 0
    return jnp.where(where, jnp.broadcast_to(lo, shape), jnp.broadcast_to(hi, shape))


def quad(parts, shape):
    lane = lax.broadcasted_iota(jnp.int32, shape, len(shape) - 1)
    out = jnp.broadcast_to(parts[-1], shape)
    for index in range(len(parts) - 2, -1, -1):
        out = jnp.where(lane == index, jnp.broadcast_to(parts[index], shape), out)
    return out


def step_kernel(instant, first, *refs):
    if first:
        (scal_ref, wint_ref, p_ref, v_ref, idn_ref, bulk_ref, src_ref,
         xl_ref, xh_ref, yl_ref, yh_ref, zl_ref, zh_ref) = refs[:13]
        outs = refs[13:]
    else:
        (scal_ref, wint_ref, p_ref, v_ref, idn_ref, bulk_ref, src_ref, sf_ref,
         xl_ref, xh_ref, yl_ref, yh_ref, zl_ref, zh_ref,
         vx_ref, vy_ref, ix_ref, iy_ref) = refs[:18]
        outs = refs[18:]
    (po_ref, vo_ref, sfo_ref, vxo_ref, vyo_ref,
     sxu_ref, sxd_ref, syu_ref, syd_ref, szu_ref, szd_ref) = outs[:11]
    X, Y, Z = p_ref.shape
    rows = syu_ref.shape[1]
    base = instant * 16
    full = (X, Y, Z)
    yi = lax.broadcasted_iota(jnp.int32, full, 1)
    zi = lax.broadcasted_iota(jnp.int32, full, 2)
    wu = wint_ref[0]
    wm = wint_ref[1]
    wl = wint_ref[2]
    wu_lo = scal_ref[base + 0]
    wm_lo = scal_ref[base + 1]
    wl_lo = scal_ref[base + 2]
    wu_hi = scal_ref[base + 3]
    wm_hi = scal_ref[base + 4]
    wl_hi = scal_ref[base + 5]
    f_ocean = scal_ref[base + 6]
    f_crust = scal_ref[base + 7]

    xl = xl_ref[...]
    xh = xh_ref[...]
    yl = yl_ref[...]
    yh = yh_ref[...]
    zl = zl_ref[...]
    zh = zh_ref[...]
    pxl2, pxl1 = xl[0:1], xl[1:2]
    pxh1, pxh2 = xh[0:1], xh[1:2]
    yl2, yl1 = pick(yl, 1, rows - 2), pick(yl, 1, rows - 1)
    yh1, yh2 = pick(yh, 1, 0), pick(yh, 1, 1)
    zl2, zl1 = pick(zl, -1, 0), pick(zl, -1, 1)
    zh1, zh2 = pick(zh, -1, 0), pick(zh, -1, 1)
    vz_lo, vz_hi, iz_lo, iz_hi = pick(zl, -1, 2), pick(zh, -1, 2), pick(zl, -1, 3), pick(zh, -1, 3)
    if first:
        vx_lo, vx_hi, ix_lo, ix_hi = xl[2:3], xh[2:3], xl[3:4], xh[3:4]
        vy_lo, vy_hi = pick(yl, 1, rows), pick(yh, 1, rows)
        iy_lo, iy_hi = pick(yl, 1, rows + 1), pick(yh, 1, rows + 1)
        ixo_ref, iyo_ref = outs[11:13]
        ixo_ref[0:1] = ix_lo
        ixo_ref[1:2] = ix_hi
        iyo_ref[...] = pair(iy_lo, iy_hi, iyo_ref.shape, 1)
    else:
        vx = vx_ref[...]
        ix = ix_ref[...]
        vy = vy_ref[...]
        iy = iy_ref[...]
        vx_lo, vx_hi, ix_lo, ix_hi = vx[0:1], vx[1:2], ix[0:1], ix[1:2]
        vy_lo, vy_hi = pick(vy, 1, 0), pick(vy, 1, 1)
        iy_lo, iy_hi = pick(iy, 1, 0), pick(iy, 1, 1)

    pres = p_ref[...]
    idn = idn_ref[...]

    p_first = pick(pres, -1, 0)
    p_last = pick(pres, -1, Z - 1)
    sea = 0.5 * (f_ocean * (p_last + zh1) + f_crust * (zl1 + p_first))
    sfo_ref[...] = sea if first else sf_ref[...] + sea

    above_x = jnp.concatenate([pres[1:], pxh1], axis=0)
    below_x = jnp.concatenate([pxl1, pres[:-1]], axis=0)
    slope_x = 0.5 * (above_x - below_x)
    v0 = v_ref[0] - time_step * idn * slope_x
    v0_lo = vx_lo - time_step * ix_lo * (0.5 * (pres[0:1] - pxl2))
    v0_hi = vx_hi - time_step * ix_hi * (0.5 * (pxh2 - pres[X - 1 : X]))

    p_y0 = pick(pres, 1, 0)
    p_yl = pick(pres, 1, Y - 1)
    above_y = jnp.where(yi == Y - 1, jnp.broadcast_to(yh1, full), pltpu.roll(pres, Y - 1, 1))
    below_y = jnp.where(yi == 0, jnp.broadcast_to(yl1, full), pltpu.roll(pres, 1, 1))
    slope_y = 0.5 * (above_y - below_y)
    v1 = v_ref[1] - time_step * idn * slope_y
    v1_lo = vy_lo - time_step * iy_lo * (0.5 * (p_y0 - yl2))
    v1_hi = vy_hi - time_step * iy_hi * (0.5 * (yh2 - p_yl))

    above_z = jnp.where(zi == Z - 1, jnp.broadcast_to(zh1, full), pltpu.roll(pres, Z - 1, 2))
    below_z = jnp.where(zi == 0, jnp.broadcast_to(zl1, full), pltpu.roll(pres, 1, 2))
    slope_z = wu * above_z + wm * pres + wl * below_z
    v2 = v_ref[2] - time_step * idn * slope_z
    v2_lo = vz_lo - time_step * iz_lo * (wu_lo * p_first + wm_lo * zl1 + wl_lo * zl2)
    v2_hi = vz_hi - time_step * iz_hi * (wu_hi * zh2 + wm_hi * zh1 + wl_hi * p_last)

    vo_ref[0] = v0
    vo_ref[1] = v1
    vo_ref[2] = v2
    vxo_ref[0:1] = v0_lo
    vxo_ref[1:2] = v0_hi
    vyo_ref[...] = pair(v1_lo, v1_hi, vyo_ref.shape, 1)

    up_x = jnp.concatenate([v0[1:], v0_hi], axis=0)
    down_x = jnp.concatenate([v0_lo, v0[:-1]], axis=0)
    up_y = jnp.where(yi == Y - 1, jnp.broadcast_to(v1_hi, full), pltpu.roll(v1, Y - 1, 1))
    down_y = jnp.where(yi == 0, jnp.broadcast_to(v1_lo, full), pltpu.roll(v1, 1, 1))
    up_z = jnp.where(zi == Z - 1, jnp.broadcast_to(v2_hi, full), pltpu.roll(v2, Z - 1, 2))
    down_z = jnp.where(zi == 0, jnp.broadcast_to(v2_lo, full), pltpu.roll(v2, 1, 2))
    spread = (
        0.5 * (up_x - down_x)
        + 0.5 * (up_y - down_y)
        + (wu * up_z + wm * v2 + wl * down_z)
    )
    new_p = pres - time_step * bulk_ref[...] * spread
    new_p = jnp.where(zi == 0, new_p + jnp.broadcast_to(src_ref[...], full), new_p)
    po_ref[...] = new_p

    sxu_ref[...] = new_p[X - 2 :]
    sxd_ref[...] = new_p[0:2]
    syu_ref[...] = new_p[:, Y - rows :]
    syd_ref[...] = new_p[:, 0:rows]
    zshape = szu_ref.shape
    szu_ref[...] = quad(
        (pick(new_p, -1, Z - 2), pick(new_p, -1, Z - 1), pick(v2, -1, Z - 1), pick(idn, -1, Z - 1)), zshape
    )
    szd_ref[...] = quad((pick(new_p, -1, 0), pick(new_p, -1, 1), pick(v2, -1, 0), pick(idn, -1, 0)), zshape)


def run_step(instant, operands, rows):
    pres = operands[2]
    X, Y, Z = pres.shape
    first = instant == 0
    f32 = jnp.float32
    shapes = [
        jax.ShapeDtypeStruct((X, Y, Z), f32),
        jax.ShapeDtypeStruct((3, X, Y, Z), f32),
        jax.ShapeDtypeStruct((X, Y, 1), f32),
        jax.ShapeDtypeStruct((2, Y, Z), f32),
        jax.ShapeDtypeStruct((X, 2, Z), f32),
        jax.ShapeDtypeStruct((2, Y, Z), f32),
        jax.ShapeDtypeStruct((2, Y, Z), f32),
        jax.ShapeDtypeStruct((X, rows, Z), f32),
        jax.ShapeDtypeStruct((X, rows, Z), f32),
        jax.ShapeDtypeStruct((X, Y, 4), f32),
        jax.ShapeDtypeStruct((X, Y, 4), f32),
    ]
    if first:
        shapes += shapes[3:5]
    vmem = pl.BlockSpec(memory_space=pltpu.VMEM)
    in_specs = [pl.BlockSpec(memory_space=pltpu.SMEM)] + [vmem] * (len(operands) - 1)
    in_specs[6] = pl.BlockSpec((None, X, Y, 1), lambda i: (instant, 0, 0, 0))
    cells = X * Y * Z
    return pl.pallas_call(
        functools.partial(step_kernel, instant, first),
        out_shape=tuple(shapes),
        grid=(1,),
        in_specs=in_specs,
        out_specs=[vmem] * len(shapes),
        cost_estimate=pl.CostEstimate(
            flops=80 * cells, transcendentals=0, bytes_accessed=4 * 4 * 12 * cells // 4
        ),
    )(*operands)


def seafloor_sums(seafloor, node_weight, node_patch, patch_slot):
    sea_values = node_weight[0, 0] * seafloor.reshape(-1)
    slots = patch_slot[node_patch[0, 0]]
    owners = lax.axis_size("gx") * lax.axis_size("gy")
    per_owner = patch_slot.shape[0] // owners
    owner_hot = slots[None, :] // per_owner == jnp.arange(owners, dtype=jnp.int32)[:, None]
    within_hot = (
        slots[:, None] % per_owner == jnp.arange(per_owner, dtype=jnp.int32)[None, :]
    ).astype(jnp.float32)
    weighted = jnp.where(owner_hot, sea_values[None, :], 0.0)
    partial_slip = jnp.dot(weighted, within_hot, precision=lax.Precision.HIGHEST).reshape(-1)
    return summed_on_arrival(partial_slip, ("gx", "gy"), 0)


def local(
    pressure,
    velocity,
    inv_density,
    bulk,
    node_weight,
    node_patch,
    patch_slot,
    gauge_x,
    gauge_y,
    gauge_misfit,
):
    X, Y, Z = pressure.shape
    rows = 8
    tiles_z = lax.axis_size("gz")
    depth_index = lax.axis_index("gz")
    first_crust = tiles_z // 2 * Z
    levels = depth_index * Z + jnp.arange(Z, dtype=jnp.int32)
    level_grid = depth_index * Z + lax.broadcasted_iota(jnp.int32, (3, 1, 1, Z), 3)
    w_up, w_mid, w_low = depth_weights(level_grid, first_crust)
    which = lax.broadcasted_iota(jnp.int32, (3, 1, 1, Z), 0)
    wint = jnp.where(which == 0, w_up, jnp.where(which == 1, w_mid, w_low))
    entry = lax.broadcasted_iota(jnp.int32, (ITERS * 16,), 0) % 16
    step_at = lax.broadcasted_iota(jnp.int32, (ITERS * 16,), 0) // 16
    edge_level = depth_index * Z + jnp.where(entry < 3, -1, Z)
    e_up, e_mid, e_low = depth_weights(edge_level, first_crust)
    kind = entry % 3
    edge_value = jnp.where(kind == 0, e_up, jnp.where(kind == 1, e_mid, e_low))
    ocean = depth_index == first_crust // Z - 1
    crust = depth_index == first_crust // Z
    before = step_at < ITERS - 1
    after = step_at < 0
    flag_value = jnp.where(
        entry == 6, before & ocean,
        jnp.where(entry == 7, before & crust,
                  jnp.where(entry == 8, after & ocean, after & crust)),
    ).astype(jnp.float32)
    scal_all = jnp.where(entry < 6, edge_value, jnp.where(entry < 10, flag_value, 0.0))
    scal_all = scal_all.astype(jnp.float32)
    top_flag = (depth_index == 0).astype(jnp.float32)
    sources = source_planes(
        gauge_x,
        gauge_y,
        gauge_misfit,
        lax.axis_index("gx") * X,
        lax.axis_index("gy") * Y,
        X,
        Y,
    )
    src_all = (time_step * sources * top_flag)[..., None]

    v0, v1, v2 = velocity[0], velocity[1], velocity[2]
    x_up = jnp.concatenate([pressure[X - 2 :], v0[X - 1 :], inv_density[X - 1 :]], axis=0)
    x_dn = jnp.concatenate([pressure[:2], v0[:1], inv_density[:1]], axis=0)
    y_up = jnp.concatenate(
        [pressure[:, Y - rows :], v1[:, Y - 1 :], inv_density[:, Y - 1 :]], axis=1
    )
    y_dn = jnp.concatenate([pressure[:, :rows], v1[:, :1], inv_density[:, :1]], axis=1)
    z_up = jnp.concatenate(
        [pressure[:, :, Z - 2 :], v2[:, :, Z - 1 :], inv_density[:, :, Z - 1 :]], axis=2
    )
    z_dn = jnp.concatenate([pressure[:, :, :2], v2[:, :, :1], inv_density[:, :, :1]], axis=2)
    halos = (
        shifted_up(x_up, "gx"),
        shifted_down(x_dn, "gx"),
        shifted_up(y_up, "gy"),
        shifted_down(y_dn, "gy"),
        shifted_up(z_up, "gz"),
        shifted_down(z_dn, "gz"),
    )
    common = (scal_all, wint)
    pres, vel = pressure, velocity
    for instant in range(ITERS):
        if instant > 0:
            halos = (
                shifted_up(sends[0], "gx"),
                shifted_down(sends[1], "gx"),
                shifted_up(sends[2], "gy"),
                shifted_down(sends[3], "gy"),
                shifted_up(sends[4], "gz"),
                shifted_down(sends[5], "gz"),
            )
        if instant == ITERS - 1:
            ocean = (depth_index == first_crust // Z - 1).astype(jnp.float32)
            crust = (depth_index == first_crust // Z).astype(jnp.float32)
            sf_last = sf + 0.5 * (
                ocean * (sends[4][:, :, 1:2] + halos[5][:, :, 0:1])
                + crust * (halos[4][:, :, 1:2] + sends[5][:, :, 0:1])
            )
            owner_sums = seafloor_sums(sf_last[:, :, 0], node_weight, node_patch, patch_slot)
        if instant == 0:
            operands = common + (pres, vel, inv_density, bulk, src_all) + halos
        else:
            operands = common + (pres, vel, inv_density, bulk, src_all, sf) + halos + tracked + media_halo
        outs = run_step(instant, operands, rows)
        pres, vel, sf = outs[0], outs[1], outs[2]
        tracked = outs[3:5]
        sends = outs[5:11]
        if instant == 0:
            media_halo = outs[11:13]
    ocean_plane = first_crust // Z - 1
    crust_plane = first_crust // Z
    spread_out = lax.ppermute(
        owner_sums, "gz", [(ocean_plane, ocean_plane - 1), (crust_plane, crust_plane + 1)]
    )
    inner = (depth_index == ocean_plane) | (depth_index == crust_plane)
    owner_sums = jnp.where(inner, owner_sums, spread_out)
    piece = owner_sums.shape[0] // tiles_z
    slip_grad = lax.dynamic_slice_in_dim(owner_sums, depth_index * piece, piece)
    return (pres, vel, slip_grad)


def solution(mesh):
    placed = (
        P("gx", "gy", "gz"),
        P(None, "gx", "gy", "gz"),
        P("gx", "gy", "gz"),
        P("gx", "gy", "gz"),
        P("gx", "gy", None),
        P("gx", "gy", None),
        P(),
        P(),
        P(),
        P(),
    )
    return jax.shard_map(
        local,
        mesh=mesh,
        in_specs=placed,
        out_specs=(P("gx", "gy", "gz"), P(None, "gx", "gy", "gz"), P(("gx", "gy", "gz"))),
        check_vma=False,
    )
```

```python
import functools

import jax
import jax.numpy as jnp
from jax import lax
from jax.experimental import pallas as pl
from jax.experimental.pallas import tpu as pltpu
from jax.sharding import PartitionSpec as P

ITERS = 4


time_step = 0.5


def shifted_up(x, axis):
    count = lax.axis_size(axis)
    return lax.ppermute(x, axis, [(i, i + 1) for i in range(count - 1)])


def shifted_down(x, axis):
    count = lax.axis_size(axis)
    return lax.ppermute(x, axis, [(i + 1, i) for i in range(count - 1)])


def in_blocks(x, dim, size):
    before, after = (x.shape[:dim], x.shape[dim + 1 :])
    return jnp.moveaxis(x.reshape(*before, size, -1, *after), dim, 0)


def summed_on_arrival(x, axis, dim):
    size = lax.axis_size(axis)
    parts = lax.all_to_all(in_blocks(x, dim, size), axis, 0, 0, tiled=True)
    return jnp.sum(parts, axis=0)


def depth_weights(levels, first_crust):
    ocean_last = levels == first_crust - 1
    crust_first = levels == first_crust
    weight_above = jnp.where(ocean_last, 0.5, jnp.where(crust_first, 1.0, 0.5)).astype(jnp.float32)
    weight_here = jnp.where(ocean_last, 0.5, jnp.where(crust_first, -1.5, 0.0)).astype(jnp.float32)
    weight_below = jnp.where(ocean_last, -1.0, jnp.where(crust_first, 0.5, -0.5)).astype(
        jnp.float32
    )
    return (weight_above, weight_here, weight_below)


def source_planes(gauge_x, gauge_y, gauge_misfit, start_x, start_y, span_x, span_y):
    local_x = gauge_x - start_x
    local_y = gauge_y - start_y
    inside = (local_x >= 0) & (local_x < span_x) & (local_y >= 0) & (local_y < span_y)
    gauge_cell = jnp.where(inside, local_x * span_y + local_y, -1)
    gauge_table = (
        gauge_cell[:, None] == jnp.arange(span_x * span_y, dtype=jnp.int32)[None, :]
    ).astype(jnp.float32)
    return jnp.dot(gauge_misfit, gauge_table, precision=lax.Precision.HIGHEST).reshape(
        gauge_misfit.shape[0], span_x, span_y
    )


def pick(a, axis, index):
    return lax.slice_in_dim(a, index, index + 1, axis=axis % a.ndim)


def pair(lo, hi, shape, axis):
    where = lax.broadcasted_iota(jnp.int32, shape, axis) == 0
    return jnp.where(where, jnp.broadcast_to(lo, shape), jnp.broadcast_to(hi, shape))


def quad(parts, shape):
    lane = lax.broadcasted_iota(jnp.int32, shape, len(shape) - 1)
    out = jnp.broadcast_to(parts[-1], shape)
    for index in range(len(parts) - 2, -1, -1):
        out = jnp.where(lane == index, jnp.broadcast_to(parts[index], shape), out)
    return out


def step_kernel(instant, first, *refs):
    if first:
        (scal_ref, wint_ref, p_ref, v_ref, idn_ref, bulk_ref, src_ref,
         xl_ref, xh_ref, yl_ref, yh_ref, zl_ref, zh_ref) = refs[:13]
        outs = refs[13:]
    else:
        (scal_ref, wint_ref, p_ref, v_ref, idn_ref, bulk_ref, src_ref, sf_ref,
         xl_ref, xh_ref, yl_ref, yh_ref, zl_ref, zh_ref,
         vx_ref, vy_ref, ix_ref, iy_ref) = refs[:18]
        outs = refs[18:]
    (po_ref, vo_ref, sfo_ref, vxo_ref, vyo_ref,
     sxu_ref, sxd_ref, syu_ref, syd_ref, szu_ref, szd_ref) = outs[:11]
    X, Y, Z = p_ref.shape
    rows = syu_ref.shape[1]
    base = instant * 16
    full = (X, Y, Z)
    yi = lax.broadcasted_iota(jnp.int32, full, 1)
    zi = lax.broadcasted_iota(jnp.int32, full, 2)
    wu = wint_ref[0]
    wm = wint_ref[1]
    wl = wint_ref[2]
    wu_lo = scal_ref[base + 0]
    wm_lo = scal_ref[base + 1]
    wl_lo = scal_ref[base + 2]
    wu_hi = scal_ref[base + 3]
    wm_hi = scal_ref[base + 4]
    wl_hi = scal_ref[base + 5]
    f_ocean = scal_ref[base + 6]
    f_crust = scal_ref[base + 7]

    xl = xl_ref[...]
    xh = xh_ref[...]
    yl = yl_ref[...]
    yh = yh_ref[...]
    zl = zl_ref[...]
    zh = zh_ref[...]
    pxl2, pxl1 = xl[0:1], xl[1:2]
    pxh1, pxh2 = xh[0:1], xh[1:2]
    yl2, yl1 = pick(yl, 1, rows - 2), pick(yl, 1, rows - 1)
    yh1, yh2 = pick(yh, 1, 0), pick(yh, 1, 1)
    zl2, zl1 = pick(zl, -1, 0), pick(zl, -1, 1)
    zh1, zh2 = pick(zh, -1, 0), pick(zh, -1, 1)
    vz_lo, vz_hi, iz_lo, iz_hi = pick(zl, -1, 2), pick(zh, -1, 2), pick(zl, -1, 3), pick(zh, -1, 3)
    if first:
        vx_lo, vx_hi, ix_lo, ix_hi = xl[2:3], xh[2:3], xl[3:4], xh[3:4]
        vy_lo, vy_hi = pick(yl, 1, rows), pick(yh, 1, rows)
        iy_lo, iy_hi = pick(yl, 1, rows + 1), pick(yh, 1, rows + 1)
        ixo_ref, iyo_ref = outs[11:13]
        ixo_ref[0:1] = ix_lo
        ixo_ref[1:2] = ix_hi
        iyo_ref[...] = pair(iy_lo, iy_hi, iyo_ref.shape, 1)
    else:
        vx = vx_ref[...]
        ix = ix_ref[...]
        vy = vy_ref[...]
        iy = iy_ref[...]
        vx_lo, vx_hi, ix_lo, ix_hi = vx[0:1], vx[1:2], ix[0:1], ix[1:2]
        vy_lo, vy_hi = pick(vy, 1, 0), pick(vy, 1, 1)
        iy_lo, iy_hi = pick(iy, 1, 0), pick(iy, 1, 1)

    pres = p_ref[...]
    idn = idn_ref[...]

    p_first = pick(pres, -1, 0)
    p_last = pick(pres, -1, Z - 1)
    sea = 0.5 * (f_ocean * p_last + f_crust * p_first)
    sfo_ref[...] = sea if first else sf_ref[...] + sea

    above_x = jnp.concatenate([pres[1:], pxh1], axis=0)
    below_x = jnp.concatenate([pxl1, pres[:-1]], axis=0)
    slope_x = 0.5 * (above_x - below_x)
    v0 = v_ref[0] - time_step * idn * slope_x
    v0_lo = vx_lo - time_step * ix_lo * (0.5 * (pres[0:1] - pxl2))
    v0_hi = vx_hi - time_step * ix_hi * (0.5 * (pxh2 - pres[X - 1 : X]))

    p_y0 = pick(pres, 1, 0)
    p_yl = pick(pres, 1, Y - 1)
    above_y = jnp.where(yi == Y - 1, jnp.broadcast_to(yh1, full), pltpu.roll(pres, Y - 1, 1))
    below_y = jnp.where(yi == 0, jnp.broadcast_to(yl1, full), pltpu.roll(pres, 1, 1))
    slope_y = 0.5 * (above_y - below_y)
    v1 = v_ref[1] - time_step * idn * slope_y
    v1_lo = vy_lo - time_step * iy_lo * (0.5 * (p_y0 - yl2))
    v1_hi = vy_hi - time_step * iy_hi * (0.5 * (yh2 - p_yl))

    above_z = jnp.where(zi == Z - 1, jnp.broadcast_to(zh1, full), pltpu.roll(pres, Z - 1, 2))
    below_z = jnp.where(zi == 0, jnp.broadcast_to(zl1, full), pltpu.roll(pres, 1, 2))
    slope_z = wu * above_z + wm * pres + wl * below_z
    v2 = v_ref[2] - time_step * idn * slope_z
    v2_lo = vz_lo - time_step * iz_lo * (wu_lo * p_first + wm_lo * zl1 + wl_lo * zl2)
    v2_hi = vz_hi - time_step * iz_hi * (wu_hi * zh2 + wm_hi * zh1 + wl_hi * p_last)

    vo_ref[0] = v0
    vo_ref[1] = v1
    vo_ref[2] = v2
    vxo_ref[0:1] = v0_lo
    vxo_ref[1:2] = v0_hi
    vyo_ref[...] = pair(v1_lo, v1_hi, vyo_ref.shape, 1)

    up_x = jnp.concatenate([v0[1:], v0_hi], axis=0)
    down_x = jnp.concatenate([v0_lo, v0[:-1]], axis=0)
    up_y = jnp.where(yi == Y - 1, jnp.broadcast_to(v1_hi, full), pltpu.roll(v1, Y - 1, 1))
    down_y = jnp.where(yi == 0, jnp.broadcast_to(v1_lo, full), pltpu.roll(v1, 1, 1))
    up_z = jnp.where(zi == Z - 1, jnp.broadcast_to(v2_hi, full), pltpu.roll(v2, Z - 1, 2))
    down_z = jnp.where(zi == 0, jnp.broadcast_to(v2_lo, full), pltpu.roll(v2, 1, 2))
    spread = (
        0.5 * (up_x - down_x)
        + 0.5 * (up_y - down_y)
        + (wu * up_z + wm * v2 + wl * down_z)
    )
    new_p = pres - time_step * bulk_ref[...] * spread
    new_p = jnp.where(zi == 0, new_p + jnp.broadcast_to(src_ref[...], full), new_p)
    po_ref[...] = new_p
    sfo_ref[...] = sfo_ref[...] + 0.5 * (
        scal_ref[base + 8] * pick(new_p, -1, Z - 1) + scal_ref[base + 9] * pick(new_p, -1, 0)
    )

    sxu_ref[...] = new_p[X - 2 :]
    sxd_ref[...] = new_p[0:2]
    syu_ref[...] = new_p[:, Y - rows :]
    syd_ref[...] = new_p[:, 0:rows]
    zshape = szu_ref.shape
    szu_ref[...] = quad(
        (pick(new_p, -1, Z - 2), pick(new_p, -1, Z - 1), pick(v2, -1, Z - 1), pick(idn, -1, Z - 1)), zshape
    )
    szd_ref[...] = quad((pick(new_p, -1, 0), pick(new_p, -1, 1), pick(v2, -1, 0), pick(idn, -1, 0)), zshape)


def run_step(instant, operands, rows):
    pres = operands[2]
    X, Y, Z = pres.shape
    first = instant == 0
    f32 = jnp.float32
    shapes = [
        jax.ShapeDtypeStruct((X, Y, Z), f32),
        jax.ShapeDtypeStruct((3, X, Y, Z), f32),
        jax.ShapeDtypeStruct((X, Y, 1), f32),
        jax.ShapeDtypeStruct((2, Y, Z), f32),
        jax.ShapeDtypeStruct((X, 2, Z), f32),
        jax.ShapeDtypeStruct((2, Y, Z), f32),
        jax.ShapeDtypeStruct((2, Y, Z), f32),
        jax.ShapeDtypeStruct((X, rows, Z), f32),
        jax.ShapeDtypeStruct((X, rows, Z), f32),
        jax.ShapeDtypeStruct((X, Y, 4), f32),
        jax.ShapeDtypeStruct((X, Y, 4), f32),
    ]
    if first:
        shapes += shapes[3:5]
    vmem = pl.BlockSpec(memory_space=pltpu.VMEM)
    in_specs = [pl.BlockSpec(memory_space=pltpu.SMEM)] + [vmem] * (len(operands) - 1)
    in_specs[6] = pl.BlockSpec((None, X, Y, 1), lambda i: (instant, 0, 0, 0))
    cells = X * Y * Z
    return pl.pallas_call(
        functools.partial(step_kernel, instant, first),
        out_shape=tuple(shapes),
        grid=(1,),
        in_specs=in_specs,
        out_specs=[vmem] * len(shapes),
        cost_estimate=pl.CostEstimate(
            flops=80 * cells, transcendentals=0, bytes_accessed=4 * 4 * 12 * cells // 4
        ),
    )(*operands)


def seafloor_sums(seafloor, node_weight, node_patch, patch_slot):
    sea_values = node_weight[0, 0] * seafloor.reshape(-1)
    slots = patch_slot[node_patch[0, 0]]
    owners = lax.axis_size("gx") * lax.axis_size("gy")
    per_owner = patch_slot.shape[0] // owners
    owner_hot = slots[None, :] // per_owner == jnp.arange(owners, dtype=jnp.int32)[:, None]
    within_hot = (
        slots[:, None] % per_owner == jnp.arange(per_owner, dtype=jnp.int32)[None, :]
    ).astype(jnp.float32)
    weighted = jnp.where(owner_hot, sea_values[None, :], 0.0)
    partial_slip = jnp.dot(weighted, within_hot, precision=lax.Precision.HIGHEST).reshape(-1)
    return summed_on_arrival(partial_slip, ("gx", "gy"), 0)


def local(
    pressure,
    velocity,
    inv_density,
    bulk,
    node_weight,
    node_patch,
    patch_slot,
    gauge_x,
    gauge_y,
    gauge_misfit,
):
    X, Y, Z = pressure.shape
    rows = 8
    tiles_z = lax.axis_size("gz")
    depth_index = lax.axis_index("gz")
    first_crust = tiles_z // 2 * Z
    levels = depth_index * Z + jnp.arange(Z, dtype=jnp.int32)
    level_grid = depth_index * Z + lax.broadcasted_iota(jnp.int32, (3, 1, 1, Z), 3)
    w_up, w_mid, w_low = depth_weights(level_grid, first_crust)
    which = lax.broadcasted_iota(jnp.int32, (3, 1, 1, Z), 0)
    wint = jnp.where(which == 0, w_up, jnp.where(which == 1, w_mid, w_low))
    entry = lax.broadcasted_iota(jnp.int32, (ITERS * 16,), 0) % 16
    step_at = lax.broadcasted_iota(jnp.int32, (ITERS * 16,), 0) // 16
    edge_level = depth_index * Z + jnp.where(entry < 3, -1, Z)
    e_up, e_mid, e_low = depth_weights(edge_level, first_crust)
    kind = entry % 3
    edge_value = jnp.where(kind == 0, e_up, jnp.where(kind == 1, e_mid, e_low))
    ocean = depth_index == first_crust // Z - 1
    crust = depth_index == first_crust // Z
    before = step_at < ITERS - 1
    after = step_at == ITERS - 2
    flag_value = jnp.where(
        entry == 6, before & ocean,
        jnp.where(entry == 7, before & crust,
                  jnp.where(entry == 8, after & ocean, after & crust)),
    ).astype(jnp.float32)
    scal_all = jnp.where(entry < 6, edge_value, jnp.where(entry < 10, flag_value, 0.0))
    scal_all = scal_all.astype(jnp.float32)
    top_flag = (depth_index == 0).astype(jnp.float32)
    sources = source_planes(
        gauge_x,
        gauge_y,
        gauge_misfit,
        lax.axis_index("gx") * X,
        lax.axis_index("gy") * Y,
        X,
        Y,
    )
    src_all = (time_step * sources * top_flag)[..., None]

    v0, v1, v2 = velocity[0], velocity[1], velocity[2]
    x_up = jnp.concatenate([pressure[X - 2 :], v0[X - 1 :], inv_density[X - 1 :]], axis=0)
    x_dn = jnp.concatenate([pressure[:2], v0[:1], inv_density[:1]], axis=0)
    y_up = jnp.concatenate(
        [pressure[:, Y - rows :], v1[:, Y - 1 :], inv_density[:, Y - 1 :]], axis=1
    )
    y_dn = jnp.concatenate([pressure[:, :rows], v1[:, :1], inv_density[:, :1]], axis=1)
    z_up = jnp.concatenate(
        [pressure[:, :, Z - 2 :], v2[:, :, Z - 1 :], inv_density[:, :, Z - 1 :]], axis=2
    )
    z_dn = jnp.concatenate([pressure[:, :, :2], v2[:, :, :1], inv_density[:, :, :1]], axis=2)
    halos = (
        shifted_up(x_up, "gx"),
        shifted_down(x_dn, "gx"),
        shifted_up(y_up, "gy"),
        shifted_down(y_dn, "gy"),
        shifted_up(z_up, "gz"),
        shifted_down(z_dn, "gz"),
    )
    common = (scal_all, wint)
    pres, vel = pressure, velocity
    for instant in range(ITERS):
        if instant > 0:
            halos = (
                shifted_up(sends[0], "gx"),
                shifted_down(sends[1], "gx"),
                shifted_up(sends[2], "gy"),
                shifted_down(sends[3], "gy"),
                shifted_up(sends[4], "gz"),
                shifted_down(sends[5], "gz"),
            )
        if instant == 0:
            operands = common + (pres, vel, inv_density, bulk, src_all) + halos
        else:
            operands = common + (pres, vel, inv_density, bulk, src_all, sf) + halos + tracked + media_halo
        outs = run_step(instant, operands, rows)
        pres, vel, sf = outs[0], outs[1], outs[2]
        tracked = outs[3:5]
        sends = outs[5:11]
        if instant == 0:
            media_halo = outs[11:13]
        if instant == ITERS - 2:
            owner_sums = seafloor_sums(sf[:, :, 0], node_weight, node_patch, patch_slot)
    ocean_plane = first_crust // Z - 1
    crust_plane = first_crust // Z
    below, above = ocean_plane - 1, crust_plane + 1
    near = lax.ppermute(owner_sums, "gz", [(ocean_plane, below), (crust_plane, above)])
    far = lax.ppermute(owner_sums, "gz", [(crust_plane, below), (ocean_plane, above)])
    across = lax.ppermute(owner_sums, "gz", [(ocean_plane, crust_plane), (crust_plane, ocean_plane)])
    inner = (depth_index == ocean_plane) | (depth_index == crust_plane)
    owner_sums = jnp.where(inner, owner_sums + across, near + far)
    piece = owner_sums.shape[0] // tiles_z
    slip_grad = lax.dynamic_slice_in_dim(owner_sums, depth_index * piece, piece)
    return (pres, vel, slip_grad)


def solution(mesh):
    placed = (
        P("gx", "gy", "gz"),
        P(None, "gx", "gy", "gz"),
        P("gx", "gy", "gz"),
        P("gx", "gy", "gz"),
        P("gx", "gy", None),
        P("gx", "gy", None),
        P(),
        P(),
        P(),
        P(),
    )
    return jax.shard_map(
        local,
        mesh=mesh,
        in_specs=placed,
        out_specs=(P("gx", "gy", "gz"), P(None, "gx", "gy", "gz"), P(("gx", "gy", "gz"))),
        check_vma=False,
    )
```

```python
import functools

import jax
import jax.numpy as jnp
from jax import lax
from jax.experimental import pallas as pl
from jax.experimental.pallas import tpu as pltpu
from jax.sharding import PartitionSpec as P

ITERS = 4


time_step = 0.5


def shifted_up(x, axis):
    count = lax.axis_size(axis)
    return lax.ppermute(x, axis, [(i, i + 1) for i in range(count - 1)])


def shifted_down(x, axis):
    count = lax.axis_size(axis)
    return lax.ppermute(x, axis, [(i + 1, i) for i in range(count - 1)])


def in_blocks(x, dim, size):
    before, after = (x.shape[:dim], x.shape[dim + 1 :])
    return jnp.moveaxis(x.reshape(*before, size, -1, *after), dim, 0)


def summed_on_arrival(x, axis, dim):
    size = lax.axis_size(axis)
    parts = lax.all_to_all(in_blocks(x, dim, size), axis, 0, 0, tiled=True)
    return jnp.sum(parts, axis=0)


def depth_weights(levels, first_crust):
    ocean_last = levels == first_crust - 1
    crust_first = levels == first_crust
    weight_above = jnp.where(ocean_last, 0.5, jnp.where(crust_first, 1.0, 0.5)).astype(jnp.float32)
    weight_here = jnp.where(ocean_last, 0.5, jnp.where(crust_first, -1.5, 0.0)).astype(jnp.float32)
    weight_below = jnp.where(ocean_last, -1.0, jnp.where(crust_first, 0.5, -0.5)).astype(
        jnp.float32
    )
    return (weight_above, weight_here, weight_below)


def source_planes(gauge_x, gauge_y, gauge_misfit, start_x, start_y, span_x, span_y):
    local_x = gauge_x - start_x
    local_y = gauge_y - start_y
    inside = (local_x >= 0) & (local_x < span_x) & (local_y >= 0) & (local_y < span_y)
    gauge_cell = jnp.where(inside, local_x * span_y + local_y, -1)
    gauge_table = (
        gauge_cell[:, None] == jnp.arange(span_x * span_y, dtype=jnp.int32)[None, :]
    ).astype(jnp.float32)
    return jnp.dot(gauge_misfit, gauge_table, precision=lax.Precision.HIGHEST).reshape(
        gauge_misfit.shape[0], span_x, span_y
    )


def pick(a, axis, index):
    return lax.slice_in_dim(a, index, index + 1, axis=axis % a.ndim)


def pair(lo, hi, shape, axis):
    where = lax.broadcasted_iota(jnp.int32, shape, axis) == 0
    return jnp.where(where, jnp.broadcast_to(lo, shape), jnp.broadcast_to(hi, shape))


def quad(parts, shape):
    lane = lax.broadcasted_iota(jnp.int32, shape, len(shape) - 1)
    out = jnp.broadcast_to(parts[-1], shape)
    for index in range(len(parts) - 2, -1, -1):
        out = jnp.where(lane == index, jnp.broadcast_to(parts[index], shape), out)
    return out


def step_kernel(instant, first, *refs):
    if first:
        (scal_ref, wint_ref, p_ref, v_ref, idn_ref, bulk_ref, src_ref,
         xl_ref, xh_ref, yl_ref, yh_ref, zl_ref, zh_ref) = refs[:13]
        outs = refs[13:]
    else:
        (scal_ref, wint_ref, p_ref, v_ref, idn_ref, bulk_ref, src_ref, sf_ref,
         xl_ref, xh_ref, yl_ref, yh_ref, zl_ref, zh_ref,
         vx_ref, vy_ref, ix_ref, iy_ref) = refs[:18]
        outs = refs[18:]
    (po_ref, vo_ref, sfo_ref, vxo_ref, vyo_ref,
     sxu_ref, sxd_ref, syu_ref, syd_ref, szu_ref, szd_ref) = outs[:11]
    X, Y, Z = p_ref.shape
    rows = syu_ref.shape[1]
    base = instant * 16
    full = (X, Y, Z)
    yi = lax.broadcasted_iota(jnp.int32, full, 1)
    zi = lax.broadcasted_iota(jnp.int32, full, 2)
    wu = wint_ref[0]
    wm = wint_ref[1]
    wl = wint_ref[2]
    wu_lo = scal_ref[base + 0]
    wm_lo = scal_ref[base + 1]
    wl_lo = scal_ref[base + 2]
    wu_hi = scal_ref[base + 3]
    wm_hi = scal_ref[base + 4]
    wl_hi = scal_ref[base + 5]
    f_ocean = scal_ref[base + 6]
    f_crust = scal_ref[base + 7]

    xl = xl_ref[...]
    xh = xh_ref[...]
    yl = yl_ref[...]
    yh = yh_ref[...]
    zl = zl_ref[...]
    zh = zh_ref[...]
    pxl2, pxl1 = xl[0:1], xl[1:2]
    pxh1, pxh2 = xh[0:1], xh[1:2]
    yl2, yl1 = pick(yl, 1, rows - 2), pick(yl, 1, rows - 1)
    yh1, yh2 = pick(yh, 1, 0), pick(yh, 1, 1)
    zl2, zl1 = pick(zl, -1, 0), pick(zl, -1, 1)
    zh1, zh2 = pick(zh, -1, 0), pick(zh, -1, 1)
    vz_lo, vz_hi, iz_lo, iz_hi = pick(zl, -1, 2), pick(zh, -1, 2), pick(zl, -1, 3), pick(zh, -1, 3)
    if first:
        vx_lo, vx_hi, ix_lo, ix_hi = xl[2:3], xh[2:3], xl[3:4], xh[3:4]
        vy_lo, vy_hi = pick(yl, 1, rows), pick(yh, 1, rows)
        iy_lo, iy_hi = pick(yl, 1, rows + 1), pick(yh, 1, rows + 1)
        ixo_ref, iyo_ref = outs[11:13]
        ixo_ref[0:1] = ix_lo
        ixo_ref[1:2] = ix_hi
        iyo_ref[...] = pair(iy_lo, iy_hi, iyo_ref.shape, 1)
    else:
        vx = vx_ref[...]
        ix = ix_ref[...]
        vy = vy_ref[...]
        iy = iy_ref[...]
        vx_lo, vx_hi, ix_lo, ix_hi = vx[0:1], vx[1:2], ix[0:1], ix[1:2]
        vy_lo, vy_hi = pick(vy, 1, 0), pick(vy, 1, 1)
        iy_lo, iy_hi = pick(iy, 1, 0), pick(iy, 1, 1)

    pres = p_ref[...]
    idn = idn_ref[...]

    p_first = pick(pres, -1, 0)
    p_last = pick(pres, -1, Z - 1)
    sea = 0.5 * (f_ocean * (p_last + zh1) + f_crust * (zl1 + p_first))
    sfo_ref[...] = sea if first else sf_ref[...] + sea

    above_x = jnp.concatenate([pres[1:], pxh1], axis=0)
    below_x = jnp.concatenate([pxl1, pres[:-1]], axis=0)
    slope_x = 0.5 * (above_x - below_x)
    v0 = v_ref[0] - time_step * idn * slope_x
    v0_lo = vx_lo - time_step * ix_lo * (0.5 * (pres[0:1] - pxl2))
    v0_hi = vx_hi - time_step * ix_hi * (0.5 * (pxh2 - pres[X - 1 : X]))

    p_y0 = pick(pres, 1, 0)
    p_yl = pick(pres, 1, Y - 1)
    above_y = jnp.where(yi == Y - 1, jnp.broadcast_to(yh1, full), pltpu.roll(pres, Y - 1, 1))
    below_y = jnp.where(yi == 0, jnp.broadcast_to(yl1, full), pltpu.roll(pres, 1, 1))
    slope_y = 0.5 * (above_y - below_y)
    v1 = v_ref[1] - time_step * idn * slope_y
    v1_lo = vy_lo - time_step * iy_lo * (0.5 * (p_y0 - yl2))
    v1_hi = vy_hi - time_step * iy_hi * (0.5 * (yh2 - p_yl))

    above_z = jnp.where(zi == Z - 1, jnp.broadcast_to(zh1, full), pltpu.roll(pres, Z - 1, 2))
    below_z = jnp.where(zi == 0, jnp.broadcast_to(zl1, full), pltpu.roll(pres, 1, 2))
    slope_z = wu * above_z + wm * pres + wl * below_z
    v2 = v_ref[2] - time_step * idn * slope_z
    v2_lo = vz_lo - time_step * iz_lo * (wu_lo * p_first + wm_lo * zl1 + wl_lo * zl2)
    v2_hi = vz_hi - time_step * iz_hi * (wu_hi * zh2 + wm_hi * zh1 + wl_hi * p_last)

    vo_ref[0] = v0
    vo_ref[1] = v1
    vo_ref[2] = v2
    vxo_ref[0:1] = v0_lo
    vxo_ref[1:2] = v0_hi
    vyo_ref[...] = pair(v1_lo, v1_hi, vyo_ref.shape, 1)

    up_x = jnp.concatenate([v0[1:], v0_hi], axis=0)
    down_x = jnp.concatenate([v0_lo, v0[:-1]], axis=0)
    up_y = jnp.where(yi == Y - 1, jnp.broadcast_to(v1_hi, full), pltpu.roll(v1, Y - 1, 1))
    down_y = jnp.where(yi == 0, jnp.broadcast_to(v1_lo, full), pltpu.roll(v1, 1, 1))
    up_z = jnp.where(zi == Z - 1, jnp.broadcast_to(v2_hi, full), pltpu.roll(v2, Z - 1, 2))
    down_z = jnp.where(zi == 0, jnp.broadcast_to(v2_lo, full), pltpu.roll(v2, 1, 2))
    spread = (
        0.5 * (up_x - down_x)
        + 0.5 * (up_y - down_y)
        + (wu * up_z + wm * v2 + wl * down_z)
    )
    new_p = pres - time_step * bulk_ref[...] * spread
    new_p = jnp.where(zi == 0, new_p + jnp.broadcast_to(src_ref[...], full), new_p)
    po_ref[...] = new_p

    sxu_ref[...] = new_p[X - 2 :]
    sxd_ref[...] = new_p[0:2]
    syu_ref[...] = new_p[:, Y - rows :]
    syd_ref[...] = new_p[:, 0:rows]
    zshape = szu_ref.shape
    szu_ref[...] = quad(
        (pick(new_p, -1, Z - 2), pick(new_p, -1, Z - 1), pick(v2, -1, Z - 1), pick(idn, -1, Z - 1)), zshape
    )
    szd_ref[...] = quad((pick(new_p, -1, 0), pick(new_p, -1, 1), pick(v2, -1, 0), pick(idn, -1, 0)), zshape)


def run_step(instant, operands, rows):
    pres = operands[2]
    X, Y, Z = pres.shape
    first = instant == 0
    f32 = jnp.float32
    shapes = [
        jax.ShapeDtypeStruct((X, Y, Z), f32),
        jax.ShapeDtypeStruct((3, X, Y, Z), f32),
        jax.ShapeDtypeStruct((X, Y, 1), f32),
        jax.ShapeDtypeStruct((2, Y, Z), f32),
        jax.ShapeDtypeStruct((X, 2, Z), f32),
        jax.ShapeDtypeStruct((2, Y, Z), f32),
        jax.ShapeDtypeStruct((2, Y, Z), f32),
        jax.ShapeDtypeStruct((X, rows, Z), f32),
        jax.ShapeDtypeStruct((X, rows, Z), f32),
        jax.ShapeDtypeStruct((X, Y, 4), f32),
        jax.ShapeDtypeStruct((X, Y, 4), f32),
    ]
    if first:
        shapes += shapes[3:5]
    vmem = pl.BlockSpec(memory_space=pltpu.VMEM)
    in_specs = [pl.BlockSpec(memory_space=pltpu.SMEM)] + [vmem] * (len(operands) - 1)
    in_specs[6] = pl.BlockSpec((None, X, Y, 1), lambda i: (instant, 0, 0, 0))
    cells = X * Y * Z
    return pl.pallas_call(
        functools.partial(step_kernel, instant, first),
        out_shape=tuple(shapes),
        grid=(1,),
        in_specs=in_specs,
        out_specs=[vmem] * len(shapes),
        cost_estimate=pl.CostEstimate(
            flops=80 * cells, transcendentals=0, bytes_accessed=4 * 4 * 12 * cells // 4
        ),
    )(*operands)


def seafloor_sums(seafloor, node_weight, node_patch, patch_slot):
    sea_values = node_weight[0, 0] * seafloor.reshape(-1)
    slots = patch_slot[node_patch[0, 0]]
    owners = lax.axis_size("gx") * lax.axis_size("gy")
    per_owner = patch_slot.shape[0] // owners
    owner_hot = slots[None, :] // per_owner == jnp.arange(owners, dtype=jnp.int32)[:, None]
    within_hot = (
        slots[:, None] % per_owner == jnp.arange(per_owner, dtype=jnp.int32)[None, :]
    ).astype(jnp.float32)
    weighted = jnp.where(owner_hot, sea_values[None, :], 0.0)
    partial_slip = jnp.dot(weighted, within_hot, precision=lax.Precision.HIGHEST).reshape(-1)
    return summed_on_arrival(partial_slip, ("gx", "gy"), 0)


def local(
    pressure,
    velocity,
    inv_density,
    bulk,
    node_weight,
    node_patch,
    patch_slot,
    gauge_x,
    gauge_y,
    gauge_misfit,
):
    X, Y, Z = pressure.shape
    rows = 8
    tiles_z = lax.axis_size("gz")
    depth_index = lax.axis_index("gz")
    first_crust = tiles_z // 2 * Z
    levels = depth_index * Z + jnp.arange(Z, dtype=jnp.int32)
    level_grid = depth_index * Z + lax.broadcasted_iota(jnp.int32, (3, 1, 1, Z), 3)
    w_up, w_mid, w_low = depth_weights(level_grid, first_crust)
    which = lax.broadcasted_iota(jnp.int32, (3, 1, 1, Z), 0)
    wint = jnp.where(which == 0, w_up, jnp.where(which == 1, w_mid, w_low))
    entry = lax.broadcasted_iota(jnp.int32, (ITERS * 16,), 0) % 16
    step_at = lax.broadcasted_iota(jnp.int32, (ITERS * 16,), 0) // 16
    edge_level = depth_index * Z + jnp.where(entry < 3, -1, Z)
    e_up, e_mid, e_low = depth_weights(edge_level, first_crust)
    kind = entry % 3
    edge_value = jnp.where(kind == 0, e_up, jnp.where(kind == 1, e_mid, e_low))
    ocean = depth_index == first_crust // Z - 1
    crust = depth_index == first_crust // Z
    before = step_at < ITERS - 1
    after = step_at < 0
    flag_value = jnp.where(
        entry == 6, before & ocean,
        jnp.where(entry == 7, before & crust,
                  jnp.where(entry == 8, after & ocean, after & crust)),
    ).astype(jnp.float32)
    scal_all = jnp.where(entry < 6, edge_value, jnp.where(entry < 10, flag_value, 0.0))
    scal_all = scal_all.astype(jnp.float32)
    top_flag = (depth_index == 0).astype(jnp.float32)
    sources = source_planes(
        gauge_x,
        gauge_y,
        gauge_misfit,
        lax.axis_index("gx") * X,
        lax.axis_index("gy") * Y,
        X,
        Y,
    )
    src_all = (time_step * sources * top_flag)[..., None]

    v0, v1, v2 = velocity[0], velocity[1], velocity[2]
    x_up = jnp.concatenate([pressure[X - 2 :], v0[X - 1 :], inv_density[X - 1 :]], axis=0)
    x_dn = jnp.concatenate([pressure[:2], v0[:1], inv_density[:1]], axis=0)
    y_up = jnp.concatenate(
        [pressure[:, Y - rows :], v1[:, Y - 1 :], inv_density[:, Y - 1 :]], axis=1
    )
    y_dn = jnp.concatenate([pressure[:, :rows], v1[:, :1], inv_density[:, :1]], axis=1)
    z_up = jnp.concatenate(
        [pressure[:, :, Z - 2 :], v2[:, :, Z - 1 :], inv_density[:, :, Z - 1 :]], axis=2
    )
    z_dn = jnp.concatenate([pressure[:, :, :2], v2[:, :, :1], inv_density[:, :, :1]], axis=2)
    halos = (
        shifted_up(x_up, "gx"),
        shifted_down(x_dn, "gx"),
        shifted_up(y_up, "gy"),
        shifted_down(y_dn, "gy"),
        shifted_up(z_up, "gz"),
        shifted_down(z_dn, "gz"),
    )
    common = (scal_all, wint)
    pres, vel = pressure, velocity
    for instant in range(ITERS):
        if instant > 0:
            halos = (
                shifted_up(sends[0], "gx"),
                shifted_down(sends[1], "gx"),
                shifted_up(sends[2], "gy"),
                shifted_down(sends[3], "gy"),
                shifted_up(sends[4], "gz"),
                shifted_down(sends[5], "gz"),
            )
        if instant == ITERS - 1:
            ocean = (depth_index == first_crust // Z - 1).astype(jnp.float32)
            crust = (depth_index == first_crust // Z).astype(jnp.float32)
            sf_last = sf + 0.5 * (
                ocean * (sends[4][:, :, 1:2] + halos[5][:, :, 0:1])
                + crust * (halos[4][:, :, 1:2] + sends[5][:, :, 0:1])
            )
            owner_sums = seafloor_sums(sf_last[:, :, 0], node_weight, node_patch, patch_slot)
        if instant == 0:
            operands = common + (pres, vel, inv_density, bulk, src_all) + halos
        else:
            operands = common + (pres, vel, inv_density, bulk, src_all, sf) + halos + tracked + media_halo
        outs = run_step(instant, operands, rows)
        pres, vel, sf = outs[0], outs[1], outs[2]
        tracked = outs[3:5]
        sends = outs[5:11]
        if instant == 0:
            media_halo = outs[11:13]
    owner_sums = owner_sums + 0.0 * pres[0, 0, 0]
    ocean_plane = first_crust // Z - 1
    crust_plane = first_crust // Z
    spread_out = lax.ppermute(
        owner_sums, "gz", [(ocean_plane, ocean_plane - 1), (crust_plane, crust_plane + 1)]
    )
    inner = (depth_index == ocean_plane) | (depth_index == crust_plane)
    owner_sums = jnp.where(inner, owner_sums, spread_out)
    piece = owner_sums.shape[0] // tiles_z
    slip_grad = lax.dynamic_slice_in_dim(owner_sums, depth_index * piece, piece)
    return (pres, vel, slip_grad)


def solution(mesh):
    placed = (
        P("gx", "gy", "gz"),
        P(None, "gx", "gy", "gz"),
        P("gx", "gy", "gz"),
        P("gx", "gy", "gz"),
        P("gx", "gy", None),
        P("gx", "gy", None),
        P(),
        P(),
        P(),
        P(),
    )
    return jax.shard_map(
        local,
        mesh=mesh,
        in_specs=placed,
        out_specs=(P("gx", "gy", "gz"), P(None, "gx", "gy", "gz"), P(("gx", "gy", "gz"))),
        check_vma=False,
    )
```

```python
import functools

import jax
import jax.numpy as jnp
from jax import lax
from jax.experimental import pallas as pl
from jax.experimental.pallas import tpu as pltpu
from jax.sharding import PartitionSpec as P

ITERS = 4


time_step = 0.5


def shifted_up(x, axis):
    count = lax.axis_size(axis)
    return lax.ppermute(x, axis, [(i, i + 1) for i in range(count - 1)])


def shifted_down(x, axis):
    count = lax.axis_size(axis)
    return lax.ppermute(x, axis, [(i + 1, i) for i in range(count - 1)])


def in_blocks(x, dim, size):
    before, after = (x.shape[:dim], x.shape[dim + 1 :])
    return jnp.moveaxis(x.reshape(*before, size, -1, *after), dim, 0)


def summed_on_arrival(x, axis, dim):
    size = lax.axis_size(axis)
    parts = lax.all_to_all(in_blocks(x, dim, size), axis, 0, 0, tiled=True)
    return jnp.sum(parts, axis=0)


def depth_weights(levels, first_crust):
    ocean_last = levels == first_crust - 1
    crust_first = levels == first_crust
    weight_above = jnp.where(ocean_last, 0.5, jnp.where(crust_first, 1.0, 0.5)).astype(jnp.float32)
    weight_here = jnp.where(ocean_last, 0.5, jnp.where(crust_first, -1.5, 0.0)).astype(jnp.float32)
    weight_below = jnp.where(ocean_last, -1.0, jnp.where(crust_first, 0.5, -0.5)).astype(
        jnp.float32
    )
    return (weight_above, weight_here, weight_below)


def source_planes(gauge_x, gauge_y, gauge_misfit, start_x, start_y, span_x, span_y):
    local_x = gauge_x - start_x
    local_y = gauge_y - start_y
    inside = (local_x >= 0) & (local_x < span_x) & (local_y >= 0) & (local_y < span_y)
    gauge_cell = jnp.where(inside, local_x * span_y + local_y, -1)
    gauge_table = (
        gauge_cell[:, None] == jnp.arange(span_x * span_y, dtype=jnp.int32)[None, :]
    ).astype(jnp.float32)
    return jnp.dot(gauge_misfit, gauge_table, precision=lax.Precision.HIGHEST).reshape(
        gauge_misfit.shape[0], span_x, span_y
    )


def pick(a, axis, index):
    return lax.slice_in_dim(a, index, index + 1, axis=axis % a.ndim)


def pair(lo, hi, shape, axis):
    where = lax.broadcasted_iota(jnp.int32, shape, axis) == 0
    return jnp.where(where, jnp.broadcast_to(lo, shape), jnp.broadcast_to(hi, shape))


def step_kernel(instant, first, *refs):
    if first:
        (scal_ref, wint_ref, p_ref, v_ref, idn_ref, bulk_ref, src_ref,
         xl_ref, xh_ref, yl_ref, yh_ref, zl_ref, zh_ref) = refs[:13]
        outs = refs[13:]
    else:
        (scal_ref, wint_ref, p_ref, v_ref, idn_ref, bulk_ref, src_ref, sf_ref,
         xl_ref, xh_ref, yl_ref, yh_ref, zl_ref, zh_ref,
         vx_ref, vy_ref, vz_ref, ix_ref, iy_ref, iz_ref) = refs[:20]
        outs = refs[20:]
    (po_ref, vo_ref, sfo_ref, vxo_ref, vyo_ref, vzo_ref,
     sxu_ref, sxd_ref, syu_ref, syd_ref, szu_ref, szd_ref) = outs[:12]
    X, Y, Z = p_ref.shape
    rows = syu_ref.shape[1]
    base = instant * 16
    full = (X, Y, Z)
    yi = lax.broadcasted_iota(jnp.int32, full, 1)
    zi = lax.broadcasted_iota(jnp.int32, full, 2)
    wu = wint_ref[0]
    wm = wint_ref[1]
    wl = wint_ref[2]
    wu_lo = scal_ref[base + 0]
    wm_lo = scal_ref[base + 1]
    wl_lo = scal_ref[base + 2]
    wu_hi = scal_ref[base + 3]
    wm_hi = scal_ref[base + 4]
    wl_hi = scal_ref[base + 5]
    f_ocean = scal_ref[base + 6]
    f_crust = scal_ref[base + 7]

    xl = xl_ref[...]
    xh = xh_ref[...]
    yl = yl_ref[...]
    yh = yh_ref[...]
    zl = zl_ref[...]
    zh = zh_ref[...]
    pxl2, pxl1 = xl[0:1], xl[1:2]
    pxh1, pxh2 = xh[0:1], xh[1:2]
    yl2, yl1 = pick(yl, 1, rows - 2), pick(yl, 1, rows - 1)
    yh1, yh2 = pick(yh, 1, 0), pick(yh, 1, 1)
    zl2, zl1 = pick(zl, -1, 0), pick(zl, -1, 1)
    zh1, zh2 = pick(zh, -1, 0), pick(zh, -1, 1)
    if first:
        vx_lo, vx_hi, ix_lo, ix_hi = xl[2:3], xh[2:3], xl[3:4], xh[3:4]
        vy_lo, vy_hi = pick(yl, 1, rows), pick(yh, 1, rows)
        iy_lo, iy_hi = pick(yl, 1, rows + 1), pick(yh, 1, rows + 1)
        vz_lo, vz_hi, iz_lo, iz_hi = pick(zl, -1, 2), pick(zh, -1, 2), pick(zl, -1, 3), pick(zh, -1, 3)
        ixo_ref, iyo_ref, izo_ref = outs[12:15]
        ixo_ref[0:1] = ix_lo
        ixo_ref[1:2] = ix_hi
        iyo_ref[...] = pair(iy_lo, iy_hi, iyo_ref.shape, 1)
        izo_ref[...] = pair(iz_lo, iz_hi, izo_ref.shape, 2)
    else:
        vx = vx_ref[...]
        ix = ix_ref[...]
        vy = vy_ref[...]
        iy = iy_ref[...]
        vz = vz_ref[...]
        iz = iz_ref[...]
        vx_lo, vx_hi, ix_lo, ix_hi = vx[0:1], vx[1:2], ix[0:1], ix[1:2]
        vy_lo, vy_hi = pick(vy, 1, 0), pick(vy, 1, 1)
        iy_lo, iy_hi = pick(iy, 1, 0), pick(iy, 1, 1)
        vz_lo, vz_hi, iz_lo, iz_hi = pick(vz, -1, 0), pick(vz, -1, 1), pick(iz, -1, 0), pick(iz, -1, 1)

    pres = p_ref[...]
    idn = idn_ref[...]

    p_first = pick(pres, -1, 0)
    p_last = pick(pres, -1, Z - 1)
    sea = 0.5 * (f_ocean * (p_last + zh1) + f_crust * (zl1 + p_first))
    sfo_ref[...] = sea if first else sf_ref[...] + sea

    above_x = jnp.concatenate([pres[1:], pxh1], axis=0)
    below_x = jnp.concatenate([pxl1, pres[:-1]], axis=0)
    slope_x = 0.5 * (above_x - below_x)
    v0 = v_ref[0] - time_step * idn * slope_x
    v0_lo = vx_lo - time_step * ix_lo * (0.5 * (pres[0:1] - pxl2))
    v0_hi = vx_hi - time_step * ix_hi * (0.5 * (pxh2 - pres[X - 1 : X]))

    p_y0 = pick(pres, 1, 0)
    p_yl = pick(pres, 1, Y - 1)
    above_y = jnp.where(yi == Y - 1, jnp.broadcast_to(yh1, full), pltpu.roll(pres, Y - 1, 1))
    below_y = jnp.where(yi == 0, jnp.broadcast_to(yl1, full), pltpu.roll(pres, 1, 1))
    slope_y = 0.5 * (above_y - below_y)
    v1 = v_ref[1] - time_step * idn * slope_y
    v1_lo = vy_lo - time_step * iy_lo * (0.5 * (p_y0 - yl2))
    v1_hi = vy_hi - time_step * iy_hi * (0.5 * (yh2 - p_yl))

    above_z = jnp.where(zi == Z - 1, jnp.broadcast_to(zh1, full), pltpu.roll(pres, Z - 1, 2))
    below_z = jnp.where(zi == 0, jnp.broadcast_to(zl1, full), pltpu.roll(pres, 1, 2))
    slope_z = wu * above_z + wm * pres + wl * below_z
    v2 = v_ref[2] - time_step * idn * slope_z
    v2_lo = vz_lo - time_step * iz_lo * (wu_lo * p_first + wm_lo * zl1 + wl_lo * zl2)
    v2_hi = vz_hi - time_step * iz_hi * (wu_hi * zh2 + wm_hi * zh1 + wl_hi * p_last)

    vo_ref[0] = v0
    vo_ref[1] = v1
    vo_ref[2] = v2
    vxo_ref[0:1] = v0_lo
    vxo_ref[1:2] = v0_hi
    vyo_ref[...] = pair(v1_lo, v1_hi, vyo_ref.shape, 1)
    vzo_ref[...] = pair(v2_lo, v2_hi, vzo_ref.shape, 2)

    up_x = jnp.concatenate([v0[1:], v0_hi], axis=0)
    down_x = jnp.concatenate([v0_lo, v0[:-1]], axis=0)
    up_y = jnp.where(yi == Y - 1, jnp.broadcast_to(v1_hi, full), pltpu.roll(v1, Y - 1, 1))
    down_y = jnp.where(yi == 0, jnp.broadcast_to(v1_lo, full), pltpu.roll(v1, 1, 1))
    up_z = jnp.where(zi == Z - 1, jnp.broadcast_to(v2_hi, full), pltpu.roll(v2, Z - 1, 2))
    down_z = jnp.where(zi == 0, jnp.broadcast_to(v2_lo, full), pltpu.roll(v2, 1, 2))
    spread = (
        0.5 * (up_x - down_x)
        + 0.5 * (up_y - down_y)
        + (wu * up_z + wm * v2 + wl * down_z)
    )
    new_p = pres - time_step * bulk_ref[...] * spread
    new_p = jnp.where(zi == 0, new_p + jnp.broadcast_to(src_ref[instant], full), new_p)
    po_ref[...] = new_p

    sxu_ref[...] = new_p[X - 2 :]
    sxd_ref[...] = new_p[0:2]
    syu_ref[...] = new_p[:, Y - rows :]
    syd_ref[...] = new_p[:, 0:rows]
    zshape = szu_ref.shape
    szu_ref[...] = pair(pick(new_p, -1, Z - 2), pick(new_p, -1, Z - 1), zshape, 2)
    szd_ref[...] = pair(pick(new_p, -1, 0), pick(new_p, -1, 1), zshape, 2)


def run_step(instant, operands, rows):
    pres = operands[2]
    X, Y, Z = pres.shape
    first = instant == 0
    f32 = jnp.float32
    shapes = [
        jax.ShapeDtypeStruct((X, Y, Z), f32),
        jax.ShapeDtypeStruct((3, X, Y, Z), f32),
        jax.ShapeDtypeStruct((X, Y, 1), f32),
        jax.ShapeDtypeStruct((2, Y, Z), f32),
        jax.ShapeDtypeStruct((X, 2, Z), f32),
        jax.ShapeDtypeStruct((X, Y, 2), f32),
        jax.ShapeDtypeStruct((2, Y, Z), f32),
        jax.ShapeDtypeStruct((2, Y, Z), f32),
        jax.ShapeDtypeStruct((X, rows, Z), f32),
        jax.ShapeDtypeStruct((X, rows, Z), f32),
        jax.ShapeDtypeStruct((X, Y, 2), f32),
        jax.ShapeDtypeStruct((X, Y, 2), f32),
    ]
    if first:
        shapes += shapes[3:6]
    vmem = pl.BlockSpec(memory_space=pltpu.VMEM)
    in_specs = [pl.BlockSpec(memory_space=pltpu.SMEM)] + [vmem] * (len(operands) - 1)
    cells = X * Y * Z
    return pl.pallas_call(
        functools.partial(step_kernel, instant, first),
        out_shape=tuple(shapes),
        in_specs=in_specs,
        out_specs=[vmem] * len(shapes),
        cost_estimate=pl.CostEstimate(
            flops=80 * cells, transcendentals=0, bytes_accessed=4 * 4 * 12 * cells // 4
        ),
    )(*operands)


def seafloor_sums(seafloor, node_weight, node_patch, patch_slot):
    sea_values = node_weight[0, 0] * seafloor.reshape(-1)
    slots = patch_slot[node_patch[0, 0]]
    owners = lax.axis_size("gx") * lax.axis_size("gy")
    per_owner = patch_slot.shape[0] // owners
    owner_hot = slots[None, :] // per_owner == jnp.arange(owners, dtype=jnp.int32)[:, None]
    within_hot = (
        slots[:, None] % per_owner == jnp.arange(per_owner, dtype=jnp.int32)[None, :]
    ).astype(jnp.float32)
    weighted = jnp.where(owner_hot, sea_values[None, :], 0.0)
    partial_slip = jnp.dot(weighted, within_hot, precision=lax.Precision.HIGHEST).reshape(-1)
    return summed_on_arrival(partial_slip, ("gx", "gy", "gz"), 0)


def local(
    pressure,
    velocity,
    inv_density,
    bulk,
    node_weight,
    node_patch,
    patch_slot,
    gauge_x,
    gauge_y,
    gauge_misfit,
):
    X, Y, Z = pressure.shape
    rows = 8
    tiles_z = lax.axis_size("gz")
    depth_index = lax.axis_index("gz")
    first_crust = tiles_z // 2 * Z
    levels = depth_index * Z + jnp.arange(Z, dtype=jnp.int32)
    level_grid = depth_index * Z + lax.broadcasted_iota(jnp.int32, (3, 1, 1, Z), 3)
    w_up, w_mid, w_low = depth_weights(level_grid, first_crust)
    which = lax.broadcasted_iota(jnp.int32, (3, 1, 1, Z), 0)
    wint = jnp.where(which == 0, w_up, jnp.where(which == 1, w_mid, w_low))
    entry = lax.broadcasted_iota(jnp.int32, (ITERS * 16,), 0) % 16
    step_at = lax.broadcasted_iota(jnp.int32, (ITERS * 16,), 0) // 16
    edge_level = depth_index * Z + jnp.where(entry < 3, -1, Z)
    e_up, e_mid, e_low = depth_weights(edge_level, first_crust)
    kind = entry % 3
    edge_value = jnp.where(kind == 0, e_up, jnp.where(kind == 1, e_mid, e_low))
    ocean = depth_index == first_crust // Z - 1
    crust = depth_index == first_crust // Z
    before = step_at < ITERS - 1
    after = step_at < 0
    flag_value = jnp.where(
        entry == 6, before & ocean,
        jnp.where(entry == 7, before & crust,
                  jnp.where(entry == 8, after & ocean, after & crust)),
    ).astype(jnp.float32)
    scal_all = jnp.where(entry < 6, edge_value, jnp.where(entry < 10, flag_value, 0.0))
    scal_all = scal_all.astype(jnp.float32)
    top_flag = (depth_index == 0).astype(jnp.float32)
    sources = source_planes(
        gauge_x,
        gauge_y,
        gauge_misfit,
        lax.axis_index("gx") * X,
        lax.axis_index("gy") * Y,
        X,
        Y,
    )
    src_all = (time_step * sources * top_flag)[..., None]

    v0, v1, v2 = velocity[0], velocity[1], velocity[2]
    x_up = jnp.concatenate([pressure[X - 2 :], v0[X - 1 :], inv_density[X - 1 :]], axis=0)
    x_dn = jnp.concatenate([pressure[:2], v0[:1], inv_density[:1]], axis=0)
    y_up = jnp.concatenate(
        [pressure[:, Y - rows :], v1[:, Y - 1 :], inv_density[:, Y - 1 :]], axis=1
    )
    y_dn = jnp.concatenate([pressure[:, :rows], v1[:, :1], inv_density[:, :1]], axis=1)
    z_up = jnp.concatenate(
        [pressure[:, :, Z - 2 :], v2[:, :, Z - 1 :], inv_density[:, :, Z - 1 :]], axis=2
    )
    z_dn = jnp.concatenate([pressure[:, :, :2], v2[:, :, :1], inv_density[:, :, :1]], axis=2)
    halos = (
        shifted_up(x_up, "gx"),
        shifted_down(x_dn, "gx"),
        shifted_up(y_up, "gy"),
        shifted_down(y_dn, "gy"),
        shifted_up(z_up, "gz"),
        shifted_down(z_dn, "gz"),
    )
    common = (scal_all, wint)
    pres, vel = pressure, velocity
    for instant in range(ITERS):
        if instant > 0:
            halos = (
                shifted_up(sends[0], "gx"),
                shifted_down(sends[1], "gx"),
                shifted_up(sends[2], "gy"),
                shifted_down(sends[3], "gy"),
                shifted_up(sends[4], "gz"),
                shifted_down(sends[5], "gz"),
            )
        if instant == ITERS - 1:
            ocean = (depth_index == first_crust // Z - 1).astype(jnp.float32)
            crust = (depth_index == first_crust // Z).astype(jnp.float32)
            sf_last = sf + 0.5 * (
                ocean * (sends[4][:, :, 1:2] + halos[5][:, :, 0:1])
                + crust * (halos[4][:, :, 1:2] + sends[5][:, :, 0:1])
            )
            sf_last = jnp.where(depth_index == first_crust // Z, sf_last, 0.0)
            slip_grad = seafloor_sums(sf_last[:, :, 0], node_weight, node_patch, patch_slot)
        if instant == 0:
            operands = common + (pres, vel, inv_density, bulk, src_all) + halos
        else:
            operands = common + (pres, vel, inv_density, bulk, src_all, sf) + halos + tracked + media_halo
        outs = run_step(instant, operands, rows)
        pres, vel, sf = outs[0], outs[1], outs[2]
        tracked = outs[3:6]
        sends = outs[6:12]
        if instant == 0:
            media_halo = outs[12:15]
    return (pres, vel, slip_grad)


def solution(mesh):
    placed = (
        P("gx", "gy", "gz"),
        P(None, "gx", "gy", "gz"),
        P("gx", "gy", "gz"),
        P("gx", "gy", "gz"),
        P("gx", "gy", None),
        P("gx", "gy", None),
        P(),
        P(),
        P(),
        P(),
    )
    return jax.shard_map(
        local,
        mesh=mesh,
        in_specs=placed,
        out_specs=(P("gx", "gy", "gz"), P(None, "gx", "gy", "gz"), P(("gx", "gy", "gz"))),
        check_vma=False,
    )
```

```python
import functools

import jax
import jax.numpy as jnp
from jax import lax
from jax.experimental import pallas as pl
from jax.experimental.pallas import tpu as pltpu
from jax.sharding import PartitionSpec as P

ITERS = 4


time_step = 0.5


def shifted_up(x, axis):
    count = lax.axis_size(axis)
    return lax.ppermute(x, axis, [(i, i + 1) for i in range(count - 1)])


def shifted_down(x, axis):
    count = lax.axis_size(axis)
    return lax.ppermute(x, axis, [(i + 1, i) for i in range(count - 1)])


def in_blocks(x, dim, size):
    before, after = (x.shape[:dim], x.shape[dim + 1 :])
    return jnp.moveaxis(x.reshape(*before, size, -1, *after), dim, 0)


def summed_on_arrival(x, axis, dim):
    size = lax.axis_size(axis)
    parts = lax.all_to_all(in_blocks(x, dim, size), axis, 0, 0, tiled=True)
    return jnp.sum(parts, axis=0)


def depth_weights(levels, first_crust):
    ocean_last = levels == first_crust - 1
    crust_first = levels == first_crust
    weight_above = jnp.where(ocean_last, 0.5, jnp.where(crust_first, 1.0, 0.5)).astype(jnp.float32)
    weight_here = jnp.where(ocean_last, 0.5, jnp.where(crust_first, -1.5, 0.0)).astype(jnp.float32)
    weight_below = jnp.where(ocean_last, -1.0, jnp.where(crust_first, 0.5, -0.5)).astype(
        jnp.float32
    )
    return (weight_above, weight_here, weight_below)


def source_planes(gauge_x, gauge_y, gauge_misfit, start_x, start_y, span_x, span_y):
    local_x = gauge_x - start_x
    local_y = gauge_y - start_y
    inside = (local_x >= 0) & (local_x < span_x) & (local_y >= 0) & (local_y < span_y)
    gauge_cell = jnp.where(inside, local_x * span_y + local_y, -1)
    gauge_table = (
        gauge_cell[:, None] == jnp.arange(span_x * span_y, dtype=jnp.int32)[None, :]
    ).astype(jnp.float32)
    return jnp.dot(gauge_misfit, gauge_table, precision=lax.Precision.HIGHEST).reshape(
        gauge_misfit.shape[0], span_x, span_y
    )


def pick(a, axis, index):
    return lax.slice_in_dim(a, index, index + 1, axis=axis % a.ndim)


def pair(lo, hi, shape, axis):
    where = lax.broadcasted_iota(jnp.int32, shape, axis) == 0
    return jnp.where(where, jnp.broadcast_to(lo, shape), jnp.broadcast_to(hi, shape))


def step_kernel(instant, first, *refs):
    if first:
        (scal_ref, wint_ref, p_ref, v_ref, idn_ref, bulk_ref, src_ref,
         xl_ref, xh_ref, yl_ref, yh_ref, zl_ref, zh_ref) = refs[:13]
        outs = refs[13:]
    else:
        (scal_ref, wint_ref, p_ref, v_ref, idn_ref, bulk_ref, src_ref, sf_ref,
         xl_ref, xh_ref, yl_ref, yh_ref, zl_ref, zh_ref,
         vx_ref, vy_ref, vz_ref, ix_ref, iy_ref, iz_ref) = refs[:20]
        outs = refs[20:]
    (po_ref, vo_ref, sfo_ref, vxo_ref, vyo_ref, vzo_ref,
     sxu_ref, sxd_ref, syu_ref, syd_ref, szu_ref, szd_ref) = outs[:12]
    X, Y, Z = p_ref.shape
    rows = syu_ref.shape[1]
    base = instant * 16
    full = (X, Y, Z)
    yi = lax.broadcasted_iota(jnp.int32, full, 1)
    zi = lax.broadcasted_iota(jnp.int32, full, 2)
    wu = wint_ref[0]
    wm = wint_ref[1]
    wl = wint_ref[2]
    wu_lo = scal_ref[base + 0]
    wm_lo = scal_ref[base + 1]
    wl_lo = scal_ref[base + 2]
    wu_hi = scal_ref[base + 3]
    wm_hi = scal_ref[base + 4]
    wl_hi = scal_ref[base + 5]
    f_ocean = scal_ref[base + 6]
    f_crust = scal_ref[base + 7]

    xl = xl_ref[...]
    xh = xh_ref[...]
    yl = yl_ref[...]
    yh = yh_ref[...]
    zl = zl_ref[...]
    zh = zh_ref[...]
    pxl2, pxl1 = (xl[0:1], xl[1:2]) if first else (xl[-2:-1], xl[-1:])
    pxh1, pxh2 = xh[0:1], xh[1:2]
    yl2, yl1 = pick(yl, 1, rows - 2), pick(yl, 1, rows - 1)
    yh1, yh2 = pick(yh, 1, 0), pick(yh, 1, 1)
    zl2, zl1 = pick(zl, -1, 0), pick(zl, -1, 1)
    zh1, zh2 = pick(zh, -1, 0), pick(zh, -1, 1)
    if first:
        vx_lo, vx_hi, ix_lo, ix_hi = xl[2:3], xh[2:3], xl[3:4], xh[3:4]
        vy_lo, vy_hi = pick(yl, 1, rows), pick(yh, 1, rows)
        iy_lo, iy_hi = pick(yl, 1, rows + 1), pick(yh, 1, rows + 1)
        vz_lo, vz_hi, iz_lo, iz_hi = pick(zl, -1, 2), pick(zh, -1, 2), pick(zl, -1, 3), pick(zh, -1, 3)
        ixo_ref, iyo_ref, izo_ref = outs[12:15]
        ixo_ref[0:1] = ix_lo
        ixo_ref[1:2] = ix_hi
        iyo_ref[...] = pair(iy_lo, iy_hi, iyo_ref.shape, 1)
        izo_ref[...] = pair(iz_lo, iz_hi, izo_ref.shape, 2)
    else:
        vx = vx_ref[...]
        ix = ix_ref[...]
        vy = vy_ref[...]
        iy = iy_ref[...]
        vz = vz_ref[...]
        iz = iz_ref[...]
        vx_lo, vx_hi, ix_lo, ix_hi = vx[0:1], vx[1:2], ix[0:1], ix[1:2]
        vy_lo, vy_hi = pick(vy, 1, 0), pick(vy, 1, 1)
        iy_lo, iy_hi = pick(iy, 1, 0), pick(iy, 1, 1)
        vz_lo, vz_hi, iz_lo, iz_hi = pick(vz, -1, 0), pick(vz, -1, 1), pick(iz, -1, 0), pick(iz, -1, 1)

    pres = p_ref[...]
    idn = idn_ref[...]

    p_first = pick(pres, -1, 0)
    p_last = pick(pres, -1, Z - 1)
    sea = 0.5 * (f_ocean * (p_last + zh1) + f_crust * (zl1 + p_first))
    sfo_ref[...] = sea if first else sf_ref[...] + sea

    above_x = jnp.concatenate([pres[1:], pxh1], axis=0)
    below_x = jnp.concatenate([pxl1, pres[:-1]], axis=0)
    slope_x = 0.5 * (above_x - below_x)
    v0 = v_ref[0] - time_step * idn * slope_x
    v0_lo = vx_lo - time_step * ix_lo * (0.5 * (pres[0:1] - pxl2))
    v0_hi = vx_hi - time_step * ix_hi * (0.5 * (pxh2 - pres[X - 1 : X]))

    p_y0 = pick(pres, 1, 0)
    p_yl = pick(pres, 1, Y - 1)
    above_y = jnp.where(yi == Y - 1, jnp.broadcast_to(yh1, full), pltpu.roll(pres, Y - 1, 1))
    below_y = jnp.where(yi == 0, jnp.broadcast_to(yl1, full), pltpu.roll(pres, 1, 1))
    slope_y = 0.5 * (above_y - below_y)
    v1 = v_ref[1] - time_step * idn * slope_y
    v1_lo = vy_lo - time_step * iy_lo * (0.5 * (p_y0 - yl2))
    v1_hi = vy_hi - time_step * iy_hi * (0.5 * (yh2 - p_yl))

    above_z = jnp.where(zi == Z - 1, jnp.broadcast_to(zh1, full), pltpu.roll(pres, Z - 1, 2))
    below_z = jnp.where(zi == 0, jnp.broadcast_to(zl1, full), pltpu.roll(pres, 1, 2))
    slope_z = wu * above_z + wm * pres + wl * below_z
    v2 = v_ref[2] - time_step * idn * slope_z
    v2_lo = vz_lo - time_step * iz_lo * (wu_lo * p_first + wm_lo * zl1 + wl_lo * zl2)
    v2_hi = vz_hi - time_step * iz_hi * (wu_hi * zh2 + wm_hi * zh1 + wl_hi * p_last)

    vo_ref[0] = v0
    vo_ref[1] = v1
    vo_ref[2] = v2
    vxo_ref[0:1] = v0_lo
    vxo_ref[1:2] = v0_hi
    vyo_ref[...] = pair(v1_lo, v1_hi, vyo_ref.shape, 1)
    vzo_ref[...] = pair(v2_lo, v2_hi, vzo_ref.shape, 2)

    up_x = jnp.concatenate([v0[1:], v0_hi], axis=0)
    down_x = jnp.concatenate([v0_lo, v0[:-1]], axis=0)
    up_y = jnp.where(yi == Y - 1, jnp.broadcast_to(v1_hi, full), pltpu.roll(v1, Y - 1, 1))
    down_y = jnp.where(yi == 0, jnp.broadcast_to(v1_lo, full), pltpu.roll(v1, 1, 1))
    up_z = jnp.where(zi == Z - 1, jnp.broadcast_to(v2_hi, full), pltpu.roll(v2, Z - 1, 2))
    down_z = jnp.where(zi == 0, jnp.broadcast_to(v2_lo, full), pltpu.roll(v2, 1, 2))
    spread = (
        0.5 * (up_x - down_x)
        + 0.5 * (up_y - down_y)
        + (wu * up_z + wm * v2 + wl * down_z)
    )
    new_p = pres - time_step * bulk_ref[...] * spread
    new_p = jnp.where(zi == 0, new_p + jnp.broadcast_to(src_ref[instant], full), new_p)
    po_ref[...] = new_p

    sxu_ref[...] = new_p[X - sxu_ref.shape[0] :]
    sxd_ref[...] = new_p[0 : sxd_ref.shape[0]]
    syu_ref[...] = new_p[:, Y - rows :]
    syd_ref[...] = new_p[:, 0:rows]
    zshape = szu_ref.shape
    szu_ref[...] = pair(pick(new_p, -1, Z - 2), pick(new_p, -1, Z - 1), zshape, 2)
    szd_ref[...] = pair(pick(new_p, -1, 0), pick(new_p, -1, 1), zshape, 2)


def run_step(instant, operands, rows):
    pres = operands[2]
    X, Y, Z = pres.shape
    first = instant == 0
    planes = rows if instant < ITERS - 2 else 2
    f32 = jnp.float32
    shapes = [
        jax.ShapeDtypeStruct((X, Y, Z), f32),
        jax.ShapeDtypeStruct((3, X, Y, Z), f32),
        jax.ShapeDtypeStruct((X, Y, 1), f32),
        jax.ShapeDtypeStruct((2, Y, Z), f32),
        jax.ShapeDtypeStruct((X, 2, Z), f32),
        jax.ShapeDtypeStruct((X, Y, 2), f32),
        jax.ShapeDtypeStruct((planes, Y, Z), f32),
        jax.ShapeDtypeStruct((planes, Y, Z), f32),
        jax.ShapeDtypeStruct((X, rows, Z), f32),
        jax.ShapeDtypeStruct((X, rows, Z), f32),
        jax.ShapeDtypeStruct((X, Y, 2), f32),
        jax.ShapeDtypeStruct((X, Y, 2), f32),
    ]
    if first:
        shapes += shapes[3:6]
    vmem = pl.BlockSpec(memory_space=pltpu.VMEM)
    in_specs = [pl.BlockSpec(memory_space=pltpu.SMEM)] + [vmem] * (len(operands) - 1)
    cells = X * Y * Z
    return pl.pallas_call(
        functools.partial(step_kernel, instant, first),
        out_shape=tuple(shapes),
        in_specs=in_specs,
        out_specs=[vmem] * len(shapes),
        cost_estimate=pl.CostEstimate(
            flops=80 * cells, transcendentals=0, bytes_accessed=4 * 4 * 12 * cells // 4
        ),
    )(*operands)


def seafloor_sums(seafloor, node_weight, node_patch, patch_slot):
    sea_values = node_weight[0, 0] * seafloor.reshape(-1)
    slots = patch_slot[node_patch[0, 0]]
    owners = lax.axis_size("gx") * lax.axis_size("gy")
    per_owner = patch_slot.shape[0] // owners
    owner_hot = slots[None, :] // per_owner == jnp.arange(owners, dtype=jnp.int32)[:, None]
    within_hot = (
        slots[:, None] % per_owner == jnp.arange(per_owner, dtype=jnp.int32)[None, :]
    ).astype(jnp.float32)
    weighted = jnp.where(owner_hot, sea_values[None, :], 0.0)
    partial_slip = jnp.dot(weighted, within_hot, precision=lax.Precision.HIGHEST).reshape(-1)
    return summed_on_arrival(partial_slip, ("gx", "gy"), 0)


def local(
    pressure,
    velocity,
    inv_density,
    bulk,
    node_weight,
    node_patch,
    patch_slot,
    gauge_x,
    gauge_y,
    gauge_misfit,
):
    X, Y, Z = pressure.shape
    rows = 8
    tiles_z = lax.axis_size("gz")
    depth_index = lax.axis_index("gz")
    first_crust = tiles_z // 2 * Z
    levels = depth_index * Z + jnp.arange(Z, dtype=jnp.int32)
    level_grid = depth_index * Z + lax.broadcasted_iota(jnp.int32, (3, 1, 1, Z), 3)
    w_up, w_mid, w_low = depth_weights(level_grid, first_crust)
    which = lax.broadcasted_iota(jnp.int32, (3, 1, 1, Z), 0)
    wint = jnp.where(which == 0, w_up, jnp.where(which == 1, w_mid, w_low))
    entry = lax.broadcasted_iota(jnp.int32, (ITERS * 16,), 0) % 16
    step_at = lax.broadcasted_iota(jnp.int32, (ITERS * 16,), 0) // 16
    edge_level = depth_index * Z + jnp.where(entry < 3, -1, Z)
    e_up, e_mid, e_low = depth_weights(edge_level, first_crust)
    kind = entry % 3
    edge_value = jnp.where(kind == 0, e_up, jnp.where(kind == 1, e_mid, e_low))
    ocean = depth_index == first_crust // Z - 1
    crust = depth_index == first_crust // Z
    before = step_at < ITERS - 1
    after = step_at < 0
    flag_value = jnp.where(
        entry == 6, before & ocean,
        jnp.where(entry == 7, before & crust,
                  jnp.where(entry == 8, after & ocean, after & crust)),
    ).astype(jnp.float32)
    scal_all = jnp.where(entry < 6, edge_value, jnp.where(entry < 10, flag_value, 0.0))
    scal_all = scal_all.astype(jnp.float32)
    top_flag = (depth_index == 0).astype(jnp.float32)
    sources = source_planes(
        gauge_x,
        gauge_y,
        gauge_misfit,
        lax.axis_index("gx") * X,
        lax.axis_index("gy") * Y,
        X,
        Y,
    )
    src_all = (time_step * sources * top_flag)[..., None]

    v0, v1, v2 = velocity[0], velocity[1], velocity[2]
    x_up = jnp.concatenate([pressure[X - 2 :], v0[X - 1 :], inv_density[X - 1 :]], axis=0)
    x_dn = jnp.concatenate([pressure[:2], v0[:1], inv_density[:1]], axis=0)
    y_up = jnp.concatenate(
        [pressure[:, Y - rows :], v1[:, Y - 1 :], inv_density[:, Y - 1 :]], axis=1
    )
    y_dn = jnp.concatenate([pressure[:, :rows], v1[:, :1], inv_density[:, :1]], axis=1)
    z_up = jnp.concatenate(
        [pressure[:, :, Z - 2 :], v2[:, :, Z - 1 :], inv_density[:, :, Z - 1 :]], axis=2
    )
    z_dn = jnp.concatenate([pressure[:, :, :2], v2[:, :, :1], inv_density[:, :, :1]], axis=2)
    halos = (
        shifted_up(x_up, "gx"),
        shifted_down(x_dn, "gx"),
        shifted_up(y_up, "gy"),
        shifted_down(y_dn, "gy"),
        shifted_up(z_up, "gz"),
        shifted_down(z_dn, "gz"),
    )
    common = (scal_all, wint)
    pres, vel = pressure, velocity
    for instant in range(ITERS):
        if instant > 0:
            halos = (
                shifted_up(sends[0], "gx"),
                shifted_down(sends[1], "gx"),
                shifted_up(sends[2], "gy"),
                shifted_down(sends[3], "gy"),
                shifted_up(sends[4], "gz"),
                shifted_down(sends[5], "gz"),
            )
        if instant == ITERS - 1:
            ocean = (depth_index == first_crust // Z - 1).astype(jnp.float32)
            crust = (depth_index == first_crust // Z).astype(jnp.float32)
            sf_last = sf + 0.5 * (
                ocean * (sends[4][:, :, 1:2] + halos[5][:, :, 0:1])
                + crust * (halos[4][:, :, 1:2] + sends[5][:, :, 0:1])
            )
            owner_sums = seafloor_sums(sf_last[:, :, 0], node_weight, node_patch, patch_slot)
        if instant == 0:
            operands = common + (pres, vel, inv_density, bulk, src_all) + halos
        else:
            operands = common + (pres, vel, inv_density, bulk, src_all, sf) + halos + tracked + media_halo
        outs = run_step(instant, operands, rows)
        pres, vel, sf = outs[0], outs[1], outs[2]
        tracked = outs[3:6]
        sends = outs[6:12]
        if instant == 0:
            media_halo = outs[12:15]
    ocean_plane = first_crust // Z - 1
    crust_plane = first_crust // Z
    spread_out = lax.ppermute(
        owner_sums, "gz", [(ocean_plane, ocean_plane - 1), (crust_plane, crust_plane + 1)]
    )
    inner = (depth_index == ocean_plane) | (depth_index == crust_plane)
    owner_sums = jnp.where(inner, owner_sums, spread_out)
    piece = owner_sums.shape[0] // tiles_z
    slip_grad = lax.dynamic_slice_in_dim(owner_sums, depth_index * piece, piece)
    return (pres, vel, slip_grad)


def solution(mesh):
    placed = (
        P("gx", "gy", "gz"),
        P(None, "gx", "gy", "gz"),
        P("gx", "gy", "gz"),
        P("gx", "gy", "gz"),
        P("gx", "gy", None),
        P("gx", "gy", None),
        P(),
        P(),
        P(),
        P(),
    )
    return jax.shard_map(
        local,
        mesh=mesh,
        in_specs=placed,
        out_specs=(P("gx", "gy", "gz"), P(None, "gx", "gy", "gz"), P(("gx", "gy", "gz"))),
        check_vma=False,
    )
```

```python
import functools

import jax
import jax.numpy as jnp
from jax import lax
from jax.experimental import pallas as pl
from jax.experimental.pallas import tpu as pltpu
from jax.sharding import PartitionSpec as P

ITERS = 4


time_step = 0.5


def shifted_up(x, axis):
    count = lax.axis_size(axis)
    return lax.ppermute(x, axis, [(i, i + 1) for i in range(count - 1)])


def shifted_down(x, axis):
    count = lax.axis_size(axis)
    return lax.ppermute(x, axis, [(i + 1, i) for i in range(count - 1)])


def in_blocks(x, dim, size):
    before, after = (x.shape[:dim], x.shape[dim + 1 :])
    return jnp.moveaxis(x.reshape(*before, size, -1, *after), dim, 0)


def summed_on_arrival(x, axis, dim):
    size = lax.axis_size(axis)
    parts = lax.all_to_all(in_blocks(x, dim, size), axis, 0, 0, tiled=True)
    return jnp.sum(parts, axis=0)


def depth_weights(levels, first_crust):
    ocean_last = levels == first_crust - 1
    crust_first = levels == first_crust
    weight_above = jnp.where(ocean_last, 0.5, jnp.where(crust_first, 1.0, 0.5)).astype(jnp.float32)
    weight_here = jnp.where(ocean_last, 0.5, jnp.where(crust_first, -1.5, 0.0)).astype(jnp.float32)
    weight_below = jnp.where(ocean_last, -1.0, jnp.where(crust_first, 0.5, -0.5)).astype(
        jnp.float32
    )
    return (weight_above, weight_here, weight_below)


def source_planes(gauge_x, gauge_y, gauge_misfit, start_x, start_y, span_x, span_y):
    local_x = gauge_x - start_x
    local_y = gauge_y - start_y
    inside = (local_x >= 0) & (local_x < span_x) & (local_y >= 0) & (local_y < span_y)
    gauge_cell = jnp.where(inside, local_x * span_y + local_y, -1)
    gauge_table = (
        gauge_cell[:, None] == jnp.arange(span_x * span_y, dtype=jnp.int32)[None, :]
    ).astype(jnp.float32)
    return jnp.dot(gauge_misfit, gauge_table, precision=lax.Precision.HIGHEST).reshape(
        gauge_misfit.shape[0], span_x, span_y
    )


def pick(a, axis, index):
    return lax.slice_in_dim(a, index, index + 1, axis=axis % a.ndim)


def pair(lo, hi, shape, axis):
    where = lax.broadcasted_iota(jnp.int32, shape, axis) == 0
    return jnp.where(where, jnp.broadcast_to(lo, shape), jnp.broadcast_to(hi, shape))


def step_kernel(instant, first, *refs):
    if first:
        (scal_ref, wint_ref, p_ref, v_ref, idn_ref, bulk_ref, src_ref,
         xl_ref, xh_ref, yl_ref, yh_ref, zl_ref, zh_ref) = refs[:13]
        outs = refs[13:]
    else:
        (scal_ref, wint_ref, p_ref, v_ref, idn_ref, bulk_ref, src_ref, sf_ref,
         xl_ref, xh_ref, yl_ref, yh_ref, zl_ref, zh_ref,
         vx_ref, vy_ref, vz_ref, ix_ref, iy_ref, iz_ref) = refs[:20]
        outs = refs[20:]
    (po_ref, vo_ref, sfo_ref, vxo_ref, vyo_ref, vzo_ref,
     sxu_ref, sxd_ref, syu_ref, syd_ref, szu_ref, szd_ref) = outs[:12]
    X, Y, Z = p_ref.shape
    rows = syu_ref.shape[1]
    base = instant * 16
    full = (X, Y, Z)
    yi = lax.broadcasted_iota(jnp.int32, full, 1)
    zi = lax.broadcasted_iota(jnp.int32, full, 2)
    wu = wint_ref[0]
    wm = wint_ref[1]
    wl = wint_ref[2]
    wu_lo = scal_ref[base + 0]
    wm_lo = scal_ref[base + 1]
    wl_lo = scal_ref[base + 2]
    wu_hi = scal_ref[base + 3]
    wm_hi = scal_ref[base + 4]
    wl_hi = scal_ref[base + 5]
    f_ocean = scal_ref[base + 6]
    f_crust = scal_ref[base + 7]

    xl = xl_ref[...]
    xh = xh_ref[...]
    yl = yl_ref[...]
    yh = yh_ref[...]
    zl = zl_ref[...]
    zh = zh_ref[...]
    pxl2, pxl1 = (xl[0:1], xl[1:2]) if first else (xl[-2:-1], xl[-1:])
    pxh1, pxh2 = xh[0:1], xh[1:2]
    yl2, yl1 = pick(yl, 1, rows - 2), pick(yl, 1, rows - 1)
    yh1, yh2 = pick(yh, 1, 0), pick(yh, 1, 1)
    zl2, zl1 = pick(zl, -1, 0), pick(zl, -1, 1)
    zh1, zh2 = pick(zh, -1, 0), pick(zh, -1, 1)
    if first:
        vx_lo, vx_hi, ix_lo, ix_hi = xl[2:3], xh[2:3], xl[3:4], xh[3:4]
        vy_lo, vy_hi = pick(yl, 1, rows), pick(yh, 1, rows)
        iy_lo, iy_hi = pick(yl, 1, rows + 1), pick(yh, 1, rows + 1)
        vz_lo, vz_hi, iz_lo, iz_hi = pick(zl, -1, 2), pick(zh, -1, 2), pick(zl, -1, 3), pick(zh, -1, 3)
        ixo_ref, iyo_ref, izo_ref = outs[12:15]
        ixo_ref[0:1] = ix_lo
        ixo_ref[1:2] = ix_hi
        iyo_ref[...] = pair(iy_lo, iy_hi, iyo_ref.shape, 1)
        izo_ref[...] = pair(iz_lo, iz_hi, izo_ref.shape, 2)
    else:
        vx = vx_ref[...]
        ix = ix_ref[...]
        vy = vy_ref[...]
        iy = iy_ref[...]
        vz = vz_ref[...]
        iz = iz_ref[...]
        vx_lo, vx_hi, ix_lo, ix_hi = vx[0:1], vx[1:2], ix[0:1], ix[1:2]
        vy_lo, vy_hi = pick(vy, 1, 0), pick(vy, 1, 1)
        iy_lo, iy_hi = pick(iy, 1, 0), pick(iy, 1, 1)
        vz_lo, vz_hi, iz_lo, iz_hi = pick(vz, -1, 0), pick(vz, -1, 1), pick(iz, -1, 0), pick(iz, -1, 1)

    pres = p_ref[...]
    idn = idn_ref[...]

    p_first = pick(pres, -1, 0)
    p_last = pick(pres, -1, Z - 1)
    sea = 0.5 * (f_ocean * (p_last + zh1) + f_crust * (zl1 + p_first))
    sfo_ref[...] = sea if first else sf_ref[...] + sea

    above_x = jnp.concatenate([pres[1:], pxh1], axis=0)
    below_x = jnp.concatenate([pxl1, pres[:-1]], axis=0)
    slope_x = 0.5 * (above_x - below_x)
    v0 = v_ref[0] - time_step * idn * slope_x
    v0_lo = vx_lo - time_step * ix_lo * (0.5 * (pres[0:1] - pxl2))
    v0_hi = vx_hi - time_step * ix_hi * (0.5 * (pxh2 - pres[X - 1 : X]))

    p_y0 = pick(pres, 1, 0)
    p_yl = pick(pres, 1, Y - 1)
    above_y = jnp.where(yi == Y - 1, jnp.broadcast_to(yh1, full), pltpu.roll(pres, Y - 1, 1))
    below_y = jnp.where(yi == 0, jnp.broadcast_to(yl1, full), pltpu.roll(pres, 1, 1))
    slope_y = 0.5 * (above_y - below_y)
    v1 = v_ref[1] - time_step * idn * slope_y
    v1_lo = vy_lo - time_step * iy_lo * (0.5 * (p_y0 - yl2))
    v1_hi = vy_hi - time_step * iy_hi * (0.5 * (yh2 - p_yl))

    above_z = jnp.where(zi == Z - 1, jnp.broadcast_to(zh1, full), pltpu.roll(pres, Z - 1, 2))
    below_z = jnp.where(zi == 0, jnp.broadcast_to(zl1, full), pltpu.roll(pres, 1, 2))
    slope_z = wu * above_z + wm * pres + wl * below_z
    v2 = v_ref[2] - time_step * idn * slope_z
    v2_lo = vz_lo - time_step * iz_lo * (wu_lo * p_first + wm_lo * zl1 + wl_lo * zl2)
    v2_hi = vz_hi - time_step * iz_hi * (wu_hi * zh2 + wm_hi * zh1 + wl_hi * p_last)

    vo_ref[0] = v0
    vo_ref[1] = v1
    vo_ref[2] = v2
    vxo_ref[0:1] = v0_lo
    vxo_ref[1:2] = v0_hi
    vyo_ref[...] = pair(v1_lo, v1_hi, vyo_ref.shape, 1)
    vzo_ref[...] = pair(v2_lo, v2_hi, vzo_ref.shape, 2)

    up_x = jnp.concatenate([v0[1:], v0_hi], axis=0)
    down_x = jnp.concatenate([v0_lo, v0[:-1]], axis=0)
    up_y = jnp.where(yi == Y - 1, jnp.broadcast_to(v1_hi, full), pltpu.roll(v1, Y - 1, 1))
    down_y = jnp.where(yi == 0, jnp.broadcast_to(v1_lo, full), pltpu.roll(v1, 1, 1))
    up_z = jnp.where(zi == Z - 1, jnp.broadcast_to(v2_hi, full), pltpu.roll(v2, Z - 1, 2))
    down_z = jnp.where(zi == 0, jnp.broadcast_to(v2_lo, full), pltpu.roll(v2, 1, 2))
    spread = (
        0.5 * (up_x - down_x)
        + 0.5 * (up_y - down_y)
        + (wu * up_z + wm * v2 + wl * down_z)
    )
    new_p = pres - time_step * bulk_ref[...] * spread
    new_p = jnp.where(zi == 0, new_p + jnp.broadcast_to(src_ref[instant], full), new_p)
    po_ref[...] = new_p

    sxu_ref[...] = new_p[X - sxu_ref.shape[0] :]
    sxd_ref[...] = new_p[0 : sxd_ref.shape[0]]
    syu_ref[...] = new_p[:, Y - rows :]
    syd_ref[...] = new_p[:, 0:rows]
    zshape = szu_ref.shape
    szu_ref[...] = pair(pick(new_p, -1, Z - 2), pick(new_p, -1, Z - 1), zshape, 2)
    szd_ref[...] = pair(pick(new_p, -1, 0), pick(new_p, -1, 1), zshape, 2)


def run_step(instant, operands, rows):
    pres = operands[2]
    X, Y, Z = pres.shape
    first = instant == 0
    planes = (rows if instant == 0 else X) if instant < ITERS - 2 else 2
    f32 = jnp.float32
    shapes = [
        jax.ShapeDtypeStruct((X, Y, Z), f32),
        jax.ShapeDtypeStruct((3, X, Y, Z), f32),
        jax.ShapeDtypeStruct((X, Y, 1), f32),
        jax.ShapeDtypeStruct((2, Y, Z), f32),
        jax.ShapeDtypeStruct((X, 2, Z), f32),
        jax.ShapeDtypeStruct((X, Y, 2), f32),
        jax.ShapeDtypeStruct((planes, Y, Z), f32),
        jax.ShapeDtypeStruct((planes, Y, Z), f32),
        jax.ShapeDtypeStruct((X, rows, Z), f32),
        jax.ShapeDtypeStruct((X, rows, Z), f32),
        jax.ShapeDtypeStruct((X, Y, 2), f32),
        jax.ShapeDtypeStruct((X, Y, 2), f32),
    ]
    if first:
        shapes += shapes[3:6]
    vmem = pl.BlockSpec(memory_space=pltpu.VMEM)
    in_specs = [pl.BlockSpec(memory_space=pltpu.SMEM)] + [vmem] * (len(operands) - 1)
    cells = X * Y * Z
    return pl.pallas_call(
        functools.partial(step_kernel, instant, first),
        out_shape=tuple(shapes),
        in_specs=in_specs,
        out_specs=[vmem] * len(shapes),
        cost_estimate=pl.CostEstimate(
            flops=80 * cells, transcendentals=0, bytes_accessed=4 * 4 * 12 * cells // 4
        ),
    )(*operands)


def seafloor_sums(seafloor, node_weight, node_patch, patch_slot):
    sea_values = node_weight[0, 0] * seafloor.reshape(-1)
    slots = patch_slot[node_patch[0, 0]]
    owners = lax.axis_size("gx") * lax.axis_size("gy")
    per_owner = patch_slot.shape[0] // owners
    owner_hot = slots[None, :] // per_owner == jnp.arange(owners, dtype=jnp.int32)[:, None]
    within_hot = (
        slots[:, None] % per_owner == jnp.arange(per_owner, dtype=jnp.int32)[None, :]
    ).astype(jnp.float32)
    weighted = jnp.where(owner_hot, sea_values[None, :], 0.0)
    partial_slip = jnp.dot(weighted, within_hot, precision=lax.Precision.HIGHEST).reshape(-1)
    return summed_on_arrival(partial_slip, ("gx", "gy"), 0)


def local(
    pressure,
    velocity,
    inv_density,
    bulk,
    node_weight,
    node_patch,
    patch_slot,
    gauge_x,
    gauge_y,
    gauge_misfit,
):
    X, Y, Z = pressure.shape
    rows = 8
    tiles_z = lax.axis_size("gz")
    depth_index = lax.axis_index("gz")
    first_crust = tiles_z // 2 * Z
    levels = depth_index * Z + jnp.arange(Z, dtype=jnp.int32)
    level_grid = depth_index * Z + lax.broadcasted_iota(jnp.int32, (3, 1, 1, Z), 3)
    w_up, w_mid, w_low = depth_weights(level_grid, first_crust)
    which = lax.broadcasted_iota(jnp.int32, (3, 1, 1, Z), 0)
    wint = jnp.where(which == 0, w_up, jnp.where(which == 1, w_mid, w_low))
    entry = lax.broadcasted_iota(jnp.int32, (ITERS * 16,), 0) % 16
    step_at = lax.broadcasted_iota(jnp.int32, (ITERS * 16,), 0) // 16
    edge_level = depth_index * Z + jnp.where(entry < 3, -1, Z)
    e_up, e_mid, e_low = depth_weights(edge_level, first_crust)
    kind = entry % 3
    edge_value = jnp.where(kind == 0, e_up, jnp.where(kind == 1, e_mid, e_low))
    ocean = depth_index == first_crust // Z - 1
    crust = depth_index == first_crust // Z
    before = step_at < ITERS - 1
    after = step_at < 0
    flag_value = jnp.where(
        entry == 6, before & ocean,
        jnp.where(entry == 7, before & crust,
                  jnp.where(entry == 8, after & ocean, after & crust)),
    ).astype(jnp.float32)
    scal_all = jnp.where(entry < 6, edge_value, jnp.where(entry < 10, flag_value, 0.0))
    scal_all = scal_all.astype(jnp.float32)
    top_flag = (depth_index == 0).astype(jnp.float32)
    sources = source_planes(
        gauge_x,
        gauge_y,
        gauge_misfit,
        lax.axis_index("gx") * X,
        lax.axis_index("gy") * Y,
        X,
        Y,
    )
    src_all = (time_step * sources * top_flag)[..., None]

    v0, v1, v2 = velocity[0], velocity[1], velocity[2]
    x_up = jnp.concatenate([pressure[X - 2 :], v0[X - 1 :], inv_density[X - 1 :]], axis=0)
    x_dn = jnp.concatenate([pressure[:2], v0[:1], inv_density[:1]], axis=0)
    y_up = jnp.concatenate(
        [pressure[:, Y - rows :], v1[:, Y - 1 :], inv_density[:, Y - 1 :]], axis=1
    )
    y_dn = jnp.concatenate([pressure[:, :rows], v1[:, :1], inv_density[:, :1]], axis=1)
    z_up = jnp.concatenate(
        [pressure[:, :, Z - 2 :], v2[:, :, Z - 1 :], inv_density[:, :, Z - 1 :]], axis=2
    )
    z_dn = jnp.concatenate([pressure[:, :, :2], v2[:, :, :1], inv_density[:, :, :1]], axis=2)
    halos = (
        shifted_up(x_up, "gx"),
        shifted_down(x_dn, "gx"),
        shifted_up(y_up, "gy"),
        shifted_down(y_dn, "gy"),
        shifted_up(z_up, "gz"),
        shifted_down(z_dn, "gz"),
    )
    common = (scal_all, wint)
    pres, vel = pressure, velocity
    for instant in range(ITERS):
        if instant > 0:
            halos = (
                shifted_up(sends[0], "gx"),
                shifted_down(sends[1], "gx"),
                shifted_up(sends[2], "gy"),
                shifted_down(sends[3], "gy"),
                shifted_up(sends[4], "gz"),
                shifted_down(sends[5], "gz"),
            )
        if instant == ITERS - 1:
            ocean = (depth_index == first_crust // Z - 1).astype(jnp.float32)
            crust = (depth_index == first_crust // Z).astype(jnp.float32)
            sf_last = sf + 0.5 * (
                ocean * (sends[4][:, :, 1:2] + halos[5][:, :, 0:1])
                + crust * (halos[4][:, :, 1:2] + sends[5][:, :, 0:1])
            )
            owner_sums = seafloor_sums(sf_last[:, :, 0], node_weight, node_patch, patch_slot)
        if instant == 0:
            operands = common + (pres, vel, inv_density, bulk, src_all) + halos
        else:
            operands = common + (pres, vel, inv_density, bulk, src_all, sf) + halos + tracked + media_halo
        outs = run_step(instant, operands, rows)
        pres, vel, sf = outs[0], outs[1], outs[2]
        tracked = outs[3:6]
        sends = outs[6:12]
        if instant == 0:
            media_halo = outs[12:15]
    ocean_plane = first_crust // Z - 1
    crust_plane = first_crust // Z
    spread_out = lax.ppermute(
        owner_sums, "gz", [(ocean_plane, ocean_plane - 1), (crust_plane, crust_plane + 1)]
    )
    inner = (depth_index == ocean_plane) | (depth_index == crust_plane)
    owner_sums = jnp.where(inner, owner_sums, spread_out)
    piece = owner_sums.shape[0] // tiles_z
    slip_grad = lax.dynamic_slice_in_dim(owner_sums, depth_index * piece, piece)
    return (pres, vel, slip_grad)


def solution(mesh):
    placed = (
        P("gx", "gy", "gz"),
        P(None, "gx", "gy", "gz"),
        P("gx", "gy", "gz"),
        P("gx", "gy", "gz"),
        P("gx", "gy", None),
        P("gx", "gy", None),
        P(),
        P(),
        P(),
        P(),
    )
    return jax.shard_map(
        local,
        mesh=mesh,
        in_specs=placed,
        out_specs=(P("gx", "gy", "gz"), P(None, "gx", "gy", "gz"), P(("gx", "gy", "gz"))),
        check_vma=False,
    )
```

```python
import functools

import jax
import jax.numpy as jnp
from jax import lax
from jax.experimental import pallas as pl
from jax.experimental.pallas import tpu as pltpu
from jax.sharding import PartitionSpec as P

ITERS = 4


time_step = 0.5


def shifted_up(x, axis):
    count = lax.axis_size(axis)
    return lax.ppermute(x, axis, [(i, i + 1) for i in range(count - 1)])


def shifted_down(x, axis):
    count = lax.axis_size(axis)
    return lax.ppermute(x, axis, [(i + 1, i) for i in range(count - 1)])


def in_blocks(x, dim, size):
    before, after = (x.shape[:dim], x.shape[dim + 1 :])
    return jnp.moveaxis(x.reshape(*before, size, -1, *after), dim, 0)


def summed_on_arrival(x, axis, dim):
    size = lax.axis_size(axis)
    parts = lax.all_to_all(in_blocks(x, dim, size), axis, 0, 0, tiled=True)
    return jnp.sum(parts, axis=0)


def depth_weights(levels, first_crust):
    ocean_last = levels == first_crust - 1
    crust_first = levels == first_crust
    weight_above = jnp.where(ocean_last, 0.5, jnp.where(crust_first, 1.0, 0.5)).astype(jnp.float32)
    weight_here = jnp.where(ocean_last, 0.5, jnp.where(crust_first, -1.5, 0.0)).astype(jnp.float32)
    weight_below = jnp.where(ocean_last, -1.0, jnp.where(crust_first, 0.5, -0.5)).astype(
        jnp.float32
    )
    return (weight_above, weight_here, weight_below)


def source_planes(gauge_x, gauge_y, gauge_misfit, start_x, start_y, span_x, span_y):
    local_x = gauge_x - start_x
    local_y = gauge_y - start_y
    inside = (local_x >= 0) & (local_x < span_x) & (local_y >= 0) & (local_y < span_y)
    gauge_cell = jnp.where(inside, local_x * span_y + local_y, -1)
    gauge_table = (
        gauge_cell[:, None] == jnp.arange(span_x * span_y, dtype=jnp.int32)[None, :]
    ).astype(jnp.float32)
    return jnp.dot(gauge_misfit, gauge_table, precision=lax.Precision.HIGHEST).reshape(
        gauge_misfit.shape[0], span_x, span_y
    )


def pick(a, axis, index):
    return lax.slice_in_dim(a, index, index + 1, axis=axis % a.ndim)


def pair(lo, hi, shape, axis):
    where = lax.broadcasted_iota(jnp.int32, shape, axis) == 0
    return jnp.where(where, jnp.broadcast_to(lo, shape), jnp.broadcast_to(hi, shape))


def step_kernel(instant, first, *refs):
    if first:
        (scal_ref, wint_ref, p_ref, v_ref, idn_ref, bulk_ref, src_ref,
         xl_ref, xh_ref, yl_ref, yh_ref, zl_ref, zh_ref) = refs[:13]
        outs = refs[13:]
    else:
        (scal_ref, wint_ref, p_ref, v_ref, idn_ref, bulk_ref, src_ref, sf_ref,
         xl_ref, xh_ref, yl_ref, yh_ref, zl_ref, zh_ref,
         vx_ref, vy_ref, vz_ref, ix_ref, iy_ref, iz_ref) = refs[:20]
        outs = refs[20:]
    (po_ref, vo_ref, sfo_ref, vxo_ref, vyo_ref, vzo_ref,
     sxu_ref, sxd_ref, syu_ref, syd_ref, szu_ref, szd_ref) = outs[:12]
    X, Y, Z = p_ref.shape
    rows = syu_ref.shape[1]
    base = instant * 16
    full = (X, Y, Z)
    yi = lax.broadcasted_iota(jnp.int32, full, 1)
    zi = lax.broadcasted_iota(jnp.int32, full, 2)
    wu = wint_ref[0]
    wm = wint_ref[1]
    wl = wint_ref[2]
    wu_lo = scal_ref[base + 0]
    wm_lo = scal_ref[base + 1]
    wl_lo = scal_ref[base + 2]
    wu_hi = scal_ref[base + 3]
    wm_hi = scal_ref[base + 4]
    wl_hi = scal_ref[base + 5]
    f_ocean = scal_ref[base + 6]
    f_crust = scal_ref[base + 7]

    xl = xl_ref[...]
    xh = xh_ref[...]
    yl = yl_ref[...]
    yh = yh_ref[...]
    zl = zl_ref[...]
    zh = zh_ref[...]
    pxl2, pxl1 = (xl[0:1], xl[1:2]) if first else (xl[-2:-1], xl[-1:])
    pxh1, pxh2 = xh[0:1], xh[1:2]
    yl2, yl1 = pick(yl, 1, rows - 2), pick(yl, 1, rows - 1)
    yh1, yh2 = pick(yh, 1, 0), pick(yh, 1, 1)
    zl2, zl1 = pick(zl, -1, 0), pick(zl, -1, 1)
    zh1, zh2 = pick(zh, -1, 0), pick(zh, -1, 1)
    if first:
        vx_lo, vx_hi, ix_lo, ix_hi = xl[2:3], xh[2:3], xl[3:4], xh[3:4]
        vy_lo, vy_hi = pick(yl, 1, rows), pick(yh, 1, rows)
        iy_lo, iy_hi = pick(yl, 1, rows + 1), pick(yh, 1, rows + 1)
        vz_lo, vz_hi, iz_lo, iz_hi = pick(zl, -1, 2), pick(zh, -1, 2), pick(zl, -1, 3), pick(zh, -1, 3)
        ixo_ref, iyo_ref, izo_ref = outs[12:15]
        ixo_ref[0:1] = ix_lo
        ixo_ref[1:2] = ix_hi
        iyo_ref[...] = pair(iy_lo, iy_hi, iyo_ref.shape, 1)
        izo_ref[...] = pair(iz_lo, iz_hi, izo_ref.shape, 2)
    else:
        vx = vx_ref[...]
        ix = ix_ref[...]
        vy = vy_ref[...]
        iy = iy_ref[...]
        vz = vz_ref[...]
        iz = iz_ref[...]
        vx_lo, vx_hi, ix_lo, ix_hi = vx[0:1], vx[1:2], ix[0:1], ix[1:2]
        vy_lo, vy_hi = pick(vy, 1, 0), pick(vy, 1, 1)
        iy_lo, iy_hi = pick(iy, 1, 0), pick(iy, 1, 1)
        vz_lo, vz_hi, iz_lo, iz_hi = pick(vz, -1, 0), pick(vz, -1, 1), pick(iz, -1, 0), pick(iz, -1, 1)

    pres = p_ref[...]
    idn = idn_ref[...]

    p_first = pick(pres, -1, 0)
    p_last = pick(pres, -1, Z - 1)
    sea = 0.5 * (f_ocean * (p_last + zh1) + f_crust * (zl1 + p_first))
    sfo_ref[...] = sea if first else sf_ref[...] + sea

    above_x = jnp.concatenate([pres[1:], pxh1], axis=0)
    below_x = jnp.concatenate([pxl1, pres[:-1]], axis=0)
    slope_x = 0.5 * (above_x - below_x)
    v0 = v_ref[0] - time_step * idn * slope_x
    v0_lo = vx_lo - time_step * ix_lo * (0.5 * (pres[0:1] - pxl2))
    v0_hi = vx_hi - time_step * ix_hi * (0.5 * (pxh2 - pres[X - 1 : X]))

    p_y0 = pick(pres, 1, 0)
    p_yl = pick(pres, 1, Y - 1)
    above_y = jnp.where(yi == Y - 1, jnp.broadcast_to(yh1, full), pltpu.roll(pres, Y - 1, 1))
    below_y = jnp.where(yi == 0, jnp.broadcast_to(yl1, full), pltpu.roll(pres, 1, 1))
    slope_y = 0.5 * (above_y - below_y)
    v1 = v_ref[1] - time_step * idn * slope_y
    v1_lo = vy_lo - time_step * iy_lo * (0.5 * (p_y0 - yl2))
    v1_hi = vy_hi - time_step * iy_hi * (0.5 * (yh2 - p_yl))

    above_z = jnp.where(zi == Z - 1, jnp.broadcast_to(zh1, full), pltpu.roll(pres, Z - 1, 2))
    below_z = jnp.where(zi == 0, jnp.broadcast_to(zl1, full), pltpu.roll(pres, 1, 2))
    slope_z = wu * above_z + wm * pres + wl * below_z
    v2 = v_ref[2] - time_step * idn * slope_z
    v2_lo = vz_lo - time_step * iz_lo * (wu_lo * p_first + wm_lo * zl1 + wl_lo * zl2)
    v2_hi = vz_hi - time_step * iz_hi * (wu_hi * zh2 + wm_hi * zh1 + wl_hi * p_last)

    vo_ref[0] = v0
    vo_ref[1] = v1
    vo_ref[2] = v2
    vxo_ref[0:1] = v0_lo
    vxo_ref[1:2] = v0_hi
    vyo_ref[...] = pair(v1_lo, v1_hi, vyo_ref.shape, 1)
    vzo_ref[...] = pair(v2_lo, v2_hi, vzo_ref.shape, 2)

    up_x = jnp.concatenate([v0[1:], v0_hi], axis=0)
    down_x = jnp.concatenate([v0_lo, v0[:-1]], axis=0)
    up_y = jnp.where(yi == Y - 1, jnp.broadcast_to(v1_hi, full), pltpu.roll(v1, Y - 1, 1))
    down_y = jnp.where(yi == 0, jnp.broadcast_to(v1_lo, full), pltpu.roll(v1, 1, 1))
    up_z = jnp.where(zi == Z - 1, jnp.broadcast_to(v2_hi, full), pltpu.roll(v2, Z - 1, 2))
    down_z = jnp.where(zi == 0, jnp.broadcast_to(v2_lo, full), pltpu.roll(v2, 1, 2))
    spread = (
        0.5 * (up_x - down_x)
        + 0.5 * (up_y - down_y)
        + (wu * up_z + wm * v2 + wl * down_z)
    )
    new_p = pres - time_step * bulk_ref[...] * spread
    new_p = jnp.where(zi == 0, new_p + jnp.broadcast_to(src_ref[instant], full), new_p)
    po_ref[...] = new_p

    sxu_ref[...] = new_p[X - sxu_ref.shape[0] :]
    sxd_ref[...] = new_p[0 : sxd_ref.shape[0]]
    syu_ref[...] = new_p[:, Y - rows :]
    syd_ref[...] = new_p[:, 0:rows]
    zshape = szu_ref.shape
    szu_ref[...] = pair(pick(new_p, -1, Z - 2), pick(new_p, -1, Z - 1), zshape, 2)
    szd_ref[...] = pair(pick(new_p, -1, 0), pick(new_p, -1, 1), zshape, 2)


def run_step(instant, operands, rows):
    pres = operands[2]
    X, Y, Z = pres.shape
    first = instant == 0
    planes = (rows if instant == 0 else X) if instant < ITERS - 2 else 2
    f32 = jnp.float32
    shapes = [
        jax.ShapeDtypeStruct((X, Y, Z), f32),
        jax.ShapeDtypeStruct((3, X, Y, Z), f32),
        jax.ShapeDtypeStruct((X, Y, 1), f32),
        jax.ShapeDtypeStruct((2, Y, Z), f32),
        jax.ShapeDtypeStruct((X, 2, Z), f32),
        jax.ShapeDtypeStruct((X, Y, 2), f32),
        jax.ShapeDtypeStruct((planes, Y, Z), f32),
        jax.ShapeDtypeStruct((planes, Y, Z), f32),
        jax.ShapeDtypeStruct((X, rows, Z), f32),
        jax.ShapeDtypeStruct((X, rows, Z), f32),
        jax.ShapeDtypeStruct((X, Y, 2), f32),
        jax.ShapeDtypeStruct((X, Y, 2), f32),
    ]
    if first:
        shapes += shapes[3:6]
    vmem = pl.BlockSpec(memory_space=pltpu.VMEM)
    in_specs = [pl.BlockSpec(memory_space=pltpu.SMEM)] + [vmem] * (len(operands) - 1)
    cells = X * Y * Z
    return pl.pallas_call(
        functools.partial(step_kernel, instant, first),
        out_shape=tuple(shapes),
        in_specs=in_specs,
        out_specs=[vmem] * len(shapes),
        cost_estimate=pl.CostEstimate(
            flops=80 * cells, transcendentals=0, bytes_accessed=4 * 4 * 12 * cells // 4
        ),
    )(*operands)


def seafloor_sums(seafloor, node_weight, node_patch, patch_slot):
    sea_values = node_weight[0, 0] * seafloor.reshape(-1)
    slots = patch_slot[node_patch[0, 0]]
    owners = lax.axis_size("gx") * lax.axis_size("gy")
    per_owner = patch_slot.shape[0] // owners
    owner_hot = slots[None, :] // per_owner == jnp.arange(owners, dtype=jnp.int32)[:, None]
    within_hot = (
        slots[:, None] % per_owner == jnp.arange(per_owner, dtype=jnp.int32)[None, :]
    ).astype(jnp.float32)
    weighted = jnp.where(owner_hot, sea_values[None, :], 0.0)
    partial_slip = jnp.dot(weighted, within_hot, precision=lax.Precision.HIGHEST).reshape(-1)
    return summed_on_arrival(partial_slip, ("gx", "gy"), 0)


def local(
    pressure,
    velocity,
    inv_density,
    bulk,
    node_weight,
    node_patch,
    patch_slot,
    gauge_x,
    gauge_y,
    gauge_misfit,
):
    X, Y, Z = pressure.shape
    rows = 8
    tiles_z = lax.axis_size("gz")
    depth_index = lax.axis_index("gz")
    first_crust = tiles_z // 2 * Z
    levels = depth_index * Z + jnp.arange(Z, dtype=jnp.int32)
    level_grid = depth_index * Z + lax.broadcasted_iota(jnp.int32, (3, 1, 1, Z), 3)
    w_up, w_mid, w_low = depth_weights(level_grid, first_crust)
    which = lax.broadcasted_iota(jnp.int32, (3, 1, 1, Z), 0)
    wint = jnp.where(which == 0, w_up, jnp.where(which == 1, w_mid, w_low))
    entry = lax.broadcasted_iota(jnp.int32, (ITERS * 16,), 0) % 16
    step_at = lax.broadcasted_iota(jnp.int32, (ITERS * 16,), 0) // 16
    edge_level = depth_index * Z + jnp.where(entry < 3, -1, Z)
    e_up, e_mid, e_low = depth_weights(edge_level, first_crust)
    kind = entry % 3
    edge_value = jnp.where(kind == 0, e_up, jnp.where(kind == 1, e_mid, e_low))
    ocean = depth_index == first_crust // Z - 1
    crust = depth_index == first_crust // Z
    before = step_at < ITERS - 1
    after = step_at < 0
    flag_value = jnp.where(
        entry == 6, before & ocean,
        jnp.where(entry == 7, before & crust,
                  jnp.where(entry == 8, after & ocean, after & crust)),
    ).astype(jnp.float32)
    scal_all = jnp.where(entry < 6, edge_value, jnp.where(entry < 10, flag_value, 0.0))
    scal_all = scal_all.astype(jnp.float32)
    top_flag = (depth_index == 0).astype(jnp.float32)
    sources = source_planes(
        gauge_x,
        gauge_y,
        gauge_misfit,
        lax.axis_index("gx") * X,
        lax.axis_index("gy") * Y,
        X,
        Y,
    )
    src_all = (time_step * sources * top_flag)[..., None]

    v0, v1, v2 = velocity[0], velocity[1], velocity[2]
    filler = jnp.zeros((X - 4, Y, Z), jnp.float32)
    x_up = jnp.concatenate([pressure[X - 2 :], v0[X - 1 :], inv_density[X - 1 :], filler], axis=0)
    x_dn = jnp.concatenate([pressure[:2], v0[:1], inv_density[:1], filler], axis=0)
    y_up = jnp.concatenate(
        [pressure[:, Y - rows :], v1[:, Y - 1 :], inv_density[:, Y - 1 :]], axis=1
    )
    y_dn = jnp.concatenate([pressure[:, :rows], v1[:, :1], inv_density[:, :1]], axis=1)
    z_up = jnp.concatenate(
        [pressure[:, :, Z - 2 :], v2[:, :, Z - 1 :], inv_density[:, :, Z - 1 :]], axis=2
    )
    z_dn = jnp.concatenate([pressure[:, :, :2], v2[:, :, :1], inv_density[:, :, :1]], axis=2)
    halos = (
        shifted_up(x_up, "gx"),
        shifted_down(x_dn, "gx"),
        shifted_up(y_up, "gy"),
        shifted_down(y_dn, "gy"),
        shifted_up(z_up, "gz"),
        shifted_down(z_dn, "gz"),
    )
    common = (scal_all, wint)
    pres, vel = pressure, velocity
    for instant in range(ITERS):
        if instant > 0:
            halos = (
                shifted_up(sends[0], "gx"),
                shifted_down(sends[1], "gx"),
                shifted_up(sends[2], "gy"),
                shifted_down(sends[3], "gy"),
                shifted_up(sends[4], "gz"),
                shifted_down(sends[5], "gz"),
            )
        if instant == ITERS - 1:
            ocean = (depth_index == first_crust // Z - 1).astype(jnp.float32)
            crust = (depth_index == first_crust // Z).astype(jnp.float32)
            sf_last = sf + 0.5 * (
                ocean * (sends[4][:, :, 1:2] + halos[5][:, :, 0:1])
                + crust * (halos[4][:, :, 1:2] + sends[5][:, :, 0:1])
            )
            owner_sums = seafloor_sums(sf_last[:, :, 0], node_weight, node_patch, patch_slot)
        if instant == 0:
            operands = common + (pres, vel, inv_density, bulk, src_all) + halos
        else:
            operands = common + (pres, vel, inv_density, bulk, src_all, sf) + halos + tracked + media_halo
        outs = run_step(instant, operands, rows)
        pres, vel, sf = outs[0], outs[1], outs[2]
        tracked = outs[3:6]
        sends = outs[6:12]
        if instant == 0:
            media_halo = outs[12:15]
    ocean_plane = first_crust // Z - 1
    crust_plane = first_crust // Z
    spread_out = lax.ppermute(
        owner_sums, "gz", [(ocean_plane, ocean_plane - 1), (crust_plane, crust_plane + 1)]
    )
    inner = (depth_index == ocean_plane) | (depth_index == crust_plane)
    owner_sums = jnp.where(inner, owner_sums, spread_out)
    piece = owner_sums.shape[0] // tiles_z
    slip_grad = lax.dynamic_slice_in_dim(owner_sums, depth_index * piece, piece)
    return (pres, vel, slip_grad)


def solution(mesh):
    placed = (
        P("gx", "gy", "gz"),
        P(None, "gx", "gy", "gz"),
        P("gx", "gy", "gz"),
        P("gx", "gy", "gz"),
        P("gx", "gy", None),
        P("gx", "gy", None),
        P(),
        P(),
        P(),
        P(),
    )
    return jax.shard_map(
        local,
        mesh=mesh,
        in_specs=placed,
        out_specs=(P("gx", "gy", "gz"), P(None, "gx", "gy", "gz"), P(("gx", "gy", "gz"))),
        check_vma=False,
    )
```
